32 devices in a mesh: img: 4 (over y, core), slab: 8 (over z, x).
Axes of the slice: x: 2, y: 2, z: 4, core: 2. Of those that a mesh axis runs over, the one named last changes fastest.
Arguments:
- images: bfloat16 [32, 400, 400], P(('img', 'slab')), may hold values from -1500 to 1500, as said below
- micrograph: int32 [32], P(('img', 'slab')), may hold values from 0 to 63
- defocus: float32 [64], replicated, may hold values from 30 to 90
- target_slab: int32 [32, 8, 1], P(('img', 'slab')), may hold values from 0 to 7; in each aligned block of 8 rows (0 to 7, 8 to 15, ..., all dimensions but the last counted through in order) at most 2 rows name the same one
- target_plane: int32 [32, 8], P(('img', 'slab')), may hold values from 0 to 1
- target_rows: int32 [32, 8], P(('img', 'slab')), may hold values from 0 to 7
- shift_index: int32 [32, 8], P(('img', 'slab')), may hold values from 0 to 7
- volume: bfloat16 [16, 128, 800], P('slab'), may hold values from -6 to 6
Outputs:
- residual: bfloat16 [32, 400, 400], P(('img', 'slab'))
- reconstruction: float32 [16, 128, 800], P('slab', 'img')
The draws below stay inside these ranges and needn't reach their ends.
Inputs may be any that keep to these rules, and one draw needn't show every extreme that they name: `target_slab`: in the 8 routed blocks of one device (aligned blocks of rows, particle by particle), no slab is named more than 2 times, a bound that some block reaches. `images`: real pixel values.
All inputs are finite; a program needn't handle non-finite values.
Results may differ from the reference program's by a relative error of at most 0.013.
Values may be sent and summed in bfloat16 or wider, within the bound.
No kernel may reach another device: no remote copies, remote signals or barrier semaphores. Data moves between devices by JAX's collectives and lax.ppermute only.
A program may use at most 128 MiB of HBM per device.

```python
import math
import jax
import jax.numpy as jnp
import numpy as np
from jax import lax

BOX = 400
RB = 16
LOW = 4
Z_DEV = 2
PART_DEV = 1
MICS = 64
WL = 8
VROWS = 128
NZ = 16
NPART = 32
ROUTE_DEV = 8
CAP = 2
N_SLAB = 8


def draw_images(key, part):
    noise_key, scale_key, column_key = jax.random.split(key, 3)
    position = jnp.arange(NPART, dtype=jnp.float32) / max(NPART - 1, 1)
    spread = jnp.exp(jax.random.uniform(scale_key, (NPART,), jnp.float32) * math.log(10.0))
    column = jnp.exp(jax.random.uniform(column_key, (BOX,), jnp.float32) * math.log(10.0))
    values = jnp.clip(jax.random.normal(noise_key, (NPART, BOX, BOX), jnp.float32), -6.0, 6.0)
    growth = 1.0 + 2.0 * position
    pictures = values * (0.3 * spread * growth)[:, None, None] * column[None, None, :]
    return pictures.astype(jnp.bfloat16)


def touch_ends(entries, rng, least, top_value):
    extent = entries.shape
    spot = [jax.random.randint(jax.random.fold_in(rng, axis), (), 0, extent[axis]) for axis in range(len(extent))]
    entries = entries.at[tuple(spot)].set(least)
    longest = extent.index(max(extent))
    spot[longest] = (spot[longest] + 1) % extent[longest]
    return entries.at[tuple(spot)].set(top_value)


def steps_of(own_key, dims, pieces, smallest, high):
    gain = 1.0
    for dim, blocks in pieces:
        draws = jax.random.uniform(jax.random.fold_in(jax.random.fold_in(own_key, 6), dim), (blocks,), jnp.float32, smallest / len(pieces), high / len(pieces))
        gain = gain * jnp.repeat(jnp.exp(draws), dims[dim] // blocks).reshape((-1,) + (1,) * (len(dims) - 1 - dim))
    return gain


def shared_out(key, own, number, rows, amount, top, limit, skew):
    ranking = jax.random.permutation(key, amount)
    heavy_load, usual = portions_of(amount, rows * top, limit, skew, True), portions_of(amount, rows * top, limit, skew, False)
    places = jnp.arange(amount)

    def named(tallies, rotation):
        used = int((tallies > 0).sum())
        fixed = max(1, used // 4)
        passed = fixed + (places - fixed + rotation * (used - fixed)) % max(1, amount - fixed)
        return jnp.zeros((amount,), jnp.int32).at[ranking[jnp.where(places < fixed, places, passed)]].set(jnp.asarray(tallies, jnp.int32))

    tallies = jnp.where(number % 4 == 0, named(heavy_load, number // 4), named(usual, number - number // 4 - 1))
    mixed = jax.random.permutation(jax.random.fold_in(own, 3), amount)
    source_of, receiver = mixed[0:amount // 2 * 2:2], mixed[1:amount // 2 * 2:2]
    margin = jnp.minimum(tallies[source_of] - 1, limit - tallies[receiver]) // 2
    margin = jnp.where((source_of == ranking[0]) | (receiver == ranking[0]) | (tallies[receiver] == 0), 0, jnp.maximum(margin, 0))
    passed = jax.random.randint(jax.random.fold_in(own, 4), (amount // 2,), 0, 1 << 20) % (margin + 1)
    tallies = tallies.at[source_of].add(-passed).at[receiver].add(passed)
    items = jnp.searchsorted(jnp.cumsum(tallies), jnp.arange(rows * top), side="right").astype(jnp.int32)
    table = items.reshape(top, rows).T
    table = table[jax.random.permutation(jax.random.fold_in(own, 1), rows)]
    rotation = jax.random.randint(jax.random.fold_in(own, 2), (rows, 1), 0, top)
    return jnp.take_along_axis(table, (jnp.arange(top)[None, :] + rotation) % top, axis=1)


def portions_of(number_of, total, bound, slope, full):
    loads = [(1 << 20) // math.isqrt(rank ** slope) + 1 for rank in range(1, number_of + 1)]
    largest = bound if full else min(bound, max(-(-total // number_of), total * loads[0] // sum(loads)))
    least = 1 if total - largest >= number_of - 1 else 0
    holding, spare = [largest] + [least] * (number_of - 1), total - largest - least * (number_of - 1)
    while spare > 0:
        free = [i for i in range(1, number_of) if holding[i] < largest] or [i for i in range(1, number_of) if holding[i] < bound]
        whole, left = sum([loads[i] for i in free]), spare
        for i in free:
            more = min(bound - holding[i], max(1, left * loads[i] // whole), spare)
            holding[i] = holding[i] + more
            spare = spare - more
    return np.array(holding)


def gaussian(stream_key, shape, scale, most, cuts=(), kind=jnp.bfloat16):
    factor_of = steps_of(stream_key, shape, cuts, -0.22, 0.18) if cuts else 1.0
    entries = jax.random.normal(stream_key, shape, jnp.float32) * scale * factor_of
    return jnp.minimum(jnp.maximum(entries, -most), most).astype(kind)


def setup_inputs(seed: int = 0) -> dict:
    arg_keys = jax.random.split(jax.random.key(seed), 9)
    images = draw_images(jax.random.fold_in(arg_keys[8], 71), 0)
    micrograph = touch_ends(jax.random.randint(arg_keys[1], (NPART,), 0, MICS), jax.random.fold_in(arg_keys[1], 1), 0, MICS - 1).astype(jnp.int32)
    defocus = jnp.clip(jnp.exp(jax.random.uniform(arg_keys[2], (MICS,), jnp.float32, math.log(30.0), math.log(90.0))), 30.0, 90.0)
    target_slab_keys = jax.random.split(jax.random.fold_in(arg_keys[3], 1), NPART * (2 * LOW) // ROUTE_DEV)
    target_slab_turns = jax.random.permutation(jax.random.fold_in(arg_keys[3], 3), NPART * (2 * LOW) // ROUTE_DEV)
    target_slab = jax.vmap(lambda own, number: shared_out(jax.random.fold_in(arg_keys[3], 2), own, number, ROUTE_DEV, N_SLAB, 1, CAP, 2))(target_slab_keys, target_slab_turns).reshape((NPART, 2 * LOW, 1))
    target_plane = touch_ends(jax.random.randint(arg_keys[4], (NPART, 2 * LOW), 0, Z_DEV), jax.random.fold_in(arg_keys[4], 1), 0, Z_DEV - 1).astype(jnp.int32)
    target_rows = touch_ends(jax.random.randint(arg_keys[5], (NPART, 2 * LOW), 0, 2 * LOW), jax.random.fold_in(arg_keys[5], 1), 0, (2 * LOW) - 1).astype(jnp.int32)
    shift_index = touch_ends(jax.random.randint(arg_keys[6], (NPART, 2 * LOW), 0, WL), jax.random.fold_in(arg_keys[6], 1), 0, WL - 1).astype(jnp.int32)
    volume = gaussian(arg_keys[7], (NZ, VROWS, 2 * BOX), 1.0, 6.0, ((0, 8),))
    return dict(images=images, micrograph=micrograph, defocus=defocus, target_slab=target_slab, target_plane=target_plane, target_rows=target_rows, shift_index=shift_index, volume=volume)


def dft_tables(box_size):
    positions = jnp.arange(box_size, dtype=jnp.int32)
    phase_steps = positions[:, None] * positions[None, :] % box_size
    angles = phase_steps.astype(jnp.float32) * (2.0 * math.pi / box_size)
    return (jnp.cos(angles).astype(jnp.bfloat16), jnp.sin(angles).astype(jnp.bfloat16))

def forward_tables(cosine_table, sine_table):
    right_table = jnp.concatenate([cosine_table, -sine_table], axis=1)
    left_table = jnp.stack([jnp.stack([cosine_table, sine_table]), jnp.stack([-sine_table, cosine_table])])
    return (right_table, left_table)

def inverse_tables(cosine_table, sine_table):
    upper_half = jnp.concatenate([cosine_table, sine_table], axis=1)
    lower_half = jnp.concatenate([-sine_table, cosine_table], axis=1)
    back_table = jnp.concatenate([upper_half, lower_half], axis=0)
    final_table = jnp.stack([cosine_table, -sine_table])
    return (back_table, final_table)

def transform(image_block, right_table, left_table):
    batch_size, box_size = (image_block.shape[0], image_block.shape[1])
    rowwise = jnp.einsum('nyx,xm->nym', image_block.astype(jnp.float32), right_table.astype(jnp.float32)).astype(jnp.bfloat16)
    quarters = rowwise.reshape(batch_size, box_size, 2, box_size)
    spectrum = jnp.einsum('ahky,nyhm->nkam', left_table.astype(jnp.float32), quarters.astype(jnp.float32))
    return spectrum.reshape(batch_size, box_size, 2 * box_size)

def invert(difference, back_table, final_table):
    batch_size, box_size = (difference.shape[0], difference.shape[1])
    rowwise = jnp.einsum('nyj,jk->nyk', difference.astype(jnp.float32), back_table.astype(jnp.float32)).astype(jnp.bfloat16)
    quarters = rowwise.reshape(batch_size, box_size, 2, box_size)
    picture = jnp.einsum('cxk,nkcm->nxm', final_table.astype(jnp.float32), quarters.astype(jnp.float32)) / box_size
    return picture.astype(jnp.bfloat16)

def radius_sq(row_ids, box_size):
    half_size = box_size // 2
    columns = jnp.arange(box_size, dtype=jnp.int32)
    freq_rows = jnp.where(row_ids < half_size, row_ids, row_ids - box_size)
    freq_cols = jnp.where(columns < half_size, columns, columns - box_size)
    total = freq_rows[..., None] * freq_rows[..., None] + freq_cols * freq_cols
    return total.astype(jnp.float32) / float(half_size * half_size)

def contrast_curve(defocus_of, row_ids, box_size):
    radius = radius_sq(row_ids, box_size)
    return (-jnp.sin(defocus_of[:, None, None] * radius + 0.1)).astype(jnp.bfloat16)

def lookup_defocus(mic_ids, defocus):
    labels = jnp.arange(defocus.shape[0], dtype=jnp.int32)
    return lax.optimization_barrier(jnp.sum(jnp.where(mic_ids[:, None] == labels[None, :], defocus[None, :], 0.0), axis=1))

def shift_halves(values, steps, box_size):
    split_shape = values.shape[:-1] + (2, box_size)
    return jnp.roll(values.reshape(split_shape), steps, axis=-1).reshape(values.shape)

def reference(images, micrograph, defocus, target_slab, target_plane, target_rows, shift_index, volume):
    box_size = BOX
    low_rows = LOW * RB
    cosine_table, sine_table = dft_tables(box_size)
    right_table, left_table = forward_tables(cosine_table, sine_table)
    back_table, final_table = inverse_tables(cosine_table, sine_table)
    blocks_total = NPART // PART_DEV
    image_blocks = images.reshape(blocks_total, PART_DEV, box_size, box_size)

    def add_power(running, image_block):
        spectrum = transform(image_block, right_table, left_table)
        real_part = spectrum[..., :box_size]
        imag_part = spectrum[..., box_size:]
        return (running + lax.optimization_barrier(jnp.sum(real_part * real_part + imag_part * imag_part, axis=0)), None)
    power_sum, unused = lax.scan(add_power, jnp.zeros((box_size, box_size), jnp.float32), image_blocks)
    noise_level = jnp.sqrt(power_sum / NPART + 1e-06)
    level_both = jnp.concatenate([noise_level, noise_level], axis=1)

    def one_block(numerator, inputs):
        image_block, mic_ids, slab_ids, plane_ids, row_block, shift_ids = inputs
        batch_size = image_block.shape[0]
        whitened = transform(image_block, right_table, left_table) / level_both
        row_all = jnp.broadcast_to(jnp.arange(box_size, dtype=jnp.int32)[None, :], (batch_size, box_size))
        contrast = contrast_curve(lookup_defocus(mic_ids, defocus), row_all, box_size)
        contrast_both = jnp.concatenate([contrast, contrast], axis=-1).astype(jnp.float32)
        weighted = (contrast_both * whitened).astype(jnp.bfloat16)
        low_blocks = jnp.concatenate([weighted[:, :low_rows], weighted[:, box_size - low_rows:]], axis=1)
        low_blocks = low_blocks.reshape(batch_size, 2 * LOW, RB, 2 * box_size).astype(jnp.float32)
        low_contrast = jnp.concatenate([contrast[:, :low_rows], contrast[:, box_size - low_rows:]], axis=1)
        low_contrast = low_contrast.reshape(batch_size, 2 * LOW, RB, box_size).astype(jnp.float32)
        row_index = row_block[..., None] * RB + jnp.arange(RB, dtype=jnp.int32)
        plane_index = jnp.broadcast_to((slab_ids[..., 0] * Z_DEV + plane_ids)[..., None], row_index.shape)
        blend_weight = ((shift_ids.astype(jnp.float32) + 0.5) / WL)[..., None, None]
        nearby = volume[plane_index, row_index].astype(jnp.float32)
        projected = ((1.0 - blend_weight) * nearby + blend_weight * shift_halves(nearby, -1, box_size)).astype(jnp.bfloat16)
        inserted = (1.0 - blend_weight) * low_blocks + blend_weight * shift_halves(low_blocks, 1, box_size)
        squared = low_contrast * low_contrast
        weights = (1.0 - blend_weight) * squared + blend_weight * jnp.roll(squared, 1, axis=-1)
        numerator = numerator.at[plane_index, row_index].add(jnp.concatenate([inserted, weights], axis=-1))
        projected = projected.reshape(batch_size, 2 * low_rows, 2 * box_size)
        middle = jnp.zeros((batch_size, box_size - 2 * low_rows, 2 * box_size), jnp.bfloat16)
        full_projection = jnp.concatenate([projected[:, :low_rows], middle, projected[:, low_rows:]], axis=1)
        difference = (whitened - contrast_both * full_projection.astype(jnp.float32)).astype(jnp.bfloat16)
        return (numerator, invert(difference, back_table, final_table))
    inputs = (image_blocks, micrograph.reshape(blocks_total, PART_DEV), target_slab.reshape(blocks_total, PART_DEV, 2 * LOW, 1), target_plane.reshape(blocks_total, PART_DEV, 2 * LOW), target_rows.reshape(blocks_total, PART_DEV, 2 * LOW), shift_index.reshape(blocks_total, PART_DEV, 2 * LOW))
    start = jnp.zeros((NZ, VROWS, 3 * box_size), jnp.float32)
    numerator, residual_blocks = lax.scan(one_block, start, inputs)
    weight_sum = numerator[..., 2 * box_size:]
    reconstruction = numerator[..., :2 * box_size] / (jnp.concatenate([weight_sum, weight_sum], axis=-1) + 1.0)
    residual = residual_blocks.reshape(NPART, box_size, box_size)
    return (residual, reconstruction)
```

```python
import math

import jax
import jax.numpy as jnp
from jax import lax
from jax.sharding import PartitionSpec as P

RB = 16
LOW = 4
WL = 8
HI = lax.Precision.HIGHEST


def dft_tables(box_size):
    positions = jnp.arange(box_size, dtype=jnp.int32)
    phase_steps = positions[:, None] * positions[None, :] % box_size
    angles = phase_steps.astype(jnp.float32) * (2.0 * math.pi / box_size)
    return (jnp.cos(angles).astype(jnp.bfloat16), jnp.sin(angles).astype(jnp.bfloat16))


def forward_tables(cosine_table, sine_table):
    right_table = jnp.concatenate([cosine_table, -sine_table], axis=1)
    left_table = jnp.stack(
        [jnp.stack([cosine_table, sine_table]), jnp.stack([-sine_table, cosine_table])]
    )
    return (right_table, left_table)


def inverse_tables(cosine_table, sine_table):
    upper_half = jnp.concatenate([cosine_table, sine_table], axis=1)
    lower_half = jnp.concatenate([-sine_table, cosine_table], axis=1)
    back_table = jnp.concatenate([upper_half, lower_half], axis=0)
    final_table = jnp.stack([cosine_table, -sine_table])
    return (back_table, final_table)


def transform(image_block, right_table, left_table):
    batch_size, box_size = (image_block.shape[0], image_block.shape[1])
    rowwise = jnp.einsum(
        "nyx,xm->nym", image_block, right_table, preferred_element_type=jnp.float32
    ).astype(jnp.bfloat16)
    quarters = rowwise.reshape(batch_size, box_size, 2, box_size)
    spectrum = jnp.einsum(
        "ahky,nyhm->nkam", left_table, quarters, preferred_element_type=jnp.float32
    )
    return spectrum.reshape(batch_size, box_size, 2 * box_size)


def invert(difference, back_table, final_table):
    batch_size, box_size = (difference.shape[0], difference.shape[1])
    rowwise = jnp.einsum(
        "nyj,jk->nyk", difference, back_table, preferred_element_type=jnp.float32
    ).astype(jnp.bfloat16)
    quarters = rowwise.reshape(batch_size, box_size, 2, box_size)
    picture = (
        jnp.einsum("cxk,nkcm->nxm", final_table, quarters, preferred_element_type=jnp.float32)
        / box_size
    )
    return picture.astype(jnp.bfloat16)


def radius_sq(row_ids, box_size):
    half_size = box_size // 2
    columns = jnp.arange(box_size, dtype=jnp.int32)
    freq_rows = jnp.where(row_ids < half_size, row_ids, row_ids - box_size)
    freq_cols = jnp.where(columns < half_size, columns, columns - box_size)
    total = freq_rows[..., None] * freq_rows[..., None] + freq_cols * freq_cols
    return total.astype(jnp.float32) / float(half_size * half_size)


def contrast_curve(defocus_of, row_ids, box_size):
    radius = radius_sq(row_ids, box_size)
    return (-jnp.sin(defocus_of[:, None, None] * radius + 0.1)).astype(jnp.bfloat16)


def lookup_defocus(mic_ids, defocus):
    labels = jnp.arange(defocus.shape[0], dtype=jnp.int32)
    return jnp.sum(jnp.where(mic_ids[:, None] == labels[None, :], defocus[None, :], 0.0), axis=1)


def shift_halves(values, steps, box_size):
    split_shape = values.shape[:-1] + (2, box_size)
    return jnp.roll(values.reshape(split_shape), steps, axis=-1).reshape(values.shape)


def low_row_ids(block_ids, box_size):
    base = block_ids * RB + jnp.where(block_ids < LOW, 0, box_size - 2 * LOW * RB)
    return base[..., None] + jnp.arange(RB, dtype=jnp.int32)


def power_all(power_half, device_count, box_size):
    rows = power_half.shape[0]
    chunk = rows * box_size // device_count
    pieces = power_half.reshape(device_count, chunk)
    gathered = lax.all_to_all(pieces, ("img", "slab"), 0, 0, tiled=True)
    total = jnp.sum(gathered, axis=0, keepdims=True)
    spread = jnp.broadcast_to(total, (device_count, chunk))
    back = lax.all_to_all(spread, ("img", "slab"), 0, 0, tiled=True)
    half = back.reshape(rows, box_size)[: box_size // 2 + 1]
    mirrored = jnp.roll(half[1 : box_size // 2][::-1, ::-1], 1, axis=1)
    return jnp.concatenate([half, mirrored], axis=0)


def half_rows(box_size, device_count):
    rows = box_size // 2 + 1
    while (rows * box_size) % device_count:
        rows += 1
    return rows


def body(images, micrograph, defocus, target_slab, target_plane, target_rows, shift_index, volume):
    particles, box_size = (images.shape[0], images.shape[1])
    slab_count = lax.axis_size("slab")
    img_count = lax.axis_size("img")
    device_count = img_count * slab_count
    low_rows = LOW * RB
    blocks_per = 2 * LOW
    routed = particles * blocks_per
    planes, vrows = volume.shape[0], volume.shape[1]
    row_blocks = vrows // RB
    slots = planes * row_blocks
    cosine_table, sine_table = dft_tables(box_size)
    right_table, left_table = forward_tables(cosine_table, sine_table)
    back_table, final_table = inverse_tables(cosine_table, sine_table)

    destination = target_slab.reshape(routed)
    capacity = max(2, (2 * routed + slab_count - 1) // slab_count)
    member = (destination[:, None] == jnp.arange(slab_count, dtype=jnp.int32)[None, :]).astype(
        jnp.int32
    )
    before = jnp.cumsum(member, axis=0) - member
    slot_rank = jnp.sum(member * before, axis=1)
    seat_index = destination * capacity + slot_rank
    seat_count = slab_count * capacity
    seat_pick = (seat_index[:, None] == jnp.arange(seat_count, dtype=jnp.int32)[None, :]).astype(
        jnp.bfloat16
    )
    source_block = jnp.tile(jnp.arange(blocks_per, dtype=jnp.int32), particles)
    block_info = jnp.stack(
        [
            jnp.ones((routed,), jnp.int32),
            target_plane.reshape(routed),
            target_rows.reshape(routed),
            shift_index.reshape(routed),
            source_block,
            jnp.repeat(micrograph, blocks_per),
        ],
        axis=1,
    )
    send_info = jnp.einsum(
        "rs,rc->sc", seat_pick.astype(jnp.int32), block_info, preferred_element_type=jnp.int32
    )
    got_info = lax.all_to_all(send_info, "slab", 0, 0, tiled=True)

    live = got_info[:, 0].astype(jnp.float32)[:, None, None]
    slot_of = got_info[:, 1] * row_blocks + got_info[:, 2]
    slot_pick = (slot_of[:, None] == jnp.arange(slots, dtype=jnp.int32)[None, :]).astype(
        jnp.bfloat16
    )
    blend_weight = ((got_info[:, 3].astype(jnp.float32) + 0.5) / WL)[:, None, None]
    volume_slots = volume.reshape(slots, RB, 2 * box_size)
    nearby = jnp.einsum(
        "sq,qrx->srx", slot_pick, volume_slots, preferred_element_type=jnp.float32
    )
    projected = (
        ((1.0 - blend_weight) * nearby + blend_weight * shift_halves(nearby, -1, box_size)) * live
    ).astype(jnp.bfloat16)
    returned_rows = lax.all_to_all(projected, "slab", 0, 0, tiled=True)

    spectrum = transform(images, right_table, left_table)
    low_spectrum = jnp.concatenate(
        [spectrum[:, :low_rows], spectrum[:, box_size - low_rows :]], axis=1
    ).astype(jnp.bfloat16)
    low_spectrum = low_spectrum.reshape(routed, RB * 2 * box_size)
    send_blocks = jnp.einsum(
        "rs,rx->sx", seat_pick, low_spectrum, preferred_element_type=jnp.float32
    ).astype(jnp.bfloat16)
    got_blocks = lax.all_to_all(
        send_blocks.reshape(seat_count, RB, 2 * box_size), "slab", 0, 0, tiled=True
    )

    rows_half = half_rows(box_size, device_count)
    real_part = spectrum[:, :rows_half, :box_size]
    imag_part = spectrum[:, :rows_half, box_size:]
    power_half = jnp.sum(real_part * real_part + imag_part * imag_part, axis=0)
    power = power_all(power_half, device_count, box_size)
    noise_level = jnp.sqrt(power / (particles * device_count) + 1e-06)
    level_both = jnp.concatenate([noise_level, noise_level], axis=1)

    got_rows = low_row_ids(got_info[:, 4], box_size)
    got_contrast = contrast_curve(lookup_defocus(got_info[:, 5], defocus), got_rows, box_size)
    got_level = level_both[got_rows]
    got_contrast_both = jnp.concatenate([got_contrast, got_contrast], axis=-1).astype(jnp.float32)
    received = got_contrast_both * got_blocks.astype(jnp.float32) / got_level
    inserted = (1.0 - blend_weight) * received + blend_weight * shift_halves(received, 1, box_size)
    contrast_rows = got_contrast.astype(jnp.float32)
    squared = contrast_rows * contrast_rows
    weights = (1.0 - blend_weight) * squared + blend_weight * jnp.roll(squared, 1, axis=-1)
    seat_data = jnp.concatenate([inserted, weights], axis=-1) * live
    numerator = jnp.einsum(
        "sq,srx->qrx", slot_pick.astype(jnp.float32), seat_data, precision=HI,
        preferred_element_type=jnp.float32,
    )
    share = vrows // img_count
    numerator = numerator.reshape(planes, img_count, share, 3 * box_size).astype(jnp.bfloat16)
    numerator = jnp.swapaxes(numerator, 0, 1)
    parts = lax.all_to_all(numerator, "img", 0, 0, tiled=True)
    volume_part = jnp.sum(parts.astype(jnp.float32), axis=0)
    weight_sum = volume_part[..., 2 * box_size :]
    reconstruction = volume_part[..., : 2 * box_size] / (
        jnp.concatenate([weight_sum, weight_sum], axis=-1) + 1.0
    )

    whitened = spectrum / level_both
    row_all = jnp.arange(box_size, dtype=jnp.int32)[None, :]
    contrast = contrast_curve(lookup_defocus(micrograph, defocus), row_all, box_size)
    contrast_both = jnp.concatenate([contrast, contrast], axis=-1).astype(jnp.float32)
    own_rows = jnp.einsum(
        "rs,sx->rx", seat_pick, returned_rows.reshape(seat_count, RB * 2 * box_size),
        preferred_element_type=jnp.float32,
    ).astype(jnp.bfloat16)
    own_rows = own_rows.reshape(particles, 2 * low_rows, 2 * box_size)
    middle = jnp.zeros((particles, box_size - 2 * low_rows, 2 * box_size), jnp.bfloat16)
    full_projection = jnp.concatenate(
        [own_rows[:, :low_rows], middle, own_rows[:, low_rows:]], axis=1
    )
    difference = (whitened - contrast_both * full_projection.astype(jnp.float32)).astype(
        jnp.bfloat16
    )
    residual = invert(difference, back_table, final_table)
    return (residual, reconstruction)


def solution(mesh):
    in_specs = (
        P(("img", "slab"), None, None),
        P(("img", "slab")),
        P(),
        P(("img", "slab"), None, None),
        P(("img", "slab"), None),
        P(("img", "slab"), None),
        P(("img", "slab"), None),
        P("slab", None, None),
    )
    out_specs = (P(("img", "slab"), None, None), P("slab", "img", None))
    return jax.shard_map(body, mesh=mesh, in_specs=in_specs, out_specs=out_specs, check_vma=False)
```

```python
import math

import jax
import ml_dtypes
import numpy as np
import jax.numpy as jnp
from jax import lax
from jax.sharding import PartitionSpec as P

RB = 16
LOW = 4
WL = 8
HI = lax.Precision.HIGHEST


def table_stack(box_size):
    positions = np.arange(box_size)
    angles = ((positions[:, None] * positions[None, :]) % box_size) * (2.0 * np.pi / box_size)
    both = np.stack([np.cos(angles), np.sin(angles)]).astype(ml_dtypes.bfloat16)
    return jnp.asarray(both)


def transform(image, tables):
    rowwise = jnp.einsum(
        "yx,hmx->hym", image, tables, preferred_element_type=jnp.float32
    ).astype(jnp.bfloat16)
    products = jnp.einsum("gky,hym->ghkm", tables, rowwise, preferred_element_type=jnp.float32)
    real = products[0, 0] - products[1, 1]
    imag = -(products[0, 1] + products[1, 0])
    return jnp.stack([real, imag])


def invert(difference, tables, box_size):
    products = jnp.einsum(
        "hyj,gmj->hgym", difference, tables, preferred_element_type=jnp.float32
    )
    back_real = products[0, 0] - products[1, 1]
    back_imag = products[0, 1] + products[1, 0]
    back_rows = jnp.stack([back_real, -back_imag]).astype(jnp.bfloat16)
    picture = jnp.einsum("hxk,hkm->hxm", tables, back_rows, preferred_element_type=jnp.float32)
    return ((picture[0] + picture[1]) / box_size).astype(jnp.bfloat16)


def radius_sq(row_ids, box_size):
    half_size = box_size // 2
    columns = jnp.arange(box_size, dtype=jnp.int32)
    freq_rows = jnp.where(row_ids < half_size, row_ids, row_ids - box_size)
    freq_cols = jnp.where(columns < half_size, columns, columns - box_size)
    total = freq_rows[..., None] * freq_rows[..., None] + freq_cols * freq_cols
    return total.astype(jnp.float32) / float(half_size * half_size)


def contrast_curve(defocus_of, row_ids, box_size):
    radius = radius_sq(row_ids, box_size)
    return (-jnp.sin(defocus_of[:, None, None] * radius + 0.1)).astype(jnp.bfloat16)


def lookup_defocus(mic_ids, defocus):
    labels = jnp.arange(defocus.shape[0], dtype=jnp.int32)
    return jnp.sum(jnp.where(mic_ids[:, None] == labels[None, :], defocus[None, :], 0.0), axis=1)


def shift_halves(values, steps, box_size):
    split_shape = values.shape[:-1] + (2, box_size)
    return jnp.roll(values.reshape(split_shape), steps, axis=-1).reshape(values.shape)


def low_row_ids(block_ids, box_size):
    base = block_ids * RB + jnp.where(block_ids < LOW, 0, box_size - 2 * LOW * RB)
    return base[..., None] + jnp.arange(RB, dtype=jnp.int32)


def power_all(power_half, device_count, box_size):
    rows = power_half.shape[0]
    chunk = rows * box_size // device_count
    pieces = power_half.reshape(device_count, chunk)
    gathered = lax.all_to_all(pieces, ("img", "slab"), 0, 0, tiled=True)
    total = jnp.sum(gathered, axis=0, keepdims=True)
    spread = jnp.broadcast_to(total, (device_count, chunk))
    back = lax.all_to_all(spread, ("img", "slab"), 0, 0, tiled=True)
    half = back.reshape(rows, box_size)[: box_size // 2 + 1]
    mirrored = jnp.roll(half[1 : box_size // 2][::-1, ::-1], 1, axis=1)
    return jnp.concatenate([half, mirrored], axis=0)


def half_rows(box_size, device_count):
    rows = box_size // 2 + 1
    while (rows * box_size) % device_count:
        rows += 1
    return rows


def body(images, micrograph, defocus, target_slab, target_plane, target_rows, shift_index, volume):
    particles, box_size = (images.shape[0], images.shape[1])
    slab_count = lax.axis_size("slab")
    img_count = lax.axis_size("img")
    device_count = img_count * slab_count
    low_rows = LOW * RB
    blocks_per = 2 * LOW
    routed = particles * blocks_per
    planes, vrows = volume.shape[0], volume.shape[1]
    row_blocks = vrows // RB
    slots = planes * row_blocks
    tables = lax.optimization_barrier(table_stack(box_size))

    destination = target_slab.reshape(routed)
    capacity = max(2, (2 * routed + slab_count - 1) // slab_count)
    member = (destination[:, None] == jnp.arange(slab_count, dtype=jnp.int32)[None, :]).astype(
        jnp.int32
    )
    before = jnp.cumsum(member, axis=0) - member
    slot_rank = jnp.sum(member * before, axis=1)
    seat_index = destination * capacity + slot_rank
    seat_count = slab_count * capacity
    seat_pick = (seat_index[:, None] == jnp.arange(seat_count, dtype=jnp.int32)[None, :]).astype(
        jnp.bfloat16
    )
    source_block = jnp.tile(jnp.arange(blocks_per, dtype=jnp.int32), particles)
    block_info = jnp.stack(
        [
            jnp.ones((routed,), jnp.int32),
            target_plane.reshape(routed),
            target_rows.reshape(routed),
            shift_index.reshape(routed),
            source_block,
            jnp.repeat(micrograph, blocks_per),
        ],
        axis=1,
    ).astype(jnp.bfloat16)
    info_width = 128
    block_info = jnp.pad(block_info, ((0, 0), (0, info_width - block_info.shape[1])))

    spectrum = jnp.stack([transform(images[n], tables) for n in range(particles)])
    low_spectrum = jnp.concatenate(
        [spectrum[:, :, :low_rows], spectrum[:, :, box_size - low_rows :]], axis=2
    ).astype(jnp.bfloat16)
    low_spectrum = jnp.moveaxis(low_spectrum, 1, 2).reshape(routed, RB * 2 * box_size)
    payload = jnp.concatenate([low_spectrum, block_info], axis=1)
    send = jnp.einsum(
        "rs,rx->sx", seat_pick, payload, preferred_element_type=jnp.float32
    ).astype(jnp.bfloat16)
    got = lax.all_to_all(send, "slab", 0, 0, tiled=True)
    got_blocks = got[:, : RB * 2 * box_size].reshape(seat_count, RB, 2 * box_size)
    got_info = got[:, RB * 2 * box_size : RB * 2 * box_size + 6].astype(jnp.int32)

    live = got_info[:, 0].astype(jnp.float32)[:, None, None]
    slot_of = got_info[:, 1] * row_blocks + got_info[:, 2]
    slot_pick = (slot_of[:, None] == jnp.arange(slots, dtype=jnp.int32)[None, :]).astype(
        jnp.bfloat16
    )
    blend_weight = ((got_info[:, 3].astype(jnp.float32) + 0.5) / WL)[:, None, None]
    volume_slots = volume.reshape(slots, RB, 2 * box_size)
    nearby = jnp.einsum(
        "sq,qrx->srx", slot_pick, volume_slots, preferred_element_type=jnp.float32
    )
    projected = (
        ((1.0 - blend_weight) * nearby + blend_weight * shift_halves(nearby, -1, box_size)) * live
    ).astype(jnp.bfloat16)
    returned_rows = lax.all_to_all(projected, "slab", 0, 0, tiled=True)

    rows_half = half_rows(box_size, device_count)
    low_half = spectrum[:, :, :rows_half]
    power_half = jnp.sum(low_half * low_half, axis=(0, 1))
    power = power_all(power_half, device_count, box_size)
    noise_level = jnp.sqrt(power / (particles * device_count) + 1e-06)
    level_both = jnp.concatenate([noise_level, noise_level], axis=1)

    got_rows = low_row_ids(got_info[:, 4], box_size)
    got_contrast = contrast_curve(lookup_defocus(got_info[:, 5], defocus), got_rows, box_size)
    got_level = level_both[got_rows]
    got_contrast_both = jnp.concatenate([got_contrast, got_contrast], axis=-1).astype(jnp.float32)
    received = got_contrast_both * got_blocks.astype(jnp.float32) / got_level
    inserted = (1.0 - blend_weight) * received + blend_weight * shift_halves(received, 1, box_size)
    contrast_rows = got_contrast.astype(jnp.float32)
    squared = contrast_rows * contrast_rows
    weights = (1.0 - blend_weight) * squared + blend_weight * jnp.roll(squared, 1, axis=-1)
    seat_data = jnp.concatenate([inserted, weights], axis=-1) * live
    numerator = jnp.einsum(
        "sq,srx->qrx", slot_pick.astype(jnp.float32), seat_data, precision=HI,
        preferred_element_type=jnp.float32,
    )
    share = vrows // img_count
    numerator = numerator.reshape(planes, img_count, share, 3 * box_size).astype(jnp.bfloat16)
    numerator = jnp.swapaxes(numerator, 0, 1)
    parts = lax.all_to_all(numerator, "img", 0, 0, tiled=True)
    volume_part = jnp.sum(parts.astype(jnp.float32), axis=0)
    weight_sum = volume_part[..., 2 * box_size :]
    reconstruction = volume_part[..., : 2 * box_size] / (
        jnp.concatenate([weight_sum, weight_sum], axis=-1) + 1.0
    )

    whitened = spectrum / noise_level
    row_all = jnp.arange(box_size, dtype=jnp.int32)[None, :]
    contrast = contrast_curve(lookup_defocus(micrograph, defocus), row_all, box_size)
    own_rows = jnp.einsum(
        "rs,sx->rx", seat_pick, returned_rows.reshape(seat_count, RB * 2 * box_size),
        preferred_element_type=jnp.float32,
    ).astype(jnp.bfloat16)
    own_rows = own_rows.reshape(particles, 2 * low_rows, 2, box_size)
    own_rows = jnp.moveaxis(own_rows, 2, 1)
    middle = jnp.zeros((particles, 2, box_size - 2 * low_rows, box_size), jnp.bfloat16)
    full_projection = jnp.concatenate(
        [own_rows[:, :, :low_rows], middle, own_rows[:, :, low_rows:]], axis=2
    )
    difference = (
        whitened - contrast.astype(jnp.float32)[:, None] * full_projection.astype(jnp.float32)
    ).astype(jnp.bfloat16)
    residual = jnp.stack([invert(difference[n], tables, box_size) for n in range(particles)])
    return (residual, reconstruction)


def solution(mesh):
    in_specs = (
        P(("img", "slab"), None, None),
        P(("img", "slab")),
        P(),
        P(("img", "slab"), None, None),
        P(("img", "slab"), None),
        P(("img", "slab"), None),
        P(("img", "slab"), None),
        P("slab", None, None),
    )
    out_specs = (P(("img", "slab"), None, None), P("slab", "img", None))
    return jax.shard_map(body, mesh=mesh, in_specs=in_specs, out_specs=out_specs, check_vma=False)
```

```python
import math

import jax
import ml_dtypes
import numpy as np
import jax.numpy as jnp
from jax import lax
from jax.sharding import PartitionSpec as P

RB = 16
LOW = 4
WL = 8
HI = lax.Precision.HIGHEST


def table_stack(box_size):
    positions = np.arange(box_size)
    angles = ((positions[:, None] * positions[None, :]) % box_size) * (2.0 * np.pi / box_size)
    both = np.stack([np.cos(angles), np.sin(angles)]).astype(ml_dtypes.bfloat16)
    return jnp.asarray(both)


def transform(image, tables):
    rowwise = jnp.einsum(
        "yx,hmx->hym", image, tables, preferred_element_type=jnp.float32
    ).astype(jnp.bfloat16)
    products = jnp.einsum("gky,hym->ghkm", tables, rowwise, preferred_element_type=jnp.float32)
    real = products[0, 0] - products[1, 1]
    imag = -(products[0, 1] + products[1, 0])
    return jnp.stack([real, imag])


def invert(difference, tables, box_size):
    products = jnp.einsum(
        "hyj,gmj->hgym", difference, tables, preferred_element_type=jnp.float32
    )
    back_real = products[0, 0] - products[1, 1]
    back_imag = products[0, 1] + products[1, 0]
    back_rows = jnp.stack([back_real, -back_imag]).astype(jnp.bfloat16)
    picture = jnp.einsum("hxk,hkm->hxm", tables, back_rows, preferred_element_type=jnp.float32)
    return ((picture[0] + picture[1]) / box_size).astype(jnp.bfloat16)


def radius_sq(row_ids, box_size):
    half_size = box_size // 2
    columns = jnp.arange(box_size, dtype=jnp.int32)
    freq_rows = jnp.where(row_ids < half_size, row_ids, row_ids - box_size)
    freq_cols = jnp.where(columns < half_size, columns, columns - box_size)
    total = freq_rows[..., None] * freq_rows[..., None] + freq_cols * freq_cols
    return total.astype(jnp.float32) / float(half_size * half_size)


def contrast_curve(defocus_of, row_ids, box_size):
    radius = radius_sq(row_ids, box_size)
    return (-jnp.sin(defocus_of[:, None, None] * radius + 0.1)).astype(jnp.bfloat16)


def lookup_defocus(mic_ids, defocus):
    labels = jnp.arange(defocus.shape[0], dtype=jnp.int32)
    return jnp.sum(jnp.where(mic_ids[:, None] == labels[None, :], defocus[None, :], 0.0), axis=1)


def shift_halves(values, steps, box_size):
    rolled = jnp.roll(values, steps, axis=-1)
    column = lax.broadcasted_iota(jnp.int32, values.shape, values.ndim - 1)
    if steps == 1:
        first, second = values[..., box_size - 1 : box_size], values[..., 2 * box_size - 1 :]
        rolled = jnp.where(column == 0, first, rolled)
        return jnp.where(column == box_size, second, rolled)
    first, second = values[..., 0:1], values[..., box_size : box_size + 1]
    rolled = jnp.where(column == box_size - 1, first, rolled)
    return jnp.where(column == 2 * box_size - 1, second, rolled)


def low_row_ids(block_ids, box_size):
    base = block_ids * RB + jnp.where(block_ids < LOW, 0, box_size - 2 * LOW * RB)
    return base[..., None] + jnp.arange(RB, dtype=jnp.int32)


def power_gather(total, device_count, rows, box_size):
    spread = jnp.broadcast_to(total, (device_count, total.shape[1]))
    back = lax.all_to_all(spread, ("img", "slab"), 0, 0, tiled=True)
    half = back.reshape(rows, box_size)[: box_size // 2 + 1]
    mirrored = jnp.roll(half[1 : box_size // 2][::-1, ::-1], 1, axis=1)
    return jnp.concatenate([half, mirrored], axis=0)


def half_rows(box_size, device_count):
    rows = box_size // 2 + 1
    while (rows * box_size) % device_count:
        rows += 1
    return rows


def body(images, micrograph, defocus, target_slab, target_plane, target_rows, shift_index, volume):
    particles, box_size = (images.shape[0], images.shape[1])
    slab_count = lax.axis_size("slab")
    img_count = lax.axis_size("img")
    device_count = img_count * slab_count
    low_rows = LOW * RB
    blocks_per = 2 * LOW
    routed = particles * blocks_per
    planes, vrows = volume.shape[0], volume.shape[1]
    row_blocks = vrows // RB
    slots = planes * row_blocks
    tables = lax.optimization_barrier(table_stack(box_size))

    destination = target_slab.reshape(routed)
    capacity = max(2, (2 * routed + slab_count - 1) // slab_count)
    member = (destination[:, None] == jnp.arange(slab_count, dtype=jnp.int32)[None, :]).astype(
        jnp.int32
    )
    before = jnp.cumsum(member, axis=0) - member
    slot_rank = jnp.sum(member * before, axis=1)
    seat_index = destination * capacity + slot_rank
    seat_count = slab_count * capacity
    seat_pick = (seat_index[:, None] == jnp.arange(seat_count, dtype=jnp.int32)[None, :]).astype(
        jnp.bfloat16
    )
    source_block = jnp.tile(jnp.arange(blocks_per, dtype=jnp.int32), particles)
    block_info = jnp.stack(
        [
            jnp.ones((routed,), jnp.int32),
            target_plane.reshape(routed),
            target_rows.reshape(routed),
            shift_index.reshape(routed),
            source_block,
            jnp.repeat(micrograph, blocks_per),
        ],
        axis=1,
    ).astype(jnp.bfloat16)
    info_width = 128
    block_info = jnp.pad(block_info, ((0, 0), (0, info_width - block_info.shape[1])))

    spectrum = jnp.stack([transform(images[n], tables) for n in range(particles)])
    low_spectrum = jnp.concatenate(
        [spectrum[:, :, :low_rows], spectrum[:, :, box_size - low_rows :]], axis=2
    ).astype(jnp.bfloat16)
    low_spectrum = jnp.moveaxis(low_spectrum, 1, 2).reshape(routed, RB * 2 * box_size)
    payload = jnp.concatenate([low_spectrum, block_info], axis=1)
    send = jnp.einsum(
        "rs,rx->sx", seat_pick, payload, preferred_element_type=jnp.float32
    ).astype(jnp.bfloat16)
    rows_half = half_rows(box_size, device_count)
    low_half = spectrum[:, :, :rows_half]
    power_half = jnp.sum(low_half * low_half, axis=(0, 1))
    pieces = power_half.reshape(device_count, rows_half * box_size // device_count)
    gathered = lax.all_to_all(pieces, ("img", "slab"), 0, 0, tiled=True)
    gathered, send = lax.optimization_barrier((gathered, send))
    got = lax.all_to_all(send, "slab", 0, 0, tiled=True)
    got_blocks = got[:, : RB * 2 * box_size].reshape(seat_count, RB, 2 * box_size)
    got_info = got[:, RB * 2 * box_size : RB * 2 * box_size + 6].astype(jnp.int32)

    live = got_info[:, 0].astype(jnp.float32)[:, None, None]
    slot_of = got_info[:, 1] * row_blocks + got_info[:, 2]
    slot_pick = (slot_of[:, None] == jnp.arange(slots, dtype=jnp.int32)[None, :]).astype(
        jnp.bfloat16
    )
    blend_weight = ((got_info[:, 3].astype(jnp.float32) + 0.5) / WL)[:, None, None]
    volume_slots = volume.reshape(slots, RB, 2 * box_size)
    nearby = jnp.einsum(
        "sq,qrx->srx", slot_pick, volume_slots, preferred_element_type=jnp.float32
    )
    projected = (
        ((1.0 - blend_weight) * nearby + blend_weight * shift_halves(nearby, -1, box_size)) * live
    ).astype(jnp.bfloat16)

    total = jnp.sum(gathered, axis=0, keepdims=True)
    total, got = lax.optimization_barrier((total, got))
    power = power_gather(total, device_count, rows_half, box_size)
    noise_level = jnp.sqrt(power / (particles * device_count) + 1e-06)
    level_both = jnp.concatenate([noise_level, noise_level], axis=1)

    projected, power = lax.optimization_barrier((projected, power))
    returned_rows = lax.all_to_all(projected, "slab", 0, 0, tiled=True)

    got_rows = low_row_ids(got_info[:, 4], box_size)
    got_contrast = contrast_curve(lookup_defocus(got_info[:, 5], defocus), got_rows, box_size)
    got_level = level_both[got_rows]
    got_contrast_both = jnp.concatenate([got_contrast, got_contrast], axis=-1).astype(jnp.float32)
    received = got_contrast_both * got_blocks.astype(jnp.float32) / got_level
    inserted = (1.0 - blend_weight) * received + blend_weight * shift_halves(received, 1, box_size)
    contrast_rows = got_contrast.astype(jnp.float32)
    squared = contrast_rows * contrast_rows
    weights = (1.0 - blend_weight) * squared + blend_weight * jnp.roll(squared, 1, axis=-1)
    seat_data = jnp.concatenate([inserted, weights], axis=-1) * live
    numerator = jnp.einsum(
        "sq,srx->qrx", slot_pick.astype(jnp.float32), seat_data, precision=HI,
        preferred_element_type=jnp.float32,
    )
    share = vrows // img_count
    numerator = numerator.reshape(planes, img_count, share, 3 * box_size).astype(jnp.bfloat16)
    numerator = jnp.swapaxes(numerator, 0, 1)
    numerator, returned_rows = lax.optimization_barrier((numerator, returned_rows))
    parts = lax.all_to_all(numerator, "img", 0, 0, tiled=True)
    volume_part = jnp.sum(parts.astype(jnp.float32), axis=0)
    weight_sum = volume_part[..., 2 * box_size :]
    reconstruction = volume_part[..., : 2 * box_size] / (
        jnp.concatenate([weight_sum, weight_sum], axis=-1) + 1.0
    )

    whitened = spectrum / noise_level
    row_all = jnp.arange(box_size, dtype=jnp.int32)[None, :]
    contrast = contrast_curve(lookup_defocus(micrograph, defocus), row_all, box_size)
    own_rows = jnp.einsum(
        "rs,sx->rx", seat_pick, returned_rows.reshape(seat_count, RB * 2 * box_size),
        preferred_element_type=jnp.float32,
    ).astype(jnp.bfloat16)
    own_rows = own_rows.reshape(particles, 2 * low_rows, 2, box_size)
    own_rows = jnp.moveaxis(own_rows, 2, 1)
    middle = jnp.zeros((particles, 2, box_size - 2 * low_rows, box_size), jnp.bfloat16)
    full_projection = jnp.concatenate(
        [own_rows[:, :, :low_rows], middle, own_rows[:, :, low_rows:]], axis=2
    )
    difference = (
        whitened - contrast.astype(jnp.float32)[:, None] * full_projection.astype(jnp.float32)
    ).astype(jnp.bfloat16)
    residual = jnp.stack([invert(difference[n], tables, box_size) for n in range(particles)])
    return (residual, reconstruction)


def solution(mesh):
    in_specs = (
        P(("img", "slab"), None, None),
        P(("img", "slab")),
        P(),
        P(("img", "slab"), None, None),
        P(("img", "slab"), None),
        P(("img", "slab"), None),
        P(("img", "slab"), None),
        P("slab", None, None),
    )
    out_specs = (P(("img", "slab"), None, None), P("slab", "img", None))
    return jax.shard_map(body, mesh=mesh, in_specs=in_specs, out_specs=out_specs, check_vma=False)
```

```python
import math

import jax
import ml_dtypes
import numpy as np
import jax.numpy as jnp
from jax import lax
from jax.sharding import PartitionSpec as P

RB = 16
LOW = 4
WL = 8
HI = lax.Precision.HIGHEST


def table_stack(box_size):
    positions = np.arange(box_size)
    angles = ((positions[:, None] * positions[None, :]) % box_size) * (2.0 * np.pi / box_size)
    both = np.stack([np.cos(angles), np.sin(angles)]).astype(ml_dtypes.bfloat16)
    return jnp.asarray(both)


def transform(image, tables):
    rowwise = jnp.einsum(
        "yx,hmx->hym", image, tables, preferred_element_type=jnp.float32
    ).astype(jnp.bfloat16)
    products = jnp.einsum("gky,hym->ghkm", tables, rowwise, preferred_element_type=jnp.float32)
    real = products[0, 0] - products[1, 1]
    imag = -(products[0, 1] + products[1, 0])
    return jnp.stack([real, imag])


def invert(difference, tables, box_size):
    products = jnp.einsum(
        "hyj,gmj->hgym", difference, tables, preferred_element_type=jnp.float32
    )
    back_real = products[0, 0] - products[1, 1]
    back_imag = products[0, 1] + products[1, 0]
    back_rows = jnp.stack([back_real, -back_imag]).astype(jnp.bfloat16)
    picture = jnp.einsum("hxk,hkm->hxm", tables, back_rows, preferred_element_type=jnp.float32)
    return ((picture[0] + picture[1]) / box_size).astype(jnp.bfloat16)


def radius_sq(row_ids, box_size):
    half_size = box_size // 2
    columns = jnp.arange(box_size, dtype=jnp.int32)
    freq_rows = jnp.where(row_ids < half_size, row_ids, row_ids - box_size)
    freq_cols = jnp.where(columns < half_size, columns, columns - box_size)
    total = freq_rows[..., None] * freq_rows[..., None] + freq_cols * freq_cols
    return total.astype(jnp.float32) / float(half_size * half_size)


def contrast_curve(defocus_of, row_ids, box_size):
    radius = radius_sq(row_ids, box_size)
    return (-jnp.sin(defocus_of[:, None, None] * radius + 0.1)).astype(jnp.bfloat16)


def lookup_defocus(mic_ids, defocus):
    labels = jnp.arange(defocus.shape[0], dtype=jnp.int32)
    return jnp.sum(jnp.where(mic_ids[:, None] == labels[None, :], defocus[None, :], 0.0), axis=1)


def shift_halves(values, steps, box_size):
    rolled = jnp.roll(values, steps, axis=-1)
    column = lax.broadcasted_iota(jnp.int32, values.shape, values.ndim - 1)
    if steps == 1:
        first, second = values[..., box_size - 1 : box_size], values[..., 2 * box_size - 1 :]
        rolled = jnp.where(column == 0, first, rolled)
        return jnp.where(column == box_size, second, rolled)
    first, second = values[..., 0:1], values[..., box_size : box_size + 1]
    rolled = jnp.where(column == box_size - 1, first, rolled)
    return jnp.where(column == 2 * box_size - 1, second, rolled)


def low_row_ids(block_ids, box_size):
    base = block_ids * RB + jnp.where(block_ids < LOW, 0, box_size - 2 * LOW * RB)
    return base[..., None] + jnp.arange(RB, dtype=jnp.int32)


def power_gather(total, device_count, rows, box_size):
    spread = jnp.broadcast_to(total, (device_count, total.shape[1]))
    back = lax.all_to_all(spread, ("img", "slab"), 0, 0, tiled=True)
    half = back.reshape(rows, box_size)[: box_size // 2 + 1].astype(jnp.float32)
    mirrored = jnp.roll(half[1 : box_size // 2][::-1, ::-1], 1, axis=1)
    return jnp.concatenate([half, mirrored], axis=0)


def half_rows(box_size, device_count):
    rows = box_size // 2 + 1
    while (rows * box_size) % device_count:
        rows += 1
    return rows


def body(images, micrograph, defocus, target_slab, target_plane, target_rows, shift_index, volume):
    particles, box_size = (images.shape[0], images.shape[1])
    slab_count = lax.axis_size("slab")
    img_count = lax.axis_size("img")
    device_count = img_count * slab_count
    low_rows = LOW * RB
    blocks_per = 2 * LOW
    routed = particles * blocks_per
    planes, vrows = volume.shape[0], volume.shape[1]
    row_blocks = vrows // RB
    slots = planes * row_blocks
    tables = lax.optimization_barrier(table_stack(box_size))

    destination = target_slab.reshape(routed)
    capacity = max(2, (2 * routed + slab_count - 1) // slab_count)
    member = (destination[:, None] == jnp.arange(slab_count, dtype=jnp.int32)[None, :]).astype(
        jnp.int32
    )
    before = jnp.cumsum(member, axis=0) - member
    slot_rank = jnp.sum(member * before, axis=1)
    seat_index = destination * capacity + slot_rank
    seat_count = slab_count * capacity
    seat_pick = (seat_index[:, None] == jnp.arange(seat_count, dtype=jnp.int32)[None, :]).astype(
        jnp.bfloat16
    )
    source_block = jnp.tile(jnp.arange(blocks_per, dtype=jnp.int32), particles)
    block_info = jnp.stack(
        [
            jnp.ones((routed,), jnp.int32),
            target_plane.reshape(routed),
            target_rows.reshape(routed),
            shift_index.reshape(routed),
            source_block,
            jnp.repeat(micrograph, blocks_per),
        ],
        axis=1,
    ).astype(jnp.bfloat16)
    info_width = 128
    block_info = jnp.pad(block_info, ((0, 0), (0, info_width - block_info.shape[1])))

    spectrum = jnp.stack([transform(images[n], tables) for n in range(particles)])
    low_spectrum = jnp.concatenate(
        [spectrum[:, :, :low_rows], spectrum[:, :, box_size - low_rows :]], axis=2
    ).astype(jnp.bfloat16)
    low_spectrum = jnp.moveaxis(low_spectrum, 1, 2).reshape(routed, RB * 2 * box_size)
    payload = jnp.concatenate([low_spectrum, block_info], axis=1)
    send = jnp.einsum(
        "rs,rx->sx", seat_pick, payload, preferred_element_type=jnp.float32
    ).astype(jnp.bfloat16)
    rows_half = half_rows(box_size, device_count)
    low_half = spectrum[:, :, :rows_half]
    power_half = jnp.sum(low_half * low_half, axis=(0, 1))
    pieces = power_half.reshape(device_count, rows_half * box_size // device_count)
    gathered = lax.all_to_all(pieces.astype(jnp.bfloat16), ("img", "slab"), 0, 0, tiled=True)
    gathered, send = lax.optimization_barrier((gathered, send))
    got = lax.all_to_all(send, "slab", 0, 0, tiled=True)
    got_blocks = got[:, : RB * 2 * box_size].reshape(seat_count, RB, 2 * box_size)
    got_info = got[:, RB * 2 * box_size : RB * 2 * box_size + 6].astype(jnp.int32)

    live = got_info[:, 0].astype(jnp.float32)[:, None, None]
    slot_of = got_info[:, 1] * row_blocks + got_info[:, 2]
    slot_pick = (slot_of[:, None] == jnp.arange(slots, dtype=jnp.int32)[None, :]).astype(
        jnp.bfloat16
    )
    blend_weight = ((got_info[:, 3].astype(jnp.float32) + 0.5) / WL)[:, None, None]
    volume_slots = volume.reshape(slots, RB, 2 * box_size)
    nearby = jnp.einsum(
        "sq,qrx->srx", slot_pick, volume_slots, preferred_element_type=jnp.float32
    )
    projected = (
        ((1.0 - blend_weight) * nearby + blend_weight * shift_halves(nearby, -1, box_size)) * live
    ).astype(jnp.bfloat16)

    total = jnp.sum(gathered.astype(jnp.float32), axis=0, keepdims=True).astype(jnp.bfloat16)
    total, got = lax.optimization_barrier((total, got))
    power = power_gather(total, device_count, rows_half, box_size)
    noise_level = jnp.sqrt(power / (particles * device_count) + 1e-06)
    level_both = jnp.concatenate([noise_level, noise_level], axis=1)

    projected, power = lax.optimization_barrier((projected, power))
    returned_rows = lax.all_to_all(projected, "slab", 0, 0, tiled=True)

    got_rows = low_row_ids(got_info[:, 4], box_size)
    got_contrast = contrast_curve(lookup_defocus(got_info[:, 5], defocus), got_rows, box_size)
    got_level = level_both[got_rows]
    got_contrast_both = jnp.concatenate([got_contrast, got_contrast], axis=-1).astype(jnp.float32)
    received = got_contrast_both * got_blocks.astype(jnp.float32) / got_level
    inserted = (1.0 - blend_weight) * received + blend_weight * shift_halves(received, 1, box_size)
    contrast_rows = got_contrast.astype(jnp.float32)
    squared = contrast_rows * contrast_rows
    weights = (1.0 - blend_weight) * squared + blend_weight * jnp.roll(squared, 1, axis=-1)
    seat_data = jnp.concatenate([inserted, weights], axis=-1) * live
    numerator = jnp.einsum(
        "sq,srx->qrx", slot_pick.astype(jnp.float32), seat_data, precision=HI,
        preferred_element_type=jnp.float32,
    )
    share = vrows // img_count
    numerator = numerator.reshape(planes, img_count, share, 3 * box_size).astype(jnp.bfloat16)
    numerator = jnp.swapaxes(numerator, 0, 1)
    numerator, returned_rows = lax.optimization_barrier((numerator, returned_rows))
    parts = lax.all_to_all(numerator, "img", 0, 0, tiled=True)
    volume_part = jnp.sum(parts.astype(jnp.float32), axis=0)
    weight_sum = volume_part[..., 2 * box_size :]
    reconstruction = volume_part[..., : 2 * box_size] / (
        jnp.concatenate([weight_sum, weight_sum], axis=-1) + 1.0
    )

    whitened = spectrum / noise_level
    row_all = jnp.arange(box_size, dtype=jnp.int32)[None, :]
    contrast = contrast_curve(lookup_defocus(micrograph, defocus), row_all, box_size)
    own_rows = jnp.einsum(
        "rs,sx->rx", seat_pick, returned_rows.reshape(seat_count, RB * 2 * box_size),
        preferred_element_type=jnp.float32,
    ).astype(jnp.bfloat16)
    own_rows = own_rows.reshape(particles, 2 * low_rows, 2, box_size)
    own_rows = jnp.moveaxis(own_rows, 2, 1)
    middle = jnp.zeros((particles, 2, box_size - 2 * low_rows, box_size), jnp.bfloat16)
    full_projection = jnp.concatenate(
        [own_rows[:, :, :low_rows], middle, own_rows[:, :, low_rows:]], axis=2
    )
    difference = (
        whitened - contrast.astype(jnp.float32)[:, None] * full_projection.astype(jnp.float32)
    ).astype(jnp.bfloat16)
    residual = jnp.stack([invert(difference[n], tables, box_size) for n in range(particles)])
    return (residual, reconstruction)


def solution(mesh):
    in_specs = (
        P(("img", "slab"), None, None),
        P(("img", "slab")),
        P(),
        P(("img", "slab"), None, None),
        P(("img", "slab"), None),
        P(("img", "slab"), None),
        P(("img", "slab"), None),
        P("slab", None, None),
    )
    out_specs = (P(("img", "slab"), None, None), P("slab", "img", None))
    return jax.shard_map(body, mesh=mesh, in_specs=in_specs, out_specs=out_specs, check_vma=False)
```

```python
import math

import jax
import ml_dtypes
import numpy as np
import jax.numpy as jnp
from jax import lax
from jax.sharding import PartitionSpec as P

RB = 16
LOW = 4
WL = 8
HI = lax.Precision.HIGHEST


def table_stack(box_size):
    positions = np.arange(box_size)
    angles = ((positions[:, None] * positions[None, :]) % box_size) * (2.0 * np.pi / box_size)
    both = np.stack([np.cos(angles), np.sin(angles)]).astype(ml_dtypes.bfloat16)
    return jnp.asarray(both)


def transform(image, tables):
    rowwise = jnp.einsum(
        "yx,hmx->hym", image, tables, preferred_element_type=jnp.float32
    ).astype(jnp.bfloat16)
    products = jnp.einsum("gky,hym->ghkm", tables, rowwise, preferred_element_type=jnp.float32)
    real = products[0, 0] - products[1, 1]
    imag = -(products[0, 1] + products[1, 0])
    return jnp.stack([real, imag])


def invert(difference, tables, box_size):
    products = jnp.einsum(
        "hyj,gmj->hgym", difference, tables, preferred_element_type=jnp.float32
    )
    back_real = products[0, 0] - products[1, 1]
    back_imag = products[0, 1] + products[1, 0]
    back_rows = jnp.stack([back_real, -back_imag]).astype(jnp.bfloat16)
    picture = jnp.einsum("hxk,hkm->hxm", tables, back_rows, preferred_element_type=jnp.float32)
    return ((picture[0] + picture[1]) / box_size).astype(jnp.bfloat16)


def radius_sq(row_ids, box_size):
    half_size = box_size // 2
    columns = jnp.arange(box_size, dtype=jnp.int32)
    freq_rows = jnp.where(row_ids < half_size, row_ids, row_ids - box_size)
    freq_cols = jnp.where(columns < half_size, columns, columns - box_size)
    total = freq_rows[..., None] * freq_rows[..., None] + freq_cols * freq_cols
    return total.astype(jnp.float32) / float(half_size * half_size)


def contrast_curve(defocus_of, row_ids, box_size):
    radius = radius_sq(row_ids, box_size)
    return (-jnp.sin(defocus_of[:, None, None] * radius + 0.1)).astype(jnp.bfloat16)


def lookup_defocus(mic_ids, defocus):
    labels = jnp.arange(defocus.shape[0], dtype=jnp.int32)
    return jnp.sum(jnp.where(mic_ids[:, None] == labels[None, :], defocus[None, :], 0.0), axis=1)


def shift_halves(values, steps, box_size):
    rolled = jnp.roll(values, steps, axis=-1)
    column = lax.broadcasted_iota(jnp.int32, values.shape, values.ndim - 1)
    if steps == 1:
        first, second = values[..., box_size - 1 : box_size], values[..., 2 * box_size - 1 :]
        rolled = jnp.where(column == 0, first, rolled)
        return jnp.where(column == box_size, second, rolled)
    first, second = values[..., 0:1], values[..., box_size : box_size + 1]
    rolled = jnp.where(column == box_size - 1, first, rolled)
    return jnp.where(column == 2 * box_size - 1, second, rolled)


def low_row_ids(block_ids, box_size):
    base = block_ids * RB + jnp.where(block_ids < LOW, 0, box_size - 2 * LOW * RB)
    return base[..., None] + jnp.arange(RB, dtype=jnp.int32)


def power_gather(total, device_count, rows, box_size):
    spread = jnp.broadcast_to(total, (device_count, total.shape[1]))
    back = lax.all_to_all(spread, ("img", "slab"), 0, 0, tiled=True)
    half = back.reshape(rows, box_size)[: box_size // 2 + 1]
    mirrored = jnp.roll(half[1 : box_size // 2][::-1, ::-1], 1, axis=1)
    return jnp.concatenate([half, mirrored], axis=0)


def shift_exchange(values, count, capacity, direction):
    pieces = [values[:capacity]]
    for d in range(1, count):
        pairs = [(i, (i + direction * d) % count) for i in range(count)]
        pieces.append(lax.ppermute(values[d * capacity : (d + 1) * capacity], "slab", pairs))
    return jnp.concatenate(pieces, axis=0)


def reduce_over_img(numerator, count):
    me = lax.axis_index("img")
    total = lax.dynamic_index_in_dim(numerator, me, 0, keepdims=False).astype(jnp.float32)
    for d in range(1, count):
        piece = lax.dynamic_index_in_dim(numerator, (me + d) % count, 0, keepdims=False)
        pairs = [(i, (i + d) % count) for i in range(count)]
        total = total + lax.ppermute(piece, "img", pairs).astype(jnp.float32)
    return total


def half_rows(box_size, device_count):
    rows = box_size // 2 + 1
    while (rows * box_size) % device_count:
        rows += 1
    return rows


def body(images, micrograph, defocus, target_slab, target_plane, target_rows, shift_index, volume):
    particles, box_size = (images.shape[0], images.shape[1])
    slab_count = lax.axis_size("slab")
    img_count = lax.axis_size("img")
    device_count = img_count * slab_count
    low_rows = LOW * RB
    blocks_per = 2 * LOW
    routed = particles * blocks_per
    planes, vrows = volume.shape[0], volume.shape[1]
    row_blocks = vrows // RB
    slots = planes * row_blocks
    tables = lax.optimization_barrier(table_stack(box_size))

    destination = target_slab.reshape(routed)
    capacity = max(2, (2 * routed + slab_count - 1) // slab_count)
    member = (destination[:, None] == jnp.arange(slab_count, dtype=jnp.int32)[None, :]).astype(
        jnp.int32
    )
    before = jnp.cumsum(member, axis=0) - member
    slot_rank = jnp.sum(member * before, axis=1)
    me = lax.axis_index("slab")
    seat_index = ((destination - me) % slab_count) * capacity + slot_rank
    seat_count = slab_count * capacity
    seat_pick = (seat_index[:, None] == jnp.arange(seat_count, dtype=jnp.int32)[None, :]).astype(
        jnp.bfloat16
    )
    source_block = jnp.tile(jnp.arange(blocks_per, dtype=jnp.int32), particles)
    block_info = jnp.stack(
        [
            jnp.ones((routed,), jnp.int32),
            target_plane.reshape(routed),
            target_rows.reshape(routed),
            shift_index.reshape(routed),
            source_block,
            jnp.repeat(micrograph, blocks_per),
        ],
        axis=1,
    ).astype(jnp.bfloat16)
    info_width = 128
    block_info = jnp.pad(block_info, ((0, 0), (0, info_width - block_info.shape[1])))

    spectrum = jnp.stack([transform(images[n], tables) for n in range(particles)])
    low_spectrum = jnp.concatenate(
        [spectrum[:, :, :low_rows], spectrum[:, :, box_size - low_rows :]], axis=2
    ).astype(jnp.bfloat16)
    low_spectrum = jnp.moveaxis(low_spectrum, 1, 2).reshape(routed, RB * 2 * box_size)
    payload = jnp.concatenate([low_spectrum, block_info], axis=1)
    send = jnp.einsum(
        "rs,rx->sx", seat_pick, payload, preferred_element_type=jnp.float32
    ).astype(jnp.bfloat16)
    rows_half = half_rows(box_size, device_count)
    low_half = spectrum[:, :, :rows_half]
    power_half = jnp.sum(low_half * low_half, axis=(0, 1))
    pieces = power_half.reshape(device_count, rows_half * box_size // device_count)
    gathered = lax.all_to_all(pieces, ("img", "slab"), 0, 0, tiled=True)
    got = shift_exchange(send, slab_count, capacity, 1)
    got_blocks = got[:, : RB * 2 * box_size].reshape(seat_count, RB, 2 * box_size)
    got_info = got[:, RB * 2 * box_size : RB * 2 * box_size + 6].astype(jnp.int32)

    live = got_info[:, 0].astype(jnp.float32)[:, None, None]
    slot_of = got_info[:, 1] * row_blocks + got_info[:, 2]
    slot_pick = (slot_of[:, None] == jnp.arange(slots, dtype=jnp.int32)[None, :]).astype(
        jnp.bfloat16
    )
    blend_weight = ((got_info[:, 3].astype(jnp.float32) + 0.5) / WL)[:, None, None]
    volume_slots = volume.reshape(slots, RB, 2 * box_size)
    nearby = jnp.einsum(
        "sq,qrx->srx", slot_pick, volume_slots, preferred_element_type=jnp.float32
    )
    projected = (
        ((1.0 - blend_weight) * nearby + blend_weight * shift_halves(nearby, -1, box_size)) * live
    ).astype(jnp.bfloat16)

    total = jnp.sum(gathered, axis=0, keepdims=True)
    power = power_gather(total, device_count, rows_half, box_size)
    noise_level = jnp.sqrt(power / (particles * device_count) + 1e-06)
    level_both = jnp.concatenate([noise_level, noise_level], axis=1)

    returned_rows = shift_exchange(projected, slab_count, capacity, -1)

    got_rows = low_row_ids(got_info[:, 4], box_size)
    got_contrast = contrast_curve(lookup_defocus(got_info[:, 5], defocus), got_rows, box_size)
    got_level = level_both[got_rows]
    got_contrast_both = jnp.concatenate([got_contrast, got_contrast], axis=-1).astype(jnp.float32)
    received = got_contrast_both * got_blocks.astype(jnp.float32) / got_level
    inserted = (1.0 - blend_weight) * received + blend_weight * shift_halves(received, 1, box_size)
    contrast_rows = got_contrast.astype(jnp.float32)
    squared = contrast_rows * contrast_rows
    weights = (1.0 - blend_weight) * squared + blend_weight * jnp.roll(squared, 1, axis=-1)
    seat_data = jnp.concatenate([inserted, weights], axis=-1) * live
    numerator = jnp.einsum(
        "sq,srx->qrx", slot_pick.astype(jnp.float32), seat_data, precision=HI,
        preferred_element_type=jnp.float32,
    )
    share = vrows // img_count
    numerator = numerator.reshape(planes, img_count, share, 3 * box_size).astype(jnp.bfloat16)
    numerator = jnp.swapaxes(numerator, 0, 1)
    volume_part = reduce_over_img(numerator, img_count)
    weight_sum = volume_part[..., 2 * box_size :]
    reconstruction = volume_part[..., : 2 * box_size] / (
        jnp.concatenate([weight_sum, weight_sum], axis=-1) + 1.0
    )

    whitened = spectrum / noise_level
    row_all = jnp.arange(box_size, dtype=jnp.int32)[None, :]
    contrast = contrast_curve(lookup_defocus(micrograph, defocus), row_all, box_size)
    own_rows = jnp.einsum(
        "rs,sx->rx", seat_pick, returned_rows.reshape(seat_count, RB * 2 * box_size),
        preferred_element_type=jnp.float32,
    ).astype(jnp.bfloat16)
    own_rows = own_rows.reshape(particles, 2 * low_rows, 2, box_size)
    own_rows = jnp.moveaxis(own_rows, 2, 1)
    middle = jnp.zeros((particles, 2, box_size - 2 * low_rows, box_size), jnp.bfloat16)
    full_projection = jnp.concatenate(
        [own_rows[:, :, :low_rows], middle, own_rows[:, :, low_rows:]], axis=2
    )
    difference = (
        whitened - contrast.astype(jnp.float32)[:, None] * full_projection.astype(jnp.float32)
    ).astype(jnp.bfloat16)
    residual = jnp.stack([invert(difference[n], tables, box_size) for n in range(particles)])
    return (residual, reconstruction)


def solution(mesh):
    in_specs = (
        P(("img", "slab"), None, None),
        P(("img", "slab")),
        P(),
        P(("img", "slab"), None, None),
        P(("img", "slab"), None),
        P(("img", "slab"), None),
        P(("img", "slab"), None),
        P("slab", None, None),
    )
    out_specs = (P(("img", "slab"), None, None), P("slab", "img", None))
    return jax.shard_map(body, mesh=mesh, in_specs=in_specs, out_specs=out_specs, check_vma=False)
```

```python
import math

import jax
import ml_dtypes
import numpy as np
import jax.numpy as jnp
from jax import lax
from jax.sharding import PartitionSpec as P

RB = 16
LOW = 4
WL = 8
HI = lax.Precision.HIGHEST


def table_stack(box_size):
    positions = np.arange(box_size)
    angles = ((positions[:, None] * positions[None, :]) % box_size) * (2.0 * np.pi / box_size)
    both = np.stack([np.cos(angles), np.sin(angles)]).astype(ml_dtypes.bfloat16)
    return jnp.asarray(both)


def transform(image, tables):
    rowwise = jnp.einsum(
        "yx,hmx->hym", image, tables, preferred_element_type=jnp.float32
    ).astype(jnp.bfloat16)
    products = jnp.einsum("gky,hym->ghkm", tables, rowwise, preferred_element_type=jnp.float32)
    real = products[0, 0] - products[1, 1]
    imag = -(products[0, 1] + products[1, 0])
    return jnp.stack([real, imag])


def invert(difference, tables, box_size):
    products = jnp.einsum(
        "hyj,gmj->hgym", difference, tables, preferred_element_type=jnp.float32
    )
    back_real = products[0, 0] - products[1, 1]
    back_imag = products[0, 1] + products[1, 0]
    back_rows = jnp.stack([back_real, -back_imag]).astype(jnp.bfloat16)
    picture = jnp.einsum("hxk,hkm->hxm", tables, back_rows, preferred_element_type=jnp.float32)
    return ((picture[0] + picture[1]) / box_size).astype(jnp.bfloat16)


def radius_sq(row_ids, box_size):
    half_size = box_size // 2
    columns = jnp.arange(box_size, dtype=jnp.int32)
    freq_rows = jnp.where(row_ids < half_size, row_ids, row_ids - box_size)
    freq_cols = jnp.where(columns < half_size, columns, columns - box_size)
    total = freq_rows[..., None] * freq_rows[..., None] + freq_cols * freq_cols
    return total.astype(jnp.float32) / float(half_size * half_size)


def contrast_curve(defocus_of, row_ids, box_size):
    radius = radius_sq(row_ids, box_size)
    return (-jnp.sin(defocus_of[:, None, None] * radius + 0.1)).astype(jnp.bfloat16)


def lookup_defocus(mic_ids, defocus):
    labels = jnp.arange(defocus.shape[0], dtype=jnp.int32)
    return jnp.sum(jnp.where(mic_ids[:, None] == labels[None, :], defocus[None, :], 0.0), axis=1)


def shift_halves(values, steps, box_size):
    rolled = jnp.roll(values, steps, axis=-1)
    column = lax.broadcasted_iota(jnp.int32, values.shape, values.ndim - 1)
    if steps == 1:
        first, second = values[..., box_size - 1 : box_size], values[..., 2 * box_size - 1 :]
        rolled = jnp.where(column == 0, first, rolled)
        return jnp.where(column == box_size, second, rolled)
    first, second = values[..., 0:1], values[..., box_size : box_size + 1]
    rolled = jnp.where(column == box_size - 1, first, rolled)
    return jnp.where(column == 2 * box_size - 1, second, rolled)


def low_row_ids(block_ids, box_size):
    base = block_ids * RB + jnp.where(block_ids < LOW, 0, box_size - 2 * LOW * RB)
    return base[..., None] + jnp.arange(RB, dtype=jnp.int32)


def power_gather(total, device_count, rows, box_size):
    spread = jnp.broadcast_to(total, (device_count, total.shape[1]))
    back = lax.all_to_all(spread, ("img", "slab"), 0, 0, tiled=True)
    half = back.reshape(rows, box_size)[: box_size // 2 + 1]
    mirrored = jnp.roll(half[1 : box_size // 2][::-1, ::-1], 1, axis=1)
    return jnp.concatenate([half, mirrored], axis=0)


def shift_exchange(values, count, capacity, direction):
    pieces = [values[:capacity]]
    for d in range(1, count):
        pairs = [(i, (i + direction * d) % count) for i in range(count)]
        pieces.append(lax.ppermute(values[d * capacity : (d + 1) * capacity], "slab", pairs))
    return jnp.concatenate(pieces, axis=0)


def reduce_over_img(numerator, count):
    me = lax.axis_index("img")
    total = lax.dynamic_index_in_dim(numerator, me, 0, keepdims=False).astype(jnp.float32)
    for d in range(1, count):
        piece = lax.dynamic_index_in_dim(numerator, (me + d) % count, 0, keepdims=False)
        pairs = [(i, (i + d) % count) for i in range(count)]
        total = total + lax.ppermute(piece, "img", pairs).astype(jnp.float32)
    return total


def half_rows(box_size, device_count):
    rows = box_size // 2 + 1
    while (rows * box_size) % device_count:
        rows += 1
    return rows


def body(images, micrograph, defocus, target_slab, target_plane, target_rows, shift_index, volume):
    particles, box_size = (images.shape[0], images.shape[1])
    slab_count = lax.axis_size("slab")
    img_count = lax.axis_size("img")
    device_count = img_count * slab_count
    low_rows = LOW * RB
    blocks_per = 2 * LOW
    routed = particles * blocks_per
    planes, vrows = volume.shape[0], volume.shape[1]
    row_blocks = vrows // RB
    slots = planes * row_blocks
    tables = lax.optimization_barrier(table_stack(box_size))

    destination = target_slab.reshape(routed)
    capacity = max(2, (2 * routed + slab_count - 1) // slab_count)
    member = (destination[:, None] == jnp.arange(slab_count, dtype=jnp.int32)[None, :]).astype(
        jnp.int32
    )
    before = jnp.cumsum(member, axis=0) - member
    slot_rank = jnp.sum(member * before, axis=1)
    me = lax.axis_index("slab")
    seat_index = ((destination - me) % slab_count) * capacity + slot_rank
    seat_count = slab_count * capacity
    seat_pick = (seat_index[:, None] == jnp.arange(seat_count, dtype=jnp.int32)[None, :]).astype(
        jnp.bfloat16
    )
    source_block = jnp.tile(jnp.arange(blocks_per, dtype=jnp.int32), particles)
    block_info = jnp.stack(
        [
            jnp.ones((routed,), jnp.int32),
            target_plane.reshape(routed),
            target_rows.reshape(routed),
            shift_index.reshape(routed),
            source_block,
            jnp.repeat(micrograph, blocks_per),
        ],
        axis=1,
    ).astype(jnp.bfloat16)
    info_width = 128
    block_info = jnp.pad(block_info, ((0, 0), (0, info_width - block_info.shape[1])))

    spectrum = jnp.stack([transform(images[n], tables) for n in range(particles)])
    low_spectrum = jnp.concatenate(
        [spectrum[:, :, :low_rows], spectrum[:, :, box_size - low_rows :]], axis=2
    ).astype(jnp.bfloat16)
    low_spectrum = jnp.moveaxis(low_spectrum, 1, 2).reshape(routed, RB * 2 * box_size)
    payload = jnp.concatenate([low_spectrum, block_info], axis=1)
    send = jnp.einsum(
        "rs,rx->sx", seat_pick, payload, preferred_element_type=jnp.float32
    ).astype(jnp.bfloat16)
    rows_half = half_rows(box_size, device_count)
    low_half = spectrum[:, :, :rows_half]
    power_half = jnp.sum(low_half * low_half, axis=(0, 1))
    pieces = power_half.reshape(device_count, rows_half * box_size // device_count)
    gathered = lax.all_to_all(pieces, ("img", "slab"), 0, 0, tiled=True)
    got = shift_exchange(send, slab_count, capacity, 1)
    got_blocks = got[:, : RB * 2 * box_size].reshape(seat_count, RB, 2 * box_size)
    got_info = got[:, RB * 2 * box_size : RB * 2 * box_size + 6].astype(jnp.int32)

    live = got_info[:, 0].astype(jnp.float32)[:, None, None]
    slot_of = got_info[:, 1] * row_blocks + got_info[:, 2]
    slot_pick = (slot_of[:, None] == jnp.arange(slots, dtype=jnp.int32)[None, :]).astype(
        jnp.bfloat16
    )
    blend_weight = ((got_info[:, 3].astype(jnp.float32) + 0.5) / WL)[:, None, None]
    volume_slots = volume.reshape(planes, row_blocks, RB, 2, box_size)
    volume_slots = jnp.transpose(volume_slots, (0, 1, 3, 2, 4)).reshape(slots, 2, RB, box_size)
    nearby = jnp.einsum(
        "sq,qhix->shix", slot_pick, volume_slots, preferred_element_type=jnp.float32
    )
    blend_4 = blend_weight[:, :, :, None]
    projected = (
        ((1.0 - blend_4) * nearby + blend_4 * jnp.roll(nearby, -1, axis=-1)) * live[..., None]
    ).astype(jnp.bfloat16)

    total = jnp.sum(gathered, axis=0, keepdims=True)
    power = power_gather(total, device_count, rows_half, box_size)
    noise_level = jnp.sqrt(power / (particles * device_count) + 1e-06)
    level_both = jnp.concatenate([noise_level, noise_level], axis=1)

    returned_rows = shift_exchange(projected, slab_count, capacity, -1)

    got_rows = low_row_ids(got_info[:, 4], box_size)
    got_contrast = contrast_curve(lookup_defocus(got_info[:, 5], defocus), got_rows, box_size)
    level_low = jnp.concatenate(
        [level_both[:low_rows], level_both[box_size - low_rows :]], axis=0
    ).reshape(blocks_per, RB, 2 * box_size)
    block_pick = (got_info[:, 4:5] == jnp.arange(blocks_per, dtype=jnp.int32)[None, :]).astype(
        jnp.float32
    )
    got_level = jnp.einsum(
        "sj,jix->six", block_pick, level_low, precision=HI, preferred_element_type=jnp.float32
    )
    got_contrast_both = jnp.concatenate([got_contrast, got_contrast], axis=-1).astype(jnp.float32)
    received = got_contrast_both * got_blocks.astype(jnp.float32) / got_level
    inserted = (1.0 - blend_weight) * received + blend_weight * shift_halves(received, 1, box_size)
    contrast_rows = got_contrast.astype(jnp.float32)
    squared = contrast_rows * contrast_rows
    weights = (1.0 - blend_weight) * squared + blend_weight * jnp.roll(squared, 1, axis=-1)
    seat_data = jnp.concatenate([inserted, weights], axis=-1) * live
    numerator = jnp.einsum(
        "sq,srx->qrx", slot_pick.astype(jnp.float32), seat_data, precision=HI,
        preferred_element_type=jnp.float32,
    )
    share = vrows // img_count
    numerator = numerator.reshape(planes, img_count, share, 3 * box_size).astype(jnp.bfloat16)
    numerator = jnp.swapaxes(numerator, 0, 1)
    volume_part = reduce_over_img(numerator, img_count)
    weight_sum = volume_part[..., 2 * box_size :]
    reconstruction = volume_part[..., : 2 * box_size] / (
        jnp.concatenate([weight_sum, weight_sum], axis=-1) + 1.0
    )

    whitened = spectrum / noise_level
    row_all = jnp.arange(box_size, dtype=jnp.int32)[None, :]
    contrast = contrast_curve(lookup_defocus(micrograph, defocus), row_all, box_size)
    own_rows = jnp.einsum(
        "rs,shix->rhix", seat_pick, returned_rows, preferred_element_type=jnp.float32
    ).astype(jnp.bfloat16)
    own_rows = own_rows.reshape(particles, blocks_per, 2, RB, box_size)
    own_rows = jnp.moveaxis(own_rows, 2, 1).reshape(particles, 2, 2 * low_rows, box_size)
    middle = jnp.zeros((particles, 2, box_size - 2 * low_rows, box_size), jnp.bfloat16)
    full_projection = jnp.concatenate(
        [own_rows[:, :, :low_rows], middle, own_rows[:, :, low_rows:]], axis=2
    )
    difference = (
        whitened - contrast.astype(jnp.float32)[:, None] * full_projection.astype(jnp.float32)
    ).astype(jnp.bfloat16)
    residual = jnp.stack([invert(difference[n], tables, box_size) for n in range(particles)])
    return (residual, reconstruction)


def solution(mesh):
    in_specs = (
        P(("img", "slab"), None, None),
        P(("img", "slab")),
        P(),
        P(("img", "slab"), None, None),
        P(("img", "slab"), None),
        P(("img", "slab"), None),
        P(("img", "slab"), None),
        P("slab", None, None),
    )
    out_specs = (P(("img", "slab"), None, None), P("slab", "img", None))
    return jax.shard_map(body, mesh=mesh, in_specs=in_specs, out_specs=out_specs, check_vma=False)
```

```python
import math

import jax
import ml_dtypes
import numpy as np
import jax.numpy as jnp
from jax import lax
from jax.sharding import PartitionSpec as P

RB = 16
LOW = 4
WL = 8
HI = lax.Precision.HIGHEST


def table_stack(box_size):
    positions = np.arange(box_size)
    angles = ((positions[:, None] * positions[None, :]) % box_size) * (2.0 * np.pi / box_size)
    both = np.stack([np.cos(angles), np.sin(angles)]).astype(ml_dtypes.bfloat16)
    return jnp.asarray(both)


def transform(image, tables):
    rowwise = jnp.einsum(
        "yx,hmx->hym", image, tables, preferred_element_type=jnp.float32
    ).astype(jnp.bfloat16)
    products = jnp.einsum("gky,hym->ghkm", tables, rowwise, preferred_element_type=jnp.float32)
    real = products[0, 0] - products[1, 1]
    imag = -(products[0, 1] + products[1, 0])
    return jnp.stack([real, imag])


def invert(difference, tables, box_size):
    products = jnp.einsum(
        "hyj,gmj->hgym", difference, tables, preferred_element_type=jnp.float32
    )
    back_real = products[0, 0] - products[1, 1]
    back_imag = products[0, 1] + products[1, 0]
    back_rows = jnp.stack([back_real, -back_imag]).astype(jnp.bfloat16)
    picture = jnp.einsum("hxk,hkm->hxm", tables, back_rows, preferred_element_type=jnp.float32)
    return ((picture[0] + picture[1]) / box_size).astype(jnp.bfloat16)


def radius_sq(row_ids, box_size):
    half_size = box_size // 2
    columns = jnp.arange(box_size, dtype=jnp.int32)
    freq_rows = jnp.where(row_ids < half_size, row_ids, row_ids - box_size)
    freq_cols = jnp.where(columns < half_size, columns, columns - box_size)
    total = freq_rows[..., None] * freq_rows[..., None] + freq_cols * freq_cols
    return total.astype(jnp.float32) / float(half_size * half_size)


def contrast_curve(defocus_of, row_ids, box_size):
    radius = radius_sq(row_ids, box_size)
    return (-jnp.sin(defocus_of[:, None, None] * radius + 0.1)).astype(jnp.bfloat16)


def lookup_defocus(mic_ids, defocus):
    labels = jnp.arange(defocus.shape[0], dtype=jnp.int32)
    return jnp.sum(jnp.where(mic_ids[:, None] == labels[None, :], defocus[None, :], 0.0), axis=1)


def shift_halves(values, steps, box_size):
    rolled = jnp.roll(values, steps, axis=-1)
    column = lax.broadcasted_iota(jnp.int32, values.shape, values.ndim - 1)
    if steps == 1:
        first, second = values[..., box_size - 1 : box_size], values[..., 2 * box_size - 1 :]
        rolled = jnp.where(column == 0, first, rolled)
        return jnp.where(column == box_size, second, rolled)
    first, second = values[..., 0:1], values[..., box_size : box_size + 1]
    rolled = jnp.where(column == box_size - 1, first, rolled)
    return jnp.where(column == 2 * box_size - 1, second, rolled)


def low_row_ids(block_ids, box_size):
    base = block_ids * RB + jnp.where(block_ids < LOW, 0, box_size - 2 * LOW * RB)
    return base[..., None] + jnp.arange(RB, dtype=jnp.int32)


def power_gather(total, device_count, rows, box_size):
    spread = jnp.broadcast_to(total, (device_count, total.shape[1]))
    back = lax.all_to_all(spread, ("img", "slab"), 0, 0, tiled=True)
    half = back.reshape(rows, box_size)
    zero = lax.optimization_barrier(jnp.zeros((), jnp.int32))
    n = lax.broadcasted_iota(jnp.int32, (box_size, box_size), 0) + zero
    m = lax.broadcasted_iota(jnp.int32, (box_size, box_size), 1)
    flip_columns = (n == (box_size - m) % box_size).astype(jnp.float32)
    flipped = jnp.dot(half, flip_columns, precision=HI)
    k = lax.broadcasted_iota(jnp.int32, (box_size, rows), 0) + zero
    j = lax.broadcasted_iota(jnp.int32, (box_size, rows), 1)
    keep = ((j == k) & (k <= box_size // 2)).astype(jnp.float32)
    turn = ((j == box_size - k) & (k > box_size // 2)).astype(jnp.float32)
    return jnp.dot(keep, half, precision=HI) + jnp.dot(turn, flipped, precision=HI)


def shift_exchange(values, count, capacity, direction):
    pieces = [values[:capacity]]
    for d in range(1, count):
        pairs = [(i, (i + direction * d) % count) for i in range(count)]
        pieces.append(lax.ppermute(values[d * capacity : (d + 1) * capacity], "slab", pairs))
    return jnp.concatenate(pieces, axis=0)


def reduce_over_img(numerator, count):
    me = lax.axis_index("img")
    total = lax.dynamic_index_in_dim(numerator, me, 0, keepdims=False).astype(jnp.float32)
    for d in range(1, count):
        piece = lax.dynamic_index_in_dim(numerator, (me + d) % count, 0, keepdims=False)
        pairs = [(i, (i + d) % count) for i in range(count)]
        total = total + lax.ppermute(piece, "img", pairs).astype(jnp.float32)
    return total


def half_rows(box_size, device_count):
    rows = box_size // 2 + 1
    while (rows * box_size) % device_count:
        rows += 1
    return rows


def body(images, micrograph, defocus, target_slab, target_plane, target_rows, shift_index, volume):
    particles, box_size = (images.shape[0], images.shape[1])
    slab_count = lax.axis_size("slab")
    img_count = lax.axis_size("img")
    device_count = img_count * slab_count
    low_rows = LOW * RB
    blocks_per = 2 * LOW
    routed = particles * blocks_per
    planes, vrows = volume.shape[0], volume.shape[1]
    row_blocks = vrows // RB
    slots = planes * row_blocks
    tables = lax.optimization_barrier(table_stack(box_size))

    destination = target_slab.reshape(routed)
    capacity = max(2, (2 * routed + slab_count - 1) // slab_count)
    member = (destination[:, None] == jnp.arange(slab_count, dtype=jnp.int32)[None, :]).astype(
        jnp.int32
    )
    before = jnp.cumsum(member, axis=0) - member
    slot_rank = jnp.sum(member * before, axis=1)
    me = lax.axis_index("slab")
    seat_index = ((destination - me) % slab_count) * capacity + slot_rank
    seat_count = slab_count * capacity
    seat_pick = (seat_index[:, None] == jnp.arange(seat_count, dtype=jnp.int32)[None, :]).astype(
        jnp.bfloat16
    )
    source_block = jnp.tile(jnp.arange(blocks_per, dtype=jnp.int32), particles)
    block_info = jnp.stack(
        [
            jnp.ones((routed,), jnp.int32),
            target_plane.reshape(routed),
            target_rows.reshape(routed),
            shift_index.reshape(routed),
            source_block,
            jnp.repeat(micrograph, blocks_per),
        ],
        axis=1,
    ).astype(jnp.bfloat16)
    info_width = 128
    block_info = jnp.pad(block_info, ((0, 0), (0, info_width - block_info.shape[1])))

    spectrum = jnp.stack([transform(images[n], tables) for n in range(particles)])
    low_spectrum = jnp.concatenate(
        [spectrum[:, :, :low_rows], spectrum[:, :, box_size - low_rows :]], axis=2
    ).astype(jnp.bfloat16)
    low_spectrum = jnp.moveaxis(low_spectrum, 1, 2).reshape(routed, RB * 2 * box_size)
    payload = jnp.concatenate([low_spectrum, block_info], axis=1)
    send = jnp.einsum(
        "rs,rx->sx", seat_pick, payload, preferred_element_type=jnp.float32
    ).astype(jnp.bfloat16)
    rows_half = half_rows(box_size, device_count)
    low_half = spectrum[:, :, :rows_half]
    power_half = jnp.sum(low_half * low_half, axis=(0, 1))
    pieces = power_half.reshape(device_count, rows_half * box_size // device_count)
    gathered = lax.all_to_all(pieces, ("img", "slab"), 0, 0, tiled=True)
    got = shift_exchange(send, slab_count, capacity, 1)
    got_blocks = got[:, : RB * 2 * box_size].reshape(seat_count, RB, 2 * box_size)
    got_info = got[:, RB * 2 * box_size : RB * 2 * box_size + 6].astype(jnp.int32)

    live = got_info[:, 0].astype(jnp.float32)[:, None, None]
    slot_of = got_info[:, 1] * row_blocks + got_info[:, 2]
    slot_pick = (slot_of[:, None] == jnp.arange(slots, dtype=jnp.int32)[None, :]).astype(
        jnp.bfloat16
    )
    blend_weight = ((got_info[:, 3].astype(jnp.float32) + 0.5) / WL)[:, None, None]
    volume_slots = volume.reshape(planes, row_blocks, RB, 2, box_size)
    volume_slots = jnp.transpose(volume_slots, (0, 1, 3, 2, 4)).reshape(slots, 2, RB, box_size)
    nearby = jnp.einsum(
        "sq,qhix->shix", slot_pick, volume_slots, preferred_element_type=jnp.float32
    )
    blend_4 = blend_weight[:, :, :, None]
    projected = (
        ((1.0 - blend_4) * nearby + blend_4 * jnp.roll(nearby, -1, axis=-1)) * live[..., None]
    ).astype(jnp.bfloat16)

    total = jnp.sum(gathered, axis=0, keepdims=True)
    power = power_gather(total, device_count, rows_half, box_size)
    noise_level = jnp.sqrt(power / (particles * device_count) + 1e-06)
    level_both = jnp.concatenate([noise_level, noise_level], axis=1)

    returned_rows = shift_exchange(projected, slab_count, capacity, -1)

    got_rows = low_row_ids(got_info[:, 4], box_size)
    got_contrast = contrast_curve(lookup_defocus(got_info[:, 5], defocus), got_rows, box_size)
    level_low = jnp.concatenate(
        [level_both[:low_rows], level_both[box_size - low_rows :]], axis=0
    ).reshape(blocks_per, RB, 2 * box_size)
    block_pick = (got_info[:, 4:5] == jnp.arange(blocks_per, dtype=jnp.int32)[None, :]).astype(
        jnp.float32
    )
    got_level = jnp.einsum(
        "sj,jix->six", block_pick, level_low, precision=HI, preferred_element_type=jnp.float32
    )
    got_contrast_both = jnp.concatenate([got_contrast, got_contrast], axis=-1).astype(jnp.float32)
    received = got_contrast_both * got_blocks.astype(jnp.float32) / got_level
    inserted = (1.0 - blend_weight) * received + blend_weight * shift_halves(received, 1, box_size)
    contrast_rows = got_contrast.astype(jnp.float32)
    squared = contrast_rows * contrast_rows
    weights = (1.0 - blend_weight) * squared + blend_weight * jnp.roll(squared, 1, axis=-1)
    seat_data = jnp.concatenate([inserted, weights], axis=-1) * live
    numerator = jnp.einsum(
        "sq,srx->qrx", slot_pick.astype(jnp.float32), seat_data, precision=HI,
        preferred_element_type=jnp.float32,
    )
    share = vrows // img_count
    numerator = numerator.reshape(planes, img_count, share, 3 * box_size).astype(jnp.bfloat16)
    numerator = jnp.swapaxes(numerator, 0, 1)
    volume_part = reduce_over_img(numerator, img_count)
    weight_sum = volume_part[..., 2 * box_size :]
    reconstruction = volume_part[..., : 2 * box_size] / (
        jnp.concatenate([weight_sum, weight_sum], axis=-1) + 1.0
    )

    whitened = spectrum / noise_level
    row_all = jnp.arange(box_size, dtype=jnp.int32)[None, :]
    contrast = contrast_curve(lookup_defocus(micrograph, defocus), row_all, box_size)
    own_rows = jnp.einsum(
        "rs,shix->rhix", seat_pick, returned_rows, preferred_element_type=jnp.float32
    ).astype(jnp.bfloat16)
    own_rows = own_rows.reshape(particles, blocks_per, 2, RB, box_size)
    own_rows = jnp.moveaxis(own_rows, 2, 1).reshape(particles, 2, 2 * low_rows, box_size)
    middle = jnp.zeros((particles, 2, box_size - 2 * low_rows, box_size), jnp.bfloat16)
    full_projection = jnp.concatenate(
        [own_rows[:, :, :low_rows], middle, own_rows[:, :, low_rows:]], axis=2
    )
    difference = (
        whitened - contrast.astype(jnp.float32)[:, None] * full_projection.astype(jnp.float32)
    ).astype(jnp.bfloat16)
    residual = jnp.stack([invert(difference[n], tables, box_size) for n in range(particles)])
    return (residual, reconstruction)


def solution(mesh):
    in_specs = (
        P(("img", "slab"), None, None),
        P(("img", "slab")),
        P(),
        P(("img", "slab"), None, None),
        P(("img", "slab"), None),
        P(("img", "slab"), None),
        P(("img", "slab"), None),
        P("slab", None, None),
    )
    out_specs = (P(("img", "slab"), None, None), P("slab", "img", None))
    return jax.shard_map(body, mesh=mesh, in_specs=in_specs, out_specs=out_specs, check_vma=False)
```

```python
import math

import jax
import ml_dtypes
import numpy as np
import jax.numpy as jnp
from jax import lax
from jax.sharding import PartitionSpec as P

RB = 16
LOW = 4
WL = 8
HI = lax.Precision.HIGHEST


def table_stack(box_size):
    positions = np.arange(box_size)
    angles = ((positions[:, None] * positions[None, :]) % box_size) * (2.0 * np.pi / box_size)
    both = np.stack([np.cos(angles), np.sin(angles)]).astype(ml_dtypes.bfloat16)
    return jnp.asarray(both)


def transform(image, tables):
    rowwise = jnp.einsum(
        "yx,hmx->hym", image, tables, preferred_element_type=jnp.float32
    ).astype(jnp.bfloat16)
    products = jnp.einsum("gky,hym->ghkm", tables, rowwise, preferred_element_type=jnp.float32)
    real = products[0, 0] - products[1, 1]
    imag = -(products[0, 1] + products[1, 0])
    return jnp.stack([real, imag])


def invert(difference, tables, box_size):
    products = jnp.einsum(
        "hyj,gmj->hgym", difference, tables, preferred_element_type=jnp.float32
    )
    back_real = products[0, 0] - products[1, 1]
    back_imag = products[0, 1] + products[1, 0]
    back_rows = jnp.stack([back_real, -back_imag]).astype(jnp.bfloat16)
    picture = jnp.einsum("hxk,hkm->hxm", tables, back_rows, preferred_element_type=jnp.float32)
    return ((picture[0] + picture[1]) / box_size).astype(jnp.bfloat16)


def radius_sq(row_ids, box_size):
    half_size = box_size // 2
    columns = jnp.arange(box_size, dtype=jnp.int32)
    freq_rows = jnp.where(row_ids < half_size, row_ids, row_ids - box_size)
    freq_cols = jnp.where(columns < half_size, columns, columns - box_size)
    total = freq_rows[..., None] * freq_rows[..., None] + freq_cols * freq_cols
    return total.astype(jnp.float32) / float(half_size * half_size)


def contrast_curve(defocus_of, row_ids, box_size):
    radius = radius_sq(row_ids, box_size)
    return (-jnp.sin(defocus_of[:, None, None] * radius + 0.1)).astype(jnp.bfloat16)


def lookup_defocus(mic_ids, defocus):
    labels = jnp.arange(defocus.shape[0], dtype=jnp.int32)
    return jnp.sum(jnp.where(mic_ids[:, None] == labels[None, :], defocus[None, :], 0.0), axis=1)


def shift_halves(values, steps, box_size):
    column = lax.broadcasted_iota(jnp.int32, values.shape, values.ndim - 1) % box_size
    seam = 0 if steps == 1 else box_size - 1
    rolled = jnp.roll(values, steps, axis=-1)
    wrapped = jnp.roll(values, -steps * (box_size - 1), axis=-1)
    return jnp.where(column == seam, wrapped, rolled)


def low_row_ids(block_ids, box_size):
    base = block_ids * RB + jnp.where(block_ids < LOW, 0, box_size - 2 * LOW * RB)
    return base[..., None] + jnp.arange(RB, dtype=jnp.int32)


def power_gather(total, device_count, rows, box_size):
    spread = jnp.broadcast_to(total, (device_count, total.shape[1]))
    back = lax.all_to_all(spread, ("img", "slab"), 0, 0, tiled=True)
    half = back.reshape(rows, box_size)
    zero = lax.optimization_barrier(jnp.zeros((), jnp.int32))
    n = lax.broadcasted_iota(jnp.int32, (box_size, box_size), 0) + zero
    m = lax.broadcasted_iota(jnp.int32, (box_size, box_size), 1)
    flip_columns = (n == (box_size - m) % box_size).astype(jnp.float32)
    flipped = jnp.dot(half, flip_columns, precision=HI)
    k = lax.broadcasted_iota(jnp.int32, (box_size, rows), 0) + zero
    j = lax.broadcasted_iota(jnp.int32, (box_size, rows), 1)
    keep = ((j == k) & (k <= box_size // 2)).astype(jnp.float32)
    turn = ((j == box_size - k) & (k > box_size // 2)).astype(jnp.float32)
    return jnp.dot(keep, half, precision=HI) + jnp.dot(turn, flipped, precision=HI)


def shift_exchange(values, count, capacity, direction):
    pieces = [values[:capacity]]
    for d in range(1, count):
        pairs = [(i, (i + direction * d) % count) for i in range(count)]
        pieces.append(lax.ppermute(values[d * capacity : (d + 1) * capacity], "slab", pairs))
    return jnp.concatenate(pieces, axis=0)


def reduce_over_img(numerator, count):
    me = lax.axis_index("img")
    total = lax.dynamic_index_in_dim(numerator, me, 0, keepdims=False).astype(jnp.float32)
    for d in range(1, count):
        piece = lax.dynamic_index_in_dim(numerator, (me + d) % count, 0, keepdims=False)
        pairs = [(i, (i + d) % count) for i in range(count)]
        total = total + lax.ppermute(piece, "img", pairs).astype(jnp.float32)
    return total


def half_rows(box_size, device_count):
    rows = box_size // 2 + 1
    while (rows * box_size) % device_count:
        rows += 1
    return rows


def body(images, micrograph, defocus, target_slab, target_plane, target_rows, shift_index, volume):
    particles, box_size = (images.shape[0], images.shape[1])
    slab_count = lax.axis_size("slab")
    img_count = lax.axis_size("img")
    device_count = img_count * slab_count
    low_rows = LOW * RB
    blocks_per = 2 * LOW
    routed = particles * blocks_per
    planes, vrows = volume.shape[0], volume.shape[1]
    row_blocks = vrows // RB
    slots = planes * row_blocks
    tables = lax.optimization_barrier(table_stack(box_size))

    destination = target_slab.reshape(routed)
    capacity = max(2, (2 * routed + slab_count - 1) // slab_count)
    member = (destination[:, None] == jnp.arange(slab_count, dtype=jnp.int32)[None, :]).astype(
        jnp.int32
    )
    before = jnp.cumsum(member, axis=0) - member
    slot_rank = jnp.sum(member * before, axis=1)
    me = lax.axis_index("slab")
    seat_index = ((destination - me) % slab_count) * capacity + slot_rank
    seat_count = slab_count * capacity
    seat_pick = (seat_index[:, None] == jnp.arange(seat_count, dtype=jnp.int32)[None, :]).astype(
        jnp.bfloat16
    )
    source_block = jnp.tile(jnp.arange(blocks_per, dtype=jnp.int32), particles)
    block_info = jnp.stack(
        [
            jnp.ones((routed,), jnp.int32),
            target_plane.reshape(routed),
            target_rows.reshape(routed),
            shift_index.reshape(routed),
            source_block,
            jnp.repeat(micrograph, blocks_per),
        ],
        axis=1,
    ).astype(jnp.bfloat16)
    info_width = 128
    block_info = jnp.pad(block_info, ((0, 0), (0, info_width - block_info.shape[1])))

    spectrum = jnp.stack([transform(images[n], tables) for n in range(particles)])
    low_spectrum = jnp.concatenate(
        [spectrum[:, :, :low_rows], spectrum[:, :, box_size - low_rows :]], axis=2
    ).astype(jnp.bfloat16)
    low_spectrum = jnp.moveaxis(low_spectrum, 1, 2).reshape(routed, RB * 2 * box_size)
    payload = jnp.concatenate([low_spectrum, block_info], axis=1)
    send = jnp.einsum(
        "rs,rx->sx", seat_pick, payload, preferred_element_type=jnp.float32
    ).astype(jnp.bfloat16)
    rows_half = half_rows(box_size, device_count)
    low_half = spectrum[:, :, :rows_half]
    power_half = jnp.sum(low_half * low_half, axis=(0, 1))
    pieces = power_half.reshape(device_count, rows_half * box_size // device_count)
    gathered = lax.all_to_all(pieces, ("img", "slab"), 0, 0, tiled=True)
    got = shift_exchange(send, slab_count, capacity, 1)
    got_blocks = got[:, : RB * 2 * box_size].reshape(seat_count, RB, 2 * box_size)
    got_info = got[:, RB * 2 * box_size : RB * 2 * box_size + 6].astype(jnp.int32)

    live = got_info[:, 0].astype(jnp.float32)[:, None, None]
    slot_of = got_info[:, 1] * row_blocks + got_info[:, 2]
    slot_pick = (slot_of[:, None] == jnp.arange(slots, dtype=jnp.int32)[None, :]).astype(
        jnp.bfloat16
    )
    blend_weight = ((got_info[:, 3].astype(jnp.float32) + 0.5) / WL)[:, None, None]
    volume_slots = volume.reshape(planes, row_blocks, RB, 2, box_size)
    volume_slots = jnp.transpose(volume_slots, (0, 1, 3, 2, 4)).reshape(slots, 2, RB, box_size)
    nearby = jnp.einsum(
        "sq,qhix->shix", slot_pick, volume_slots, preferred_element_type=jnp.float32
    )
    blend_4 = blend_weight[:, :, :, None]
    projected = (
        ((1.0 - blend_4) * nearby + blend_4 * jnp.roll(nearby, -1, axis=-1)) * live[..., None]
    ).astype(jnp.bfloat16)

    total = jnp.sum(gathered, axis=0, keepdims=True)
    power = power_gather(total, device_count, rows_half, box_size)
    noise_level = jnp.sqrt(power / (particles * device_count) + 1e-06)
    level_both = jnp.concatenate([noise_level, noise_level], axis=1)

    returned_rows = shift_exchange(projected, slab_count, capacity, -1)

    got_rows = low_row_ids(got_info[:, 4], box_size)
    got_contrast = contrast_curve(lookup_defocus(got_info[:, 5], defocus), got_rows, box_size)
    level_low = jnp.concatenate(
        [level_both[:low_rows], level_both[box_size - low_rows :]], axis=0
    ).reshape(blocks_per, RB, 2 * box_size)
    block_pick = (got_info[:, 4:5] == jnp.arange(blocks_per, dtype=jnp.int32)[None, :]).astype(
        jnp.float32
    )
    got_level = jnp.einsum(
        "sj,jix->six", block_pick, level_low, precision=HI, preferred_element_type=jnp.float32
    )
    got_contrast_both = jnp.concatenate([got_contrast, got_contrast], axis=-1).astype(jnp.float32)
    received = got_contrast_both * got_blocks.astype(jnp.float32) / got_level
    inserted = (1.0 - blend_weight) * received + blend_weight * shift_halves(received, 1, box_size)
    contrast_rows = got_contrast.astype(jnp.float32)
    squared = contrast_rows * contrast_rows
    weights = (1.0 - blend_weight) * squared + blend_weight * jnp.roll(squared, 1, axis=-1)
    seat_data = jnp.concatenate([inserted, weights], axis=-1) * live
    numerator = jnp.einsum(
        "sq,srx->qrx", slot_pick.astype(jnp.float32), seat_data, precision=HI,
        preferred_element_type=jnp.float32,
    )
    share = vrows // img_count
    numerator = numerator.reshape(planes, img_count, share, 3 * box_size).astype(jnp.bfloat16)
    numerator = jnp.swapaxes(numerator, 0, 1)
    volume_part = reduce_over_img(numerator, img_count)
    weight_sum = volume_part[..., 2 * box_size :]
    reconstruction = volume_part[..., : 2 * box_size] / (
        jnp.concatenate([weight_sum, weight_sum], axis=-1) + 1.0
    )

    whitened = spectrum / noise_level
    row_all = jnp.arange(box_size, dtype=jnp.int32)[None, :]
    contrast = contrast_curve(lookup_defocus(micrograph, defocus), row_all, box_size)
    own_rows = jnp.einsum(
        "rs,shix->rhix", seat_pick, returned_rows, preferred_element_type=jnp.float32
    ).astype(jnp.bfloat16)
    own_rows = own_rows.reshape(particles, blocks_per, 2, RB, box_size)
    own_rows = jnp.moveaxis(own_rows, 2, 1).reshape(particles, 2, 2 * low_rows, box_size)
    middle = jnp.zeros((particles, 2, box_size - 2 * low_rows, box_size), jnp.bfloat16)
    full_projection = jnp.concatenate(
        [own_rows[:, :, :low_rows], middle, own_rows[:, :, low_rows:]], axis=2
    )
    difference = (
        whitened - contrast.astype(jnp.float32)[:, None] * full_projection.astype(jnp.float32)
    ).astype(jnp.bfloat16)
    residual = jnp.stack([invert(difference[n], tables, box_size) for n in range(particles)])
    return (residual, reconstruction)


def solution(mesh):
    in_specs = (
        P(("img", "slab"), None, None),
        P(("img", "slab")),
        P(),
        P(("img", "slab"), None, None),
        P(("img", "slab"), None),
        P(("img", "slab"), None),
        P(("img", "slab"), None),
        P("slab", None, None),
    )
    out_specs = (P(("img", "slab"), None, None), P("slab", "img", None))
    return jax.shard_map(body, mesh=mesh, in_specs=in_specs, out_specs=out_specs, check_vma=False)
```

```python
import math

import jax
import ml_dtypes
import numpy as np
import jax.numpy as jnp
from jax import lax
from jax.sharding import PartitionSpec as P

RB = 16
LOW = 4
WL = 8
HI = lax.Precision.HIGHEST


def table_stack(box_size):
    positions = np.arange(box_size)
    angles = ((positions[:, None] * positions[None, :]) % box_size) * (2.0 * np.pi / box_size)
    both = np.stack([np.cos(angles), np.sin(angles)]).astype(ml_dtypes.bfloat16)
    return jnp.asarray(both)


def transform(image, tables):
    rowwise = jnp.einsum(
        "yx,hmx->hym", image, tables, preferred_element_type=jnp.float32
    ).astype(jnp.bfloat16)
    products = jnp.einsum("gky,hym->ghkm", tables, rowwise, preferred_element_type=jnp.float32)
    real = products[0, 0] - products[1, 1]
    imag = -(products[0, 1] + products[1, 0])
    return jnp.stack([real, imag])


def invert(difference, tables, box_size):
    products = jnp.einsum(
        "hyj,gmj->hgym", difference, tables, preferred_element_type=jnp.float32
    )
    back_real = products[0, 0] - products[1, 1]
    back_imag = products[0, 1] + products[1, 0]
    back_rows = jnp.stack([back_real, -back_imag]).astype(jnp.bfloat16)
    picture = jnp.einsum("hxk,hkm->hxm", tables, back_rows, preferred_element_type=jnp.float32)
    return ((picture[0] + picture[1]) / box_size).astype(jnp.bfloat16)


def radius_sq(row_ids, box_size):
    half_size = box_size // 2
    columns = jnp.arange(box_size, dtype=jnp.int32)
    freq_rows = jnp.where(row_ids < half_size, row_ids, row_ids - box_size)
    freq_cols = jnp.where(columns < half_size, columns, columns - box_size)
    total = freq_rows[..., None] * freq_rows[..., None] + freq_cols * freq_cols
    return total.astype(jnp.float32) / float(half_size * half_size)


def contrast_curve(defocus_of, row_ids, box_size):
    radius = radius_sq(row_ids, box_size)
    return (-jnp.sin(defocus_of[:, None, None] * radius + 0.1)).astype(jnp.bfloat16)


def lookup_defocus(mic_ids, defocus):
    labels = jnp.arange(defocus.shape[0], dtype=jnp.int32)
    return jnp.sum(jnp.where(mic_ids[:, None] == labels[None, :], defocus[None, :], 0.0), axis=1)


def shift_halves(values, steps, box_size):
    column = lax.broadcasted_iota(jnp.int32, values.shape, values.ndim - 1) % box_size
    seam = 0 if steps == 1 else box_size - 1
    rolled = jnp.roll(values, steps, axis=-1)
    wrapped = jnp.roll(values, -steps * (box_size - 1), axis=-1)
    return jnp.where(column == seam, wrapped, rolled)


def low_row_ids(block_ids, box_size):
    base = block_ids * RB + jnp.where(block_ids < LOW, 0, box_size - 2 * LOW * RB)
    return base[..., None] + jnp.arange(RB, dtype=jnp.int32)


def power_gather(total, device_count, rows, box_size):
    spread = jnp.broadcast_to(total, (device_count, total.shape[1]))
    back = lax.all_to_all(spread, ("img", "slab"), 0, 0, tiled=True)
    half = back.reshape(rows, box_size)
    zero = lax.optimization_barrier(jnp.zeros((), jnp.int32))
    n = lax.broadcasted_iota(jnp.int32, (box_size, box_size), 0) + zero
    m = lax.broadcasted_iota(jnp.int32, (box_size, box_size), 1)
    flip_columns = (n == (box_size - m) % box_size).astype(jnp.float32)
    flipped = jnp.dot(half, flip_columns, precision=HI)
    k = lax.broadcasted_iota(jnp.int32, (box_size, rows), 0) + zero
    j = lax.broadcasted_iota(jnp.int32, (box_size, rows), 1)
    keep = ((j == k) & (k <= box_size // 2)).astype(jnp.float32)
    turn = ((j == box_size - k) & (k > box_size // 2)).astype(jnp.float32)
    return jnp.dot(keep, half, precision=HI) + jnp.dot(turn, flipped, precision=HI)


def shift_exchange(values, count, capacity, direction):
    pieces = [values[:capacity]]
    for d in range(1, count):
        pairs = [(i, (i + direction * d) % count) for i in range(count)]
        pieces.append(lax.ppermute(values[d * capacity : (d + 1) * capacity], "slab", pairs))
    return jnp.concatenate(pieces, axis=0)


def reduce_over_img(numerator, count):
    me = lax.axis_index("img")
    total = lax.dynamic_index_in_dim(numerator, me, 0, keepdims=False).astype(jnp.float32)
    for d in range(1, count):
        piece = lax.dynamic_index_in_dim(numerator, (me + d) % count, 0, keepdims=False)
        pairs = [(i, (i + d) % count) for i in range(count)]
        total = total + lax.ppermute(piece, "img", pairs).astype(jnp.float32)
    return total


def half_rows(box_size, device_count):
    rows = box_size // 2 + 1
    while (rows * box_size) % device_count:
        rows += 1
    return rows


def body(images, micrograph, defocus, target_slab, target_plane, target_rows, shift_index, volume):
    particles, box_size = (images.shape[0], images.shape[1])
    slab_count = lax.axis_size("slab")
    img_count = lax.axis_size("img")
    device_count = img_count * slab_count
    low_rows = LOW * RB
    blocks_per = 2 * LOW
    routed = particles * blocks_per
    planes, vrows = volume.shape[0], volume.shape[1]
    row_blocks = vrows // RB
    slots = planes * row_blocks
    tables = lax.optimization_barrier(table_stack(box_size))

    destination = target_slab.reshape(routed)
    capacity = max(2, (2 * routed + slab_count - 1) // slab_count)
    member = (destination[:, None] == jnp.arange(slab_count, dtype=jnp.int32)[None, :]).astype(
        jnp.int32
    )
    before = jnp.cumsum(member, axis=0) - member
    slot_rank = jnp.sum(member * before, axis=1)
    me = lax.axis_index("slab")
    seat_index = destination * capacity + slot_rank
    seat_count = slab_count * capacity
    seat_pick = (seat_index[:, None] == jnp.arange(seat_count, dtype=jnp.int32)[None, :]).astype(
        jnp.bfloat16
    )
    source_block = jnp.tile(jnp.arange(blocks_per, dtype=jnp.int32), particles)
    block_info = jnp.stack(
        [
            jnp.ones((routed,), jnp.int32),
            target_plane.reshape(routed),
            target_rows.reshape(routed),
            shift_index.reshape(routed),
            source_block,
            jnp.repeat(micrograph, blocks_per),
        ],
        axis=1,
    ).astype(jnp.bfloat16)
    info_width = 128
    block_info = jnp.pad(block_info, ((0, 0), (0, info_width - block_info.shape[1])))

    spectrum = jnp.stack([transform(images[n], tables) for n in range(particles)])
    low_spectrum = jnp.concatenate(
        [spectrum[:, :, :low_rows], spectrum[:, :, box_size - low_rows :]], axis=2
    ).astype(jnp.bfloat16)
    low_spectrum = jnp.moveaxis(low_spectrum, 1, 2).reshape(routed, RB * 2 * box_size)
    payload = jnp.concatenate([low_spectrum, block_info], axis=1)
    send = jnp.einsum(
        "rs,rx->sx", seat_pick, payload, preferred_element_type=jnp.float32
    ).astype(jnp.bfloat16)
    rows_half = half_rows(box_size, device_count)
    low_half = spectrum[:, :, :rows_half]
    power_half = jnp.sum(low_half * low_half, axis=(0, 1))
    pieces = power_half.reshape(device_count, rows_half * box_size // device_count)
    gathered = lax.all_to_all(pieces, ("img", "slab"), 0, 0, tiled=True)
    got = lax.all_to_all(send, "slab", 0, 0, tiled=True)
    got_blocks = got[:, : RB * 2 * box_size].reshape(seat_count, RB, 2 * box_size)
    got_info = got[:, RB * 2 * box_size : RB * 2 * box_size + 6].astype(jnp.int32)

    live = got_info[:, 0].astype(jnp.float32)[:, None, None]
    slot_of = got_info[:, 1] * row_blocks + got_info[:, 2]
    slot_pick = (slot_of[:, None] == jnp.arange(slots, dtype=jnp.int32)[None, :]).astype(
        jnp.bfloat16
    )
    blend_weight = ((got_info[:, 3].astype(jnp.float32) + 0.5) / WL)[:, None, None]
    volume_slots = volume.reshape(planes, row_blocks, RB, 2, box_size)
    volume_slots = jnp.transpose(volume_slots, (0, 1, 3, 2, 4)).reshape(slots, 2, RB, box_size)
    nearby = jnp.einsum(
        "sq,qhix->shix", slot_pick, volume_slots, preferred_element_type=jnp.float32
    )
    blend_4 = blend_weight[:, :, :, None]
    projected = (
        ((1.0 - blend_4) * nearby + blend_4 * jnp.roll(nearby, -1, axis=-1)) * live[..., None]
    ).astype(jnp.bfloat16)

    total = jnp.sum(gathered, axis=0, keepdims=True)
    power = power_gather(total, device_count, rows_half, box_size)
    noise_level = jnp.sqrt(power / (particles * device_count) + 1e-06)
    level_both = jnp.concatenate([noise_level, noise_level], axis=1)

    returned_rows = lax.all_to_all(projected, "slab", 0, 0, tiled=True)

    got_rows = low_row_ids(got_info[:, 4], box_size)
    got_contrast = contrast_curve(lookup_defocus(got_info[:, 5], defocus), got_rows, box_size)
    level_low = jnp.concatenate(
        [level_both[:low_rows], level_both[box_size - low_rows :]], axis=0
    ).reshape(blocks_per, RB, 2 * box_size)
    block_pick = (got_info[:, 4:5] == jnp.arange(blocks_per, dtype=jnp.int32)[None, :]).astype(
        jnp.float32
    )
    got_level = jnp.einsum(
        "sj,jix->six", block_pick, level_low, precision=HI, preferred_element_type=jnp.float32
    )
    got_contrast_both = jnp.concatenate([got_contrast, got_contrast], axis=-1).astype(jnp.float32)
    received = got_contrast_both * got_blocks.astype(jnp.float32) / got_level
    inserted = (1.0 - blend_weight) * received + blend_weight * shift_halves(received, 1, box_size)
    contrast_rows = got_contrast.astype(jnp.float32)
    squared = contrast_rows * contrast_rows
    weights = (1.0 - blend_weight) * squared + blend_weight * jnp.roll(squared, 1, axis=-1)
    seat_data = jnp.concatenate([inserted, weights], axis=-1) * live
    numerator = jnp.einsum(
        "sq,srx->qrx", slot_pick.astype(jnp.float32), seat_data, precision=HI,
        preferred_element_type=jnp.float32,
    )
    share = vrows // img_count
    numerator = numerator.reshape(planes, img_count, share, 3 * box_size).astype(jnp.bfloat16)
    numerator = jnp.swapaxes(numerator, 0, 1)
    volume_part = reduce_over_img(numerator, img_count)
    weight_sum = volume_part[..., 2 * box_size :]
    reconstruction = volume_part[..., : 2 * box_size] / (
        jnp.concatenate([weight_sum, weight_sum], axis=-1) + 1.0
    )

    whitened = spectrum / noise_level
    row_all = jnp.arange(box_size, dtype=jnp.int32)[None, :]
    contrast = contrast_curve(lookup_defocus(micrograph, defocus), row_all, box_size)
    own_rows = jnp.einsum(
        "rs,shix->rhix", seat_pick, returned_rows, preferred_element_type=jnp.float32
    ).astype(jnp.bfloat16)
    own_rows = own_rows.reshape(particles, blocks_per, 2, RB, box_size)
    own_rows = jnp.moveaxis(own_rows, 2, 1).reshape(particles, 2, 2 * low_rows, box_size)
    middle = jnp.zeros((particles, 2, box_size - 2 * low_rows, box_size), jnp.bfloat16)
    full_projection = jnp.concatenate(
        [own_rows[:, :, :low_rows], middle, own_rows[:, :, low_rows:]], axis=2
    )
    difference = (
        whitened - contrast.astype(jnp.float32)[:, None] * full_projection.astype(jnp.float32)
    ).astype(jnp.bfloat16)
    residual = jnp.stack([invert(difference[n], tables, box_size) for n in range(particles)])
    return (residual, reconstruction)


def solution(mesh):
    in_specs = (
        P(("img", "slab"), None, None),
        P(("img", "slab")),
        P(),
        P(("img", "slab"), None, None),
        P(("img", "slab"), None),
        P(("img", "slab"), None),
        P(("img", "slab"), None),
        P("slab", None, None),
    )
    out_specs = (P(("img", "slab"), None, None), P("slab", "img", None))
    return jax.shard_map(body, mesh=mesh, in_specs=in_specs, out_specs=out_specs, check_vma=False)
```

```python
import math

import jax
import ml_dtypes
import numpy as np
import jax.numpy as jnp
from jax import lax
from jax.sharding import PartitionSpec as P

RB = 16
LOW = 4
WL = 8
HI = lax.Precision.HIGHEST


def table_stack(box_size):
    positions = np.arange(box_size)
    angles = ((positions[:, None] * positions[None, :]) % box_size) * (2.0 * np.pi / box_size)
    both = np.stack([np.cos(angles), np.sin(angles)]).astype(ml_dtypes.bfloat16)
    return jnp.asarray(both)


def transform(image, tables):
    rowwise = jnp.einsum(
        "yx,hmx->hym", image, tables, preferred_element_type=jnp.float32
    ).astype(jnp.bfloat16)
    products = jnp.einsum("gky,hym->ghkm", tables, rowwise, preferred_element_type=jnp.float32)
    real = products[0, 0] - products[1, 1]
    imag = -(products[0, 1] + products[1, 0])
    return jnp.stack([real, imag])


def invert(difference, tables, box_size):
    products = jnp.einsum(
        "hyj,gmj->hgym", difference, tables, preferred_element_type=jnp.float32
    )
    back_real = products[0, 0] - products[1, 1]
    back_imag = products[0, 1] + products[1, 0]
    back_rows = jnp.stack([back_real, -back_imag]).astype(jnp.bfloat16)
    picture = jnp.einsum("hxk,hkm->hxm", tables, back_rows, preferred_element_type=jnp.float32)
    return ((picture[0] + picture[1]) / box_size).astype(jnp.bfloat16)


def radius_sq(row_ids, box_size):
    half_size = box_size // 2
    columns = jnp.arange(box_size, dtype=jnp.int32)
    freq_rows = jnp.where(row_ids < half_size, row_ids, row_ids - box_size)
    freq_cols = jnp.where(columns < half_size, columns, columns - box_size)
    total = freq_rows[..., None] * freq_rows[..., None] + freq_cols * freq_cols
    return total.astype(jnp.float32) / float(half_size * half_size)


def contrast_curve(defocus_of, row_ids, box_size):
    radius = radius_sq(row_ids, box_size)
    return (-jnp.sin(defocus_of[:, None, None] * radius + 0.1)).astype(jnp.bfloat16)


def lookup_defocus(mic_ids, defocus):
    labels = jnp.arange(defocus.shape[0], dtype=jnp.int32)
    return jnp.sum(jnp.where(mic_ids[:, None] == labels[None, :], defocus[None, :], 0.0), axis=1)


def shift_halves(values, steps, box_size):
    column = lax.broadcasted_iota(jnp.int32, values.shape, values.ndim - 1) % box_size
    seam = 0 if steps == 1 else box_size - 1
    rolled = jnp.roll(values, steps, axis=-1)
    wrapped = jnp.roll(values, -steps * (box_size - 1), axis=-1)
    return jnp.where(column == seam, wrapped, rolled)


def low_row_ids(block_ids, box_size):
    base = block_ids * RB + jnp.where(block_ids < LOW, 0, box_size - 2 * LOW * RB)
    return base[..., None] + jnp.arange(RB, dtype=jnp.int32)


def power_gather(total, device_count, rows, box_size):
    spread = jnp.broadcast_to(total, (device_count, total.shape[1]))
    back = lax.all_to_all(spread, ("img", "slab"), 0, 0, tiled=True)
    half = back.reshape(rows, box_size)
    zero = lax.optimization_barrier(jnp.zeros((), jnp.int32))
    n = lax.broadcasted_iota(jnp.int32, (box_size, box_size), 0) + zero
    m = lax.broadcasted_iota(jnp.int32, (box_size, box_size), 1)
    flip_columns = (n == (box_size - m) % box_size).astype(jnp.float32)
    flipped = jnp.dot(half, flip_columns, precision=HI)
    k = lax.broadcasted_iota(jnp.int32, (box_size, rows), 0) + zero
    j = lax.broadcasted_iota(jnp.int32, (box_size, rows), 1)
    keep = ((j == k) & (k <= box_size // 2)).astype(jnp.float32)
    turn = ((j == box_size - k) & (k > box_size // 2)).astype(jnp.float32)
    return jnp.dot(keep, half, precision=HI) + jnp.dot(turn, flipped, precision=HI)


def shift_exchange(values, count, capacity, direction):
    pieces = [values[:capacity]]
    for d in range(1, count):
        pairs = [(i, (i + direction * d) % count) for i in range(count)]
        pieces.append(lax.ppermute(values[d * capacity : (d + 1) * capacity], "slab", pairs))
    return jnp.concatenate(pieces, axis=0)


def reduce_over_img(numerator, count):
    me = lax.axis_index("img")
    total = lax.dynamic_index_in_dim(numerator, me, 0, keepdims=False).astype(jnp.float32)
    for d in range(1, count):
        piece = lax.dynamic_index_in_dim(numerator, (me + d) % count, 0, keepdims=False)
        pairs = [(i, (i + d) % count) for i in range(count)]
        total = total + lax.ppermute(piece, "img", pairs).astype(jnp.float32)
    return total


def half_rows(box_size, device_count):
    rows = box_size // 2 + 1
    while (rows * box_size) % device_count:
        rows += 1
    return rows


def body(images, micrograph, defocus, target_slab, target_plane, target_rows, shift_index, volume):
    particles, box_size = (images.shape[0], images.shape[1])
    slab_count = lax.axis_size("slab")
    img_count = lax.axis_size("img")
    device_count = img_count * slab_count
    low_rows = LOW * RB
    blocks_per = 2 * LOW
    routed = particles * blocks_per
    planes, vrows = volume.shape[0], volume.shape[1]
    row_blocks = vrows // RB
    slots = planes * row_blocks
    tables = lax.optimization_barrier(table_stack(box_size))

    destination = target_slab.reshape(routed)
    capacity = max(2, (2 * routed + slab_count - 1) // slab_count)
    member = (destination[:, None] == jnp.arange(slab_count, dtype=jnp.int32)[None, :]).astype(
        jnp.int32
    )
    before = jnp.cumsum(member, axis=0) - member
    slot_rank = jnp.sum(member * before, axis=1)
    me = lax.axis_index("slab")
    seat_index = destination * capacity + slot_rank
    seat_count = slab_count * capacity
    seat_pick = (seat_index[:, None] == jnp.arange(seat_count, dtype=jnp.int32)[None, :]).astype(
        jnp.bfloat16
    )
    source_block = jnp.tile(jnp.arange(blocks_per, dtype=jnp.int32), particles)
    block_info = jnp.stack(
        [
            jnp.ones((routed,), jnp.int32),
            target_plane.reshape(routed),
            target_rows.reshape(routed),
            shift_index.reshape(routed),
            source_block,
            jnp.repeat(micrograph, blocks_per),
        ],
        axis=1,
    ).astype(jnp.bfloat16)
    info_width = 128
    block_info = jnp.pad(block_info, ((0, 0), (0, info_width - block_info.shape[1])))

    spectrum = jnp.stack([transform(images[n], tables) for n in range(particles)])
    low_spectrum = jnp.concatenate(
        [spectrum[:, :, :low_rows], spectrum[:, :, box_size - low_rows :]], axis=2
    ).astype(jnp.bfloat16)
    low_spectrum = jnp.moveaxis(low_spectrum, 1, 2).reshape(routed, RB * 2 * box_size)
    payload = jnp.concatenate([low_spectrum, block_info], axis=1)
    send = jnp.einsum(
        "rs,rx->sx", seat_pick, payload, preferred_element_type=jnp.float32
    ).astype(jnp.bfloat16)
    rows_half = half_rows(box_size, device_count)
    low_half = spectrum[:, :, :rows_half]
    power_half = jnp.sum(low_half * low_half, axis=(0, 1))
    pieces = power_half.reshape(device_count, rows_half * box_size // device_count)
    gathered = lax.all_to_all(pieces, ("img", "slab"), 0, 0, tiled=True)
    got = lax.all_to_all(send, "slab", 0, 0, tiled=True)
    got_blocks = got[:, : RB * 2 * box_size].reshape(seat_count, RB, 2 * box_size)
    got_info = got[:, RB * 2 * box_size : RB * 2 * box_size + 6].astype(jnp.int32)

    live = got_info[:, 0].astype(jnp.float32)[:, None, None]
    slot_of = got_info[:, 1] * row_blocks + got_info[:, 2]
    slot_pick = (slot_of[:, None] == jnp.arange(slots, dtype=jnp.int32)[None, :]).astype(
        jnp.bfloat16
    )
    blend_weight = ((got_info[:, 3].astype(jnp.float32) + 0.5) / WL)[:, None, None]
    volume_slots = volume.reshape(planes, row_blocks, RB, 2, box_size)
    volume_slots = jnp.transpose(volume_slots, (0, 1, 3, 2, 4)).reshape(slots, 2, RB, box_size)
    nearby = jnp.einsum(
        "sq,qhix->shix", slot_pick, volume_slots, preferred_element_type=jnp.float32
    )
    blend_4 = blend_weight[:, :, :, None]
    projected = (
        ((1.0 - blend_4) * nearby + blend_4 * jnp.roll(nearby, -1, axis=-1)) * live[..., None]
    ).astype(jnp.bfloat16)

    total = jnp.sum(gathered, axis=0, keepdims=True)
    power = power_gather(total, device_count, rows_half, box_size)
    noise_level = jnp.sqrt(power / (particles * device_count) + 1e-06)
    level_both = jnp.concatenate([noise_level, noise_level], axis=1)

    groups = projected.reshape((slab_count, capacity) + projected.shape[1:])
    steps = jnp.arange(slab_count, dtype=jnp.int32)
    by_shift = jnp.take(groups, (me - steps) % slab_count, axis=0).reshape(projected.shape)
    came_back = shift_exchange(by_shift, slab_count, capacity, -1)
    came_back = came_back.reshape((slab_count, capacity) + projected.shape[1:])
    returned_rows = jnp.take(came_back, (steps - me) % slab_count, axis=0).reshape(projected.shape)

    got_rows = low_row_ids(got_info[:, 4], box_size)
    got_contrast = contrast_curve(lookup_defocus(got_info[:, 5], defocus), got_rows, box_size)
    level_low = jnp.concatenate(
        [level_both[:low_rows], level_both[box_size - low_rows :]], axis=0
    ).reshape(blocks_per, RB, 2 * box_size)
    block_pick = (got_info[:, 4:5] == jnp.arange(blocks_per, dtype=jnp.int32)[None, :]).astype(
        jnp.float32
    )
    got_level = jnp.einsum(
        "sj,jix->six", block_pick, level_low, precision=HI, preferred_element_type=jnp.float32
    )
    got_contrast_both = jnp.concatenate([got_contrast, got_contrast], axis=-1).astype(jnp.float32)
    received = got_contrast_both * got_blocks.astype(jnp.float32) / got_level
    inserted = (1.0 - blend_weight) * received + blend_weight * shift_halves(received, 1, box_size)
    contrast_rows = got_contrast.astype(jnp.float32)
    squared = contrast_rows * contrast_rows
    weights = (1.0 - blend_weight) * squared + blend_weight * jnp.roll(squared, 1, axis=-1)
    seat_data = jnp.concatenate([inserted, weights], axis=-1) * live
    numerator = jnp.einsum(
        "sq,srx->qrx", slot_pick.astype(jnp.float32), seat_data, precision=HI,
        preferred_element_type=jnp.float32,
    )
    share = vrows // img_count
    numerator = numerator.reshape(planes, img_count, share, 3 * box_size).astype(jnp.bfloat16)
    numerator = jnp.swapaxes(numerator, 0, 1)
    volume_part = reduce_over_img(numerator, img_count)
    weight_sum = volume_part[..., 2 * box_size :]
    reconstruction = volume_part[..., : 2 * box_size] / (
        jnp.concatenate([weight_sum, weight_sum], axis=-1) + 1.0
    )

    whitened = spectrum / noise_level
    row_all = jnp.arange(box_size, dtype=jnp.int32)[None, :]
    contrast = contrast_curve(lookup_defocus(micrograph, defocus), row_all, box_size)
    own_rows = jnp.einsum(
        "rs,shix->rhix", seat_pick, returned_rows, preferred_element_type=jnp.float32
    ).astype(jnp.bfloat16)
    own_rows = own_rows.reshape(particles, blocks_per, 2, RB, box_size)
    own_rows = jnp.moveaxis(own_rows, 2, 1).reshape(particles, 2, 2 * low_rows, box_size)
    middle = jnp.zeros((particles, 2, box_size - 2 * low_rows, box_size), jnp.bfloat16)
    full_projection = jnp.concatenate(
        [own_rows[:, :, :low_rows], middle, own_rows[:, :, low_rows:]], axis=2
    )
    difference = (
        whitened - contrast.astype(jnp.float32)[:, None] * full_projection.astype(jnp.float32)
    ).astype(jnp.bfloat16)
    residual = jnp.stack([invert(difference[n], tables, box_size) for n in range(particles)])
    return (residual, reconstruction)


def solution(mesh):
    in_specs = (
        P(("img", "slab"), None, None),
        P(("img", "slab")),
        P(),
        P(("img", "slab"), None, None),
        P(("img", "slab"), None),
        P(("img", "slab"), None),
        P(("img", "slab"), None),
        P("slab", None, None),
    )
    out_specs = (P(("img", "slab"), None, None), P("slab", "img", None))
    return jax.shard_map(body, mesh=mesh, in_specs=in_specs, out_specs=out_specs, check_vma=False)
```

```python
import math

import jax
import ml_dtypes
import numpy as np
import jax.numpy as jnp
from jax import lax
from jax.sharding import PartitionSpec as P

RB = 16
LOW = 4
WL = 8
HI = lax.Precision.HIGHEST


def table_stack(box_size):
    positions = np.arange(box_size)
    angles = ((positions[:, None] * positions[None, :]) % box_size) * (2.0 * np.pi / box_size)
    both = np.stack([np.cos(angles), np.sin(angles)]).astype(ml_dtypes.bfloat16)
    return jnp.asarray(both)


def transform(image, tables):
    rowwise = jnp.einsum(
        "yx,hmx->hym", image, tables, preferred_element_type=jnp.float32
    ).astype(jnp.bfloat16)
    products = jnp.einsum("gky,hym->ghkm", tables, rowwise, preferred_element_type=jnp.float32)
    real = products[0, 0] - products[1, 1]
    imag = -(products[0, 1] + products[1, 0])
    return jnp.stack([real, imag])


def back_rows_of(difference, tables):
    products = jnp.einsum(
        "hyj,gmj->hgym", difference, tables, preferred_element_type=jnp.float32
    )
    back_real = products[0, 0] - products[1, 1]
    back_imag = products[0, 1] + products[1, 0]
    return jnp.stack([back_real, -back_imag]).astype(jnp.bfloat16)


def picture_of(back_rows, tables):
    picture = jnp.einsum("hxk,hkm->hxm", tables, back_rows, preferred_element_type=jnp.float32)
    return picture[0] + picture[1]


def radius_sq(row_ids, box_size):
    half_size = box_size // 2
    columns = jnp.arange(box_size, dtype=jnp.int32)
    freq_rows = jnp.where(row_ids < half_size, row_ids, row_ids - box_size)
    freq_cols = jnp.where(columns < half_size, columns, columns - box_size)
    total = freq_rows[..., None] * freq_rows[..., None] + freq_cols * freq_cols
    return total.astype(jnp.float32) / float(half_size * half_size)


def contrast_curve(defocus_of, row_ids, box_size):
    radius = radius_sq(row_ids, box_size)
    return (-jnp.sin(defocus_of[:, None, None] * radius + 0.1)).astype(jnp.bfloat16)


def lookup_defocus(mic_ids, defocus):
    labels = jnp.arange(defocus.shape[0], dtype=jnp.int32)
    return jnp.sum(jnp.where(mic_ids[:, None] == labels[None, :], defocus[None, :], 0.0), axis=1)


def shift_halves(values, steps, box_size):
    column = lax.broadcasted_iota(jnp.int32, values.shape, values.ndim - 1) % box_size
    seam = 0 if steps == 1 else box_size - 1
    rolled = jnp.roll(values, steps, axis=-1)
    wrapped = jnp.roll(values, -steps * (box_size - 1), axis=-1)
    return jnp.where(column == seam, wrapped, rolled)


def low_row_ids(block_ids, box_size):
    base = block_ids * RB + jnp.where(block_ids < LOW, 0, box_size - 2 * LOW * RB)
    return base[..., None] + jnp.arange(RB, dtype=jnp.int32)


def power_gather(total, device_count, rows, box_size):
    spread = jnp.broadcast_to(total, (device_count, total.shape[1]))
    back = lax.all_to_all(spread, ("img", "slab"), 0, 0, tiled=True)
    half = back.reshape(rows, box_size)
    zero = lax.optimization_barrier(jnp.zeros((), jnp.int32))
    n = lax.broadcasted_iota(jnp.int32, (box_size, box_size), 0) + zero
    m = lax.broadcasted_iota(jnp.int32, (box_size, box_size), 1)
    flip_columns = (n == (box_size - m) % box_size).astype(jnp.float32)
    flipped = jnp.dot(half, flip_columns, precision=HI)
    k = lax.broadcasted_iota(jnp.int32, (box_size, rows), 0) + zero
    j = lax.broadcasted_iota(jnp.int32, (box_size, rows), 1)
    keep = ((j == k) & (k <= box_size // 2)).astype(jnp.float32)
    turn = ((j == box_size - k) & (k > box_size // 2)).astype(jnp.float32)
    return jnp.dot(keep, half, precision=HI) + jnp.dot(turn, flipped, precision=HI)


def shift_exchange(values, count, capacity, direction):
    pieces = [values[:capacity]]
    for d in range(1, count):
        pairs = [(i, (i + direction * d) % count) for i in range(count)]
        pieces.append(lax.ppermute(values[d * capacity : (d + 1) * capacity], "slab", pairs))
    return jnp.concatenate(pieces, axis=0)


def reduce_over_img(numerator, count):
    me = lax.axis_index("img")
    total = lax.dynamic_index_in_dim(numerator, me, 0, keepdims=False).astype(jnp.float32)
    for d in range(1, count):
        piece = lax.dynamic_index_in_dim(numerator, (me + d) % count, 0, keepdims=False)
        pairs = [(i, (i + d) % count) for i in range(count)]
        total = total + lax.ppermute(piece, "img", pairs).astype(jnp.float32)
    return total


def half_rows(box_size, device_count):
    rows = box_size // 2 + 1
    while (rows * box_size) % device_count:
        rows += 1
    return rows


def body(images, micrograph, defocus, target_slab, target_plane, target_rows, shift_index, volume):
    particles, box_size = (images.shape[0], images.shape[1])
    slab_count = lax.axis_size("slab")
    img_count = lax.axis_size("img")
    device_count = img_count * slab_count
    low_rows = LOW * RB
    blocks_per = 2 * LOW
    routed = particles * blocks_per
    planes, vrows = volume.shape[0], volume.shape[1]
    row_blocks = vrows // RB
    slots = planes * row_blocks
    tables = lax.optimization_barrier(table_stack(box_size))

    destination = target_slab.reshape(routed)
    capacity = max(2, (2 * routed + slab_count - 1) // slab_count)
    member = (destination[:, None] == jnp.arange(slab_count, dtype=jnp.int32)[None, :]).astype(
        jnp.int32
    )
    before = jnp.cumsum(member, axis=0) - member
    slot_rank = jnp.sum(member * before, axis=1)
    me = lax.axis_index("slab")
    seat_index = destination * capacity + slot_rank
    seat_count = slab_count * capacity
    seat_pick = (seat_index[:, None] == jnp.arange(seat_count, dtype=jnp.int32)[None, :]).astype(
        jnp.bfloat16
    )
    source_block = jnp.tile(jnp.arange(blocks_per, dtype=jnp.int32), particles)
    block_info = jnp.stack(
        [
            jnp.ones((routed,), jnp.int32),
            target_plane.reshape(routed),
            target_rows.reshape(routed),
            shift_index.reshape(routed),
            source_block,
            jnp.repeat(micrograph, blocks_per),
        ],
        axis=1,
    ).astype(jnp.bfloat16)
    info_width = 128
    block_info = jnp.pad(block_info, ((0, 0), (0, info_width - block_info.shape[1])))

    spectrum = jnp.stack([transform(images[n], tables) for n in range(particles)])
    low_spectrum = jnp.concatenate(
        [spectrum[:, :, :low_rows], spectrum[:, :, box_size - low_rows :]], axis=2
    ).astype(jnp.bfloat16)
    low_spectrum = jnp.moveaxis(low_spectrum, 1, 2).reshape(routed, RB * 2 * box_size)
    payload = jnp.concatenate([low_spectrum, block_info], axis=1)
    send = jnp.einsum(
        "rs,rx->sx", seat_pick, payload, preferred_element_type=jnp.float32
    ).astype(jnp.bfloat16)
    rows_half = half_rows(box_size, device_count)
    low_half = spectrum[:, :, :rows_half]
    power_half = jnp.sum(low_half * low_half, axis=(0, 1))
    pieces = power_half.reshape(device_count, rows_half * box_size // device_count)
    gathered = lax.all_to_all(pieces, ("img", "slab"), 0, 0, tiled=True)
    got = lax.all_to_all(send, "slab", 0, 0, tiled=True)
    got_blocks = got[:, : RB * 2 * box_size].reshape(seat_count, RB, 2 * box_size)
    got_info = got[:, RB * 2 * box_size : RB * 2 * box_size + 6].astype(jnp.int32)

    live = got_info[:, 0].astype(jnp.float32)[:, None, None]
    slot_of = got_info[:, 1] * row_blocks + got_info[:, 2]
    slot_pick = (slot_of[:, None] == jnp.arange(slots, dtype=jnp.int32)[None, :]).astype(
        jnp.bfloat16
    )
    blend_weight = ((got_info[:, 3].astype(jnp.float32) + 0.5) / WL)[:, None, None]
    volume_slots = volume.reshape(planes, row_blocks, RB, 2, box_size)
    volume_slots = jnp.transpose(volume_slots, (0, 1, 3, 2, 4)).reshape(slots, 2, RB, box_size)
    nearby = jnp.einsum(
        "sq,qhix->shix", slot_pick, volume_slots, preferred_element_type=jnp.float32
    )
    blend_4 = blend_weight[:, :, :, None]
    projected = (
        ((1.0 - blend_4) * nearby + blend_4 * jnp.roll(nearby, -1, axis=-1)) * live[..., None]
    ).astype(jnp.bfloat16)

    total = jnp.sum(gathered, axis=0, keepdims=True)
    power = power_gather(total, device_count, rows_half, box_size)
    noise_level = jnp.sqrt(power / (particles * device_count) + 1e-06)
    level_both = jnp.concatenate([noise_level, noise_level], axis=1)

    returned_rows = lax.all_to_all(projected, "slab", 0, 0, tiled=True)

    got_rows = low_row_ids(got_info[:, 4], box_size)
    got_contrast = contrast_curve(lookup_defocus(got_info[:, 5], defocus), got_rows, box_size)
    level_low = jnp.concatenate(
        [level_both[:low_rows], level_both[box_size - low_rows :]], axis=0
    ).reshape(blocks_per, RB, 2 * box_size)
    block_pick = (got_info[:, 4:5] == jnp.arange(blocks_per, dtype=jnp.int32)[None, :]).astype(
        jnp.float32
    )
    got_level = jnp.einsum(
        "sj,jix->six", block_pick, level_low, precision=HI, preferred_element_type=jnp.float32
    )
    got_contrast_both = jnp.concatenate([got_contrast, got_contrast], axis=-1).astype(jnp.float32)
    received = got_contrast_both * got_blocks.astype(jnp.float32) / got_level
    inserted = (1.0 - blend_weight) * received + blend_weight * shift_halves(received, 1, box_size)
    contrast_rows = got_contrast.astype(jnp.float32)
    squared = contrast_rows * contrast_rows
    weights = (1.0 - blend_weight) * squared + blend_weight * jnp.roll(squared, 1, axis=-1)
    seat_data = jnp.concatenate([inserted, weights], axis=-1) * live
    numerator = jnp.einsum(
        "sq,srx->qrx", slot_pick.astype(jnp.float32), seat_data, precision=HI,
        preferred_element_type=jnp.float32,
    )
    share = vrows // img_count
    numerator = numerator.reshape(planes, img_count, share, 3 * box_size).astype(jnp.bfloat16)
    numerator = jnp.swapaxes(numerator, 0, 1)
    volume_part = reduce_over_img(numerator, img_count)
    weight_sum = volume_part[..., 2 * box_size :]
    reconstruction = volume_part[..., : 2 * box_size] / (
        jnp.concatenate([weight_sum, weight_sum], axis=-1) + 1.0
    )

    whitened = spectrum / noise_level
    row_all = jnp.arange(box_size, dtype=jnp.int32)[None, :]
    contrast = contrast_curve(lookup_defocus(micrograph, defocus), row_all, box_size)
    own_rows = jnp.einsum(
        "rs,shix->rhix", seat_pick, returned_rows, preferred_element_type=jnp.float32
    ).astype(jnp.bfloat16)
    own_rows = own_rows.reshape(particles, blocks_per, 2, RB, box_size)
    own_rows = jnp.moveaxis(own_rows, 2, 1).reshape(particles, 2, 2 * low_rows, box_size)
    inner = box_size - 2 * low_rows
    inner_rows = whitened[:, :, low_rows : box_size - low_rows].astype(jnp.bfloat16)
    residual = []
    for n in range(particles):
        inner_back = back_rows_of(inner_rows[n], tables)
        edge = jnp.zeros((2, low_rows, box_size), jnp.bfloat16)
        inner_part = picture_of(jnp.concatenate([edge, inner_back, edge], axis=1), tables)
        routed_white = jnp.concatenate(
            [whitened[n, :, :low_rows], whitened[n, :, box_size - low_rows :]], axis=1
        )
        routed_contrast = jnp.concatenate(
            [contrast[n, :low_rows], contrast[n, box_size - low_rows :]], axis=0
        ).astype(jnp.float32)
        routed_difference = (
            routed_white - routed_contrast[None] * own_rows[n].astype(jnp.float32)
        ).astype(jnp.bfloat16)
        routed_back = back_rows_of(routed_difference, tables)
        middle = jnp.zeros((2, inner, box_size), jnp.bfloat16)
        routed_part = picture_of(
            jnp.concatenate([routed_back[:, :low_rows], middle, routed_back[:, low_rows:]], axis=1),
            tables,
        )
        residual.append(((inner_part + routed_part) / box_size).astype(jnp.bfloat16))
    residual = jnp.stack(residual)
    return (residual, reconstruction)


def solution(mesh):
    in_specs = (
        P(("img", "slab"), None, None),
        P(("img", "slab")),
        P(),
        P(("img", "slab"), None, None),
        P(("img", "slab"), None),
        P(("img", "slab"), None),
        P(("img", "slab"), None),
        P("slab", None, None),
    )
    out_specs = (P(("img", "slab"), None, None), P("slab", "img", None))
    return jax.shard_map(body, mesh=mesh, in_specs=in_specs, out_specs=out_specs, check_vma=False)
```

```python
import math

import jax
import ml_dtypes
import numpy as np
import jax.numpy as jnp
from jax import lax
from jax.sharding import PartitionSpec as P

RB = 16
LOW = 4
WL = 8
HI = lax.Precision.HIGHEST


def table_stack(box_size):
    positions = np.arange(box_size)
    angles = ((positions[:, None] * positions[None, :]) % box_size) * (2.0 * np.pi / box_size)
    both = np.stack([np.cos(angles), np.sin(angles)]).astype(ml_dtypes.bfloat16)
    return jnp.asarray(both)


def transform(image, tables):
    rowwise = jnp.einsum(
        "yx,hmx->hym", image, tables, preferred_element_type=jnp.float32
    ).astype(jnp.bfloat16)
    products = jnp.einsum("gky,hym->ghkm", tables, rowwise, preferred_element_type=jnp.float32)
    real = products[0, 0] - products[1, 1]
    imag = -(products[0, 1] + products[1, 0])
    return jnp.stack([real, imag])


def back_rows_of(difference, tables):
    products = jnp.einsum(
        "hyj,gmj->hgym", difference, tables, preferred_element_type=jnp.float32
    )
    back_real = products[0, 0] - products[1, 1]
    back_imag = products[0, 1] + products[1, 0]
    return jnp.stack([back_real, -back_imag]).astype(jnp.bfloat16)


def picture_of(back_rows, tables):
    picture = jnp.einsum("hxk,hkm->hxm", tables, back_rows, preferred_element_type=jnp.float32)
    return picture[0] + picture[1]


def radius_sq(row_ids, box_size):
    half_size = box_size // 2
    columns = jnp.arange(box_size, dtype=jnp.int32)
    freq_rows = jnp.where(row_ids < half_size, row_ids, row_ids - box_size)
    freq_cols = jnp.where(columns < half_size, columns, columns - box_size)
    total = freq_rows[..., None] * freq_rows[..., None] + freq_cols * freq_cols
    return total.astype(jnp.float32) / float(half_size * half_size)


def contrast_curve(defocus_of, row_ids, box_size):
    radius = radius_sq(row_ids, box_size)
    return (-jnp.sin(defocus_of[:, None, None] * radius + 0.1)).astype(jnp.bfloat16)


def lookup_defocus(mic_ids, defocus):
    labels = jnp.arange(defocus.shape[0], dtype=jnp.int32)
    return jnp.sum(jnp.where(mic_ids[:, None] == labels[None, :], defocus[None, :], 0.0), axis=1)


def shift_halves(values, steps, box_size):
    column = lax.broadcasted_iota(jnp.int32, values.shape, values.ndim - 1) % box_size
    seam = 0 if steps == 1 else box_size - 1
    rolled = jnp.roll(values, steps, axis=-1)
    wrapped = jnp.roll(values, -steps * (box_size - 1), axis=-1)
    return jnp.where(column == seam, wrapped, rolled)


def low_row_ids(block_ids, box_size):
    base = block_ids * RB + jnp.where(block_ids < LOW, 0, box_size - 2 * LOW * RB)
    return base[..., None] + jnp.arange(RB, dtype=jnp.int32)


def power_gather(total, device_count, rows, box_size):
    spread = jnp.broadcast_to(total, (device_count, total.shape[1]))
    back = lax.all_to_all(spread, ("img", "slab"), 0, 0, tiled=True)
    half = back.reshape(rows, box_size)
    zero = lax.optimization_barrier(jnp.zeros((), jnp.int32))
    n = lax.broadcasted_iota(jnp.int32, (box_size, box_size), 0) + zero
    m = lax.broadcasted_iota(jnp.int32, (box_size, box_size), 1)
    flip_columns = (n == (box_size - m) % box_size).astype(jnp.float32)
    flipped = jnp.dot(half, flip_columns, precision=HI)
    k = lax.broadcasted_iota(jnp.int32, (box_size, rows), 0) + zero
    j = lax.broadcasted_iota(jnp.int32, (box_size, rows), 1)
    keep = ((j == k) & (k <= box_size // 2)).astype(jnp.float32)
    turn = ((j == box_size - k) & (k > box_size // 2)).astype(jnp.float32)
    return jnp.dot(keep, half, precision=HI) + jnp.dot(turn, flipped, precision=HI)


def shift_exchange(values, count, capacity, direction):
    pieces = [values[:capacity]]
    for d in range(1, count):
        pairs = [(i, (i + direction * d) % count) for i in range(count)]
        pieces.append(lax.ppermute(values[d * capacity : (d + 1) * capacity], "slab", pairs))
    return jnp.concatenate(pieces, axis=0)


def reduce_over_img(numerator, count):
    me = lax.axis_index("img")
    total = lax.dynamic_index_in_dim(numerator, me, 0, keepdims=False).astype(jnp.float32)
    for d in range(1, count):
        piece = lax.dynamic_index_in_dim(numerator, (me + d) % count, 0, keepdims=False)
        pairs = [(i, (i + d) % count) for i in range(count)]
        total = total + lax.ppermute(piece, "img", pairs).astype(jnp.float32)
    return total


def half_rows(box_size, device_count):
    rows = box_size // 2 + 1
    while (rows * box_size) % device_count:
        rows += 1
    return rows


def body(images, micrograph, defocus, target_slab, target_plane, target_rows, shift_index, volume):
    particles, box_size = (images.shape[0], images.shape[1])
    slab_count = lax.axis_size("slab")
    img_count = lax.axis_size("img")
    device_count = img_count * slab_count
    low_rows = LOW * RB
    blocks_per = 2 * LOW
    routed = particles * blocks_per
    planes, vrows = volume.shape[0], volume.shape[1]
    row_blocks = vrows // RB
    slots = planes * row_blocks
    tables = lax.optimization_barrier(table_stack(box_size))

    destination = target_slab.reshape(routed)
    capacity = max(2, (2 * routed + slab_count - 1) // slab_count)
    member = (destination[:, None] == jnp.arange(slab_count, dtype=jnp.int32)[None, :]).astype(
        jnp.int32
    )
    before = jnp.cumsum(member, axis=0) - member
    slot_rank = jnp.sum(member * before, axis=1)
    me = lax.axis_index("slab")
    seat_index = destination * capacity + slot_rank
    seat_count = slab_count * capacity
    seat_pick = (seat_index[:, None] == jnp.arange(seat_count, dtype=jnp.int32)[None, :]).astype(
        jnp.bfloat16
    )
    source_block = jnp.tile(jnp.arange(blocks_per, dtype=jnp.int32), particles)
    block_info = jnp.stack(
        [
            jnp.ones((routed,), jnp.int32),
            target_plane.reshape(routed),
            target_rows.reshape(routed),
            shift_index.reshape(routed),
            source_block,
            jnp.repeat(micrograph, blocks_per),
        ],
        axis=1,
    ).astype(jnp.bfloat16)
    info_width = 128
    block_info = jnp.pad(block_info, ((0, 0), (0, info_width - block_info.shape[1])))

    spectrum = jnp.stack([transform(images[n], tables) for n in range(particles)])
    low_spectrum = jnp.concatenate(
        [spectrum[:, :, :low_rows], spectrum[:, :, box_size - low_rows :]], axis=2
    ).astype(jnp.bfloat16)
    low_spectrum = jnp.moveaxis(low_spectrum, 1, 2).reshape(routed, RB * 2 * box_size)
    payload = jnp.concatenate([low_spectrum, block_info], axis=1)
    send = jnp.einsum(
        "rs,rx->sx", seat_pick, payload, preferred_element_type=jnp.float32
    ).astype(jnp.bfloat16)
    rows_half = half_rows(box_size, device_count)
    low_half = spectrum[:, :, :rows_half]
    power_half = jnp.sum(low_half * low_half, axis=(0, 1))
    pieces = power_half.reshape(device_count, rows_half * box_size // device_count)
    gathered = lax.all_to_all(pieces, ("img", "slab"), 0, 0, tiled=True)
    total = jnp.sum(gathered, axis=0, keepdims=True)
    power = power_gather(total, device_count, rows_half, box_size)
    send, power = lax.optimization_barrier((send, power))
    got = lax.all_to_all(send, "slab", 0, 0, tiled=True)
    got_blocks = got[:, : RB * 2 * box_size].reshape(seat_count, RB, 2 * box_size)
    got_info = got[:, RB * 2 * box_size : RB * 2 * box_size + 6].astype(jnp.int32)

    live = got_info[:, 0].astype(jnp.float32)[:, None, None]
    slot_of = got_info[:, 1] * row_blocks + got_info[:, 2]
    slot_pick = (slot_of[:, None] == jnp.arange(slots, dtype=jnp.int32)[None, :]).astype(
        jnp.bfloat16
    )
    blend_weight = ((got_info[:, 3].astype(jnp.float32) + 0.5) / WL)[:, None, None]
    volume_slots = volume.reshape(planes, row_blocks, RB, 2, box_size)
    volume_slots = jnp.transpose(volume_slots, (0, 1, 3, 2, 4)).reshape(slots, 2, RB, box_size)
    nearby = jnp.einsum(
        "sq,qhix->shix", slot_pick, volume_slots, preferred_element_type=jnp.float32
    )
    blend_4 = blend_weight[:, :, :, None]
    projected = (
        ((1.0 - blend_4) * nearby + blend_4 * jnp.roll(nearby, -1, axis=-1)) * live[..., None]
    ).astype(jnp.bfloat16)

    noise_level = jnp.sqrt(power / (particles * device_count) + 1e-06)
    level_both = jnp.concatenate([noise_level, noise_level], axis=1)

    returned_rows = lax.all_to_all(projected, "slab", 0, 0, tiled=True)

    got_rows = low_row_ids(got_info[:, 4], box_size)
    got_contrast = contrast_curve(lookup_defocus(got_info[:, 5], defocus), got_rows, box_size)
    level_low = jnp.concatenate(
        [level_both[:low_rows], level_both[box_size - low_rows :]], axis=0
    ).reshape(blocks_per, RB, 2 * box_size)
    block_pick = (got_info[:, 4:5] == jnp.arange(blocks_per, dtype=jnp.int32)[None, :]).astype(
        jnp.float32
    )
    got_level = jnp.einsum(
        "sj,jix->six", block_pick, level_low, precision=HI, preferred_element_type=jnp.float32
    )
    got_contrast_both = jnp.concatenate([got_contrast, got_contrast], axis=-1).astype(jnp.float32)
    received = got_contrast_both * got_blocks.astype(jnp.float32) / got_level
    inserted = (1.0 - blend_weight) * received + blend_weight * shift_halves(received, 1, box_size)
    contrast_rows = got_contrast.astype(jnp.float32)
    squared = contrast_rows * contrast_rows
    weights = (1.0 - blend_weight) * squared + blend_weight * jnp.roll(squared, 1, axis=-1)
    seat_data = jnp.concatenate([inserted, weights], axis=-1) * live
    numerator = jnp.einsum(
        "sq,srx->qrx", slot_pick.astype(jnp.float32), seat_data, precision=HI,
        preferred_element_type=jnp.float32,
    )
    share = vrows // img_count
    numerator = numerator.reshape(planes, img_count, share, 3 * box_size).astype(jnp.bfloat16)
    numerator = jnp.swapaxes(numerator, 0, 1)
    volume_part = reduce_over_img(numerator, img_count)
    weight_sum = volume_part[..., 2 * box_size :]
    reconstruction = volume_part[..., : 2 * box_size] / (
        jnp.concatenate([weight_sum, weight_sum], axis=-1) + 1.0
    )

    whitened = spectrum / noise_level
    row_all = jnp.arange(box_size, dtype=jnp.int32)[None, :]
    contrast = contrast_curve(lookup_defocus(micrograph, defocus), row_all, box_size)
    own_rows = jnp.einsum(
        "rs,shix->rhix", seat_pick, returned_rows, preferred_element_type=jnp.float32
    ).astype(jnp.bfloat16)
    own_rows = own_rows.reshape(particles, blocks_per, 2, RB, box_size)
    own_rows = jnp.moveaxis(own_rows, 2, 1).reshape(particles, 2, 2 * low_rows, box_size)
    inner = box_size - 2 * low_rows
    inner_rows = whitened[:, :, low_rows : box_size - low_rows].astype(jnp.bfloat16)
    residual = []
    for n in range(particles):
        inner_back = back_rows_of(inner_rows[n], tables)
        edge = jnp.zeros((2, low_rows, box_size), jnp.bfloat16)
        inner_part = picture_of(jnp.concatenate([edge, inner_back, edge], axis=1), tables)
        routed_white = jnp.concatenate(
            [whitened[n, :, :low_rows], whitened[n, :, box_size - low_rows :]], axis=1
        )
        routed_contrast = jnp.concatenate(
            [contrast[n, :low_rows], contrast[n, box_size - low_rows :]], axis=0
        ).astype(jnp.float32)
        routed_difference = (
            routed_white - routed_contrast[None] * own_rows[n].astype(jnp.float32)
        ).astype(jnp.bfloat16)
        routed_back = back_rows_of(routed_difference, tables)
        middle = jnp.zeros((2, inner, box_size), jnp.bfloat16)
        routed_part = picture_of(
            jnp.concatenate([routed_back[:, :low_rows], middle, routed_back[:, low_rows:]], axis=1),
            tables,
        )
        residual.append(((inner_part + routed_part) / box_size).astype(jnp.bfloat16))
    residual = jnp.stack(residual)
    return (residual, reconstruction)


def solution(mesh):
    in_specs = (
        P(("img", "slab"), None, None),
        P(("img", "slab")),
        P(),
        P(("img", "slab"), None, None),
        P(("img", "slab"), None),
        P(("img", "slab"), None),
        P(("img", "slab"), None),
        P("slab", None, None),
    )
    out_specs = (P(("img", "slab"), None, None), P("slab", "img", None))
    return jax.shard_map(body, mesh=mesh, in_specs=in_specs, out_specs=out_specs, check_vma=False)
```

```python
import math

import jax
import ml_dtypes
import numpy as np
import jax.numpy as jnp
from jax import lax
from jax.sharding import PartitionSpec as P

RB = 16
LOW = 4
WL = 8
HI = lax.Precision.HIGHEST


def table_stack(box_size):
    positions = np.arange(box_size)
    angles = ((positions[:, None] * positions[None, :]) % box_size) * (2.0 * np.pi / box_size)
    both = np.stack([np.cos(angles), np.sin(angles)]).astype(ml_dtypes.bfloat16)
    return jnp.asarray(both)


def rowwise_of(image, tables):
    return jnp.einsum(
        "yx,hmx->hym", image, tables, preferred_element_type=jnp.float32
    ).astype(jnp.bfloat16)


def transform(rowwise, tables):
    products = jnp.einsum("gky,hym->ghkm", tables, rowwise, preferred_element_type=jnp.float32)
    real = products[0, 0] - products[1, 1]
    imag = -(products[0, 1] + products[1, 0])
    return jnp.stack([real, imag])


def back_rows_of(difference, tables):
    products = jnp.einsum(
        "hyj,gmj->hgym", difference, tables, preferred_element_type=jnp.float32
    )
    back_real = products[0, 0] - products[1, 1]
    back_imag = products[0, 1] + products[1, 0]
    return jnp.stack([back_real, -back_imag]).astype(jnp.bfloat16)


def picture_of(back_rows, tables):
    picture = jnp.einsum("hxk,hkm->hxm", tables, back_rows, preferred_element_type=jnp.float32)
    return picture[0] + picture[1]


def radius_sq(row_ids, box_size):
    half_size = box_size // 2
    columns = jnp.arange(box_size, dtype=jnp.int32)
    freq_rows = jnp.where(row_ids < half_size, row_ids, row_ids - box_size)
    freq_cols = jnp.where(columns < half_size, columns, columns - box_size)
    total = freq_rows[..., None] * freq_rows[..., None] + freq_cols * freq_cols
    return total.astype(jnp.float32) / float(half_size * half_size)


def contrast_curve(defocus_of, row_ids, box_size):
    radius = radius_sq(row_ids, box_size)
    return (-jnp.sin(defocus_of[:, None, None] * radius + 0.1)).astype(jnp.bfloat16)


def lookup_defocus(mic_ids, defocus):
    labels = jnp.arange(defocus.shape[0], dtype=jnp.int32)
    return jnp.sum(jnp.where(mic_ids[:, None] == labels[None, :], defocus[None, :], 0.0), axis=1)


def shift_halves(values, steps, box_size):
    column = lax.broadcasted_iota(jnp.int32, values.shape, values.ndim - 1) % box_size
    seam = 0 if steps == 1 else box_size - 1
    rolled = jnp.roll(values, steps, axis=-1)
    wrapped = jnp.roll(values, -steps * (box_size - 1), axis=-1)
    return jnp.where(column == seam, wrapped, rolled)


def low_row_ids(block_ids, box_size):
    base = block_ids * RB + jnp.where(block_ids < LOW, 0, box_size - 2 * LOW * RB)
    return base[..., None] + jnp.arange(RB, dtype=jnp.int32)


def power_gather(total, device_count, rows, box_size):
    spread = jnp.broadcast_to(total, (device_count, total.shape[1]))
    back = lax.all_to_all(spread, ("img", "slab"), 0, 0, tiled=True)
    half = back.reshape(rows, box_size)
    zero = lax.optimization_barrier(jnp.zeros((), jnp.int32))
    n = lax.broadcasted_iota(jnp.int32, (box_size, box_size), 0) + zero
    m = lax.broadcasted_iota(jnp.int32, (box_size, box_size), 1)
    flip_columns = (n == (box_size - m) % box_size).astype(jnp.float32)
    flipped = jnp.dot(half, flip_columns, precision=HI)
    k = lax.broadcasted_iota(jnp.int32, (box_size, rows), 0) + zero
    j = lax.broadcasted_iota(jnp.int32, (box_size, rows), 1)
    keep = ((j == k) & (k <= box_size // 2)).astype(jnp.float32)
    turn = ((j == box_size - k) & (k > box_size // 2)).astype(jnp.float32)
    return jnp.dot(keep, half, precision=HI) + jnp.dot(turn, flipped, precision=HI)


def shift_exchange(values, count, capacity, direction):
    pieces = [values[:capacity]]
    for d in range(1, count):
        pairs = [(i, (i + direction * d) % count) for i in range(count)]
        pieces.append(lax.ppermute(values[d * capacity : (d + 1) * capacity], "slab", pairs))
    return jnp.concatenate(pieces, axis=0)


def reduce_over_img(numerator, count):
    me = lax.axis_index("img")
    total = lax.dynamic_index_in_dim(numerator, me, 0, keepdims=False).astype(jnp.float32)
    for d in range(1, count):
        piece = lax.dynamic_index_in_dim(numerator, (me + d) % count, 0, keepdims=False)
        pairs = [(i, (i + d) % count) for i in range(count)]
        total = total + lax.ppermute(piece, "img", pairs).astype(jnp.float32)
    return total


def half_rows(box_size, device_count):
    rows = box_size // 2 + 1
    while (rows * box_size) % device_count:
        rows += 1
    return rows


def body(images, micrograph, defocus, target_slab, target_plane, target_rows, shift_index, volume):
    particles, box_size = (images.shape[0], images.shape[1])
    slab_count = lax.axis_size("slab")
    img_count = lax.axis_size("img")
    device_count = img_count * slab_count
    low_rows = LOW * RB
    blocks_per = 2 * LOW
    routed = particles * blocks_per
    planes, vrows = volume.shape[0], volume.shape[1]
    row_blocks = vrows // RB
    slots = planes * row_blocks
    tables = lax.optimization_barrier(table_stack(box_size))

    destination = target_slab.reshape(routed)
    capacity = max(2, (2 * routed + slab_count - 1) // slab_count)
    member = (destination[:, None] == jnp.arange(slab_count, dtype=jnp.int32)[None, :]).astype(
        jnp.int32
    )
    before = jnp.cumsum(member, axis=0) - member
    slot_rank = jnp.sum(member * before, axis=1)
    me = lax.axis_index("slab")
    seat_index = destination * capacity + slot_rank
    seat_count = slab_count * capacity
    seat_pick = (seat_index[:, None] == jnp.arange(seat_count, dtype=jnp.int32)[None, :]).astype(
        jnp.bfloat16
    )
    source_block = jnp.tile(jnp.arange(blocks_per, dtype=jnp.int32), particles)
    block_info = jnp.stack(
        [
            jnp.ones((routed,), jnp.int32),
            target_plane.reshape(routed),
            target_rows.reshape(routed),
            shift_index.reshape(routed),
            source_block,
            jnp.repeat(micrograph, blocks_per),
        ],
        axis=1,
    ).astype(jnp.bfloat16)
    info_width = 128
    block_info = jnp.pad(block_info, ((0, 0), (0, info_width - block_info.shape[1])))

    rowwise = [rowwise_of(images[n], tables) for n in range(particles)]
    spectrum = jnp.stack([transform(r, tables) for r in rowwise])
    low_spectrum = jnp.concatenate(
        [spectrum[:, :, :low_rows], spectrum[:, :, box_size - low_rows :]], axis=2
    ).astype(jnp.bfloat16)
    low_spectrum = jnp.moveaxis(low_spectrum, 1, 2).reshape(routed, RB * 2 * box_size)
    payload = jnp.concatenate([low_spectrum, block_info], axis=1)
    send = jnp.einsum(
        "rs,rx->sx", seat_pick, payload, preferred_element_type=jnp.float32
    ).astype(jnp.bfloat16)
    rows_half = half_rows(box_size, device_count)
    top_rows = -(-rows_half // RB) * RB
    low_half = jnp.stack([transform(r, tables[:, :top_rows]) for r in rowwise])[:, :, :rows_half]
    power_half = jnp.sum(low_half * low_half, axis=(0, 1))
    pieces = power_half.reshape(device_count, rows_half * box_size // device_count)
    gathered = lax.all_to_all(pieces, ("img", "slab"), 0, 0, tiled=True)
    got = lax.all_to_all(send, "slab", 0, 0, tiled=True)
    got_blocks = got[:, : RB * 2 * box_size].reshape(seat_count, RB, 2 * box_size)
    got_info = got[:, RB * 2 * box_size : RB * 2 * box_size + 6].astype(jnp.int32)

    live = got_info[:, 0].astype(jnp.float32)[:, None, None]
    slot_of = got_info[:, 1] * row_blocks + got_info[:, 2]
    slot_pick = (slot_of[:, None] == jnp.arange(slots, dtype=jnp.int32)[None, :]).astype(
        jnp.bfloat16
    )
    blend_weight = ((got_info[:, 3].astype(jnp.float32) + 0.5) / WL)[:, None, None]
    volume_slots = volume.reshape(planes, row_blocks, RB, 2, box_size)
    volume_slots = jnp.transpose(volume_slots, (0, 1, 3, 2, 4)).reshape(slots, 2, RB, box_size)
    nearby = jnp.einsum(
        "sq,qhix->shix", slot_pick, volume_slots, preferred_element_type=jnp.float32
    )
    blend_4 = blend_weight[:, :, :, None]
    projected = (
        ((1.0 - blend_4) * nearby + blend_4 * jnp.roll(nearby, -1, axis=-1)) * live[..., None]
    ).astype(jnp.bfloat16)

    total = jnp.sum(gathered, axis=0, keepdims=True)
    power = power_gather(total, device_count, rows_half, box_size)
    noise_level = jnp.sqrt(power / (particles * device_count) + 1e-06)
    level_both = jnp.concatenate([noise_level, noise_level], axis=1)

    returned_rows = lax.all_to_all(projected, "slab", 0, 0, tiled=True)

    got_rows = low_row_ids(got_info[:, 4], box_size)
    got_contrast = contrast_curve(lookup_defocus(got_info[:, 5], defocus), got_rows, box_size)
    level_low = jnp.concatenate(
        [level_both[:low_rows], level_both[box_size - low_rows :]], axis=0
    ).reshape(blocks_per, RB, 2 * box_size)
    block_pick = (got_info[:, 4:5] == jnp.arange(blocks_per, dtype=jnp.int32)[None, :]).astype(
        jnp.float32
    )
    got_level = jnp.einsum(
        "sj,jix->six", block_pick, level_low, precision=HI, preferred_element_type=jnp.float32
    )
    got_contrast_both = jnp.concatenate([got_contrast, got_contrast], axis=-1).astype(jnp.float32)
    received = got_contrast_both * got_blocks.astype(jnp.float32) / got_level
    inserted = (1.0 - blend_weight) * received + blend_weight * shift_halves(received, 1, box_size)
    contrast_rows = got_contrast.astype(jnp.float32)
    squared = contrast_rows * contrast_rows
    weights = (1.0 - blend_weight) * squared + blend_weight * jnp.roll(squared, 1, axis=-1)
    seat_data = jnp.concatenate([inserted, weights], axis=-1) * live
    numerator = jnp.einsum(
        "sq,srx->qrx", slot_pick.astype(jnp.float32), seat_data, precision=HI,
        preferred_element_type=jnp.float32,
    )
    share = vrows // img_count
    numerator = numerator.reshape(planes, img_count, share, 3 * box_size).astype(jnp.bfloat16)
    numerator = jnp.swapaxes(numerator, 0, 1)
    volume_part = reduce_over_img(numerator, img_count)
    weight_sum = volume_part[..., 2 * box_size :]
    reconstruction = volume_part[..., : 2 * box_size] / (
        jnp.concatenate([weight_sum, weight_sum], axis=-1) + 1.0
    )

    whitened = spectrum / noise_level
    row_all = jnp.arange(box_size, dtype=jnp.int32)[None, :]
    contrast = contrast_curve(lookup_defocus(micrograph, defocus), row_all, box_size)
    own_rows = jnp.einsum(
        "rs,shix->rhix", seat_pick, returned_rows, preferred_element_type=jnp.float32
    ).astype(jnp.bfloat16)
    own_rows = own_rows.reshape(particles, blocks_per, 2, RB, box_size)
    own_rows = jnp.moveaxis(own_rows, 2, 1).reshape(particles, 2, 2 * low_rows, box_size)
    inner = box_size - 2 * low_rows
    inner_rows = whitened[:, :, low_rows : box_size - low_rows].astype(jnp.bfloat16)
    residual = []
    for n in range(particles):
        inner_back = back_rows_of(inner_rows[n], tables)
        edge = jnp.zeros((2, low_rows, box_size), jnp.bfloat16)
        inner_part = picture_of(jnp.concatenate([edge, inner_back, edge], axis=1), tables)
        routed_white = jnp.concatenate(
            [whitened[n, :, :low_rows], whitened[n, :, box_size - low_rows :]], axis=1
        )
        routed_contrast = jnp.concatenate(
            [contrast[n, :low_rows], contrast[n, box_size - low_rows :]], axis=0
        ).astype(jnp.float32)
        routed_difference = (
            routed_white - routed_contrast[None] * own_rows[n].astype(jnp.float32)
        ).astype(jnp.bfloat16)
        routed_back = back_rows_of(routed_difference, tables)
        middle = jnp.zeros((2, inner, box_size), jnp.bfloat16)
        routed_part = picture_of(
            jnp.concatenate([routed_back[:, :low_rows], middle, routed_back[:, low_rows:]], axis=1),
            tables,
        )
        residual.append(((inner_part + routed_part) / box_size).astype(jnp.bfloat16))
    residual = jnp.stack(residual)
    return (residual, reconstruction)


def solution(mesh):
    in_specs = (
        P(("img", "slab"), None, None),
        P(("img", "slab")),
        P(),
        P(("img", "slab"), None, None),
        P(("img", "slab"), None),
        P(("img", "slab"), None),
        P(("img", "slab"), None),
        P("slab", None, None),
    )
    out_specs = (P(("img", "slab"), None, None), P("slab", "img", None))
    return jax.shard_map(body, mesh=mesh, in_specs=in_specs, out_specs=out_specs, check_vma=False)
```

```python
import math

import jax
import ml_dtypes
import numpy as np
import jax.numpy as jnp
from jax import lax
from jax.sharding import PartitionSpec as P

RB = 16
LOW = 4
WL = 8
HI = lax.Precision.HIGHEST


def table_stack(box_size):
    positions = np.arange(box_size)
    angles = ((positions[:, None] * positions[None, :]) % box_size) * (2.0 * np.pi / box_size)
    both = np.stack([np.cos(angles), np.sin(angles)]).astype(ml_dtypes.bfloat16)
    return jnp.asarray(both)


def rowwise_of(image, tables):
    return jnp.einsum(
        "yx,hmx->hym", image, tables, preferred_element_type=jnp.float32
    ).astype(jnp.bfloat16)


def transform(rowwise, tables):
    products = jnp.einsum("gky,hym->ghkm", tables, rowwise, preferred_element_type=jnp.float32)
    real = products[0, 0] - products[1, 1]
    imag = -(products[0, 1] + products[1, 0])
    return jnp.stack([real, imag])


def back_rows_of(difference, tables):
    products = jnp.einsum(
        "hyj,gmj->hgym", difference, tables, preferred_element_type=jnp.float32
    )
    back_real = products[0, 0] - products[1, 1]
    back_imag = products[0, 1] + products[1, 0]
    return jnp.stack([back_real, -back_imag]).astype(jnp.bfloat16)


def picture_of(back_rows, tables):
    picture = jnp.einsum("hxk,hkm->hxm", tables, back_rows, preferred_element_type=jnp.float32)
    return picture[0] + picture[1]


def radius_sq(row_ids, box_size):
    half_size = box_size // 2
    columns = jnp.arange(box_size, dtype=jnp.int32)
    freq_rows = jnp.where(row_ids < half_size, row_ids, row_ids - box_size)
    freq_cols = jnp.where(columns < half_size, columns, columns - box_size)
    total = freq_rows[..., None] * freq_rows[..., None] + freq_cols * freq_cols
    return total.astype(jnp.float32) / float(half_size * half_size)


def contrast_curve(defocus_of, row_ids, box_size):
    radius = radius_sq(row_ids, box_size)
    return (-jnp.sin(defocus_of[:, None, None] * radius + 0.1)).astype(jnp.bfloat16)


def lookup_defocus(mic_ids, defocus):
    labels = jnp.arange(defocus.shape[0], dtype=jnp.int32)
    return jnp.sum(jnp.where(mic_ids[:, None] == labels[None, :], defocus[None, :], 0.0), axis=1)


def shift_halves(values, steps, box_size):
    column = lax.broadcasted_iota(jnp.int32, values.shape, values.ndim - 1) % box_size
    seam = 0 if steps == 1 else box_size - 1
    rolled = jnp.roll(values, steps, axis=-1)
    wrapped = jnp.roll(values, -steps * (box_size - 1), axis=-1)
    return jnp.where(column == seam, wrapped, rolled)


def low_row_ids(block_ids, box_size):
    base = block_ids * RB + jnp.where(block_ids < LOW, 0, box_size - 2 * LOW * RB)
    return base[..., None] + jnp.arange(RB, dtype=jnp.int32)


def power_gather(total, device_count, rows, box_size):
    spread = jnp.broadcast_to(total, (device_count,) + total.shape[1:])
    back = lax.all_to_all(spread, ("img", "slab"), 0, 0, tiled=True)
    half = back.reshape(rows, box_size)
    zero = lax.optimization_barrier(jnp.zeros((), jnp.int32))
    n = lax.broadcasted_iota(jnp.int32, (box_size, box_size), 0) + zero
    m = lax.broadcasted_iota(jnp.int32, (box_size, box_size), 1)
    flip_columns = (n == (box_size - m) % box_size).astype(jnp.float32)
    flipped = jnp.dot(half, flip_columns, precision=HI)
    k = lax.broadcasted_iota(jnp.int32, (box_size, rows), 0) + zero
    j = lax.broadcasted_iota(jnp.int32, (box_size, rows), 1)
    keep = ((j == k) & (k <= box_size // 2)).astype(jnp.float32)
    turn = ((j == box_size - k) & (k > box_size // 2)).astype(jnp.float32)
    return jnp.dot(keep, half, precision=HI) + jnp.dot(turn, flipped, precision=HI)


def shift_exchange(values, count, capacity, direction):
    pieces = [values[:capacity]]
    for d in range(1, count):
        pairs = [(i, (i + direction * d) % count) for i in range(count)]
        pieces.append(lax.ppermute(values[d * capacity : (d + 1) * capacity], "slab", pairs))
    return jnp.concatenate(pieces, axis=0)


def reduce_over_img(numerator, count):
    me = lax.axis_index("img")
    total = lax.dynamic_index_in_dim(numerator, me, 0, keepdims=False).astype(jnp.float32)
    for d in range(1, count):
        piece = lax.dynamic_index_in_dim(numerator, (me + d) % count, 0, keepdims=False)
        pairs = [(i, (i + d) % count) for i in range(count)]
        total = total + lax.ppermute(piece, "img", pairs).astype(jnp.float32)
    return total


def half_rows(box_size, device_count):
    need = box_size // 2 + 1
    per = -(-(-(-need // device_count)) // 8) * 8
    if per * device_count <= box_size:
        return per * device_count, per
    rows = need
    while (rows * box_size) % device_count:
        rows += 1
    return rows, 0


def body(images, micrograph, defocus, target_slab, target_plane, target_rows, shift_index, volume):
    particles, box_size = (images.shape[0], images.shape[1])
    slab_count = lax.axis_size("slab")
    img_count = lax.axis_size("img")
    device_count = img_count * slab_count
    low_rows = LOW * RB
    blocks_per = 2 * LOW
    routed = particles * blocks_per
    planes, vrows = volume.shape[0], volume.shape[1]
    row_blocks = vrows // RB
    slots = planes * row_blocks
    tables = lax.optimization_barrier(table_stack(box_size))

    destination = target_slab.reshape(routed)
    capacity = max(2, (2 * routed + slab_count - 1) // slab_count)
    member = (destination[:, None] == jnp.arange(slab_count, dtype=jnp.int32)[None, :]).astype(
        jnp.int32
    )
    before = jnp.cumsum(member, axis=0) - member
    slot_rank = jnp.sum(member * before, axis=1)
    me = lax.axis_index("slab")
    seat_index = destination * capacity + slot_rank
    seat_count = slab_count * capacity
    seat_pick = (seat_index[:, None] == jnp.arange(seat_count, dtype=jnp.int32)[None, :]).astype(
        jnp.bfloat16
    )
    source_block = jnp.tile(jnp.arange(blocks_per, dtype=jnp.int32), particles)
    block_info = jnp.stack(
        [
            jnp.ones((routed,), jnp.int32),
            target_plane.reshape(routed),
            target_rows.reshape(routed),
            shift_index.reshape(routed),
            source_block,
            jnp.repeat(micrograph, blocks_per),
        ],
        axis=1,
    ).astype(jnp.bfloat16)
    info_width = 128
    block_info = jnp.pad(block_info, ((0, 0), (0, info_width - block_info.shape[1])))

    rowwise = [rowwise_of(images[n], tables) for n in range(particles)]
    spectrum = jnp.stack([transform(r, tables) for r in rowwise])
    low_spectrum = jnp.concatenate(
        [spectrum[:, :, :low_rows], spectrum[:, :, box_size - low_rows :]], axis=2
    ).astype(jnp.bfloat16)
    low_spectrum = jnp.moveaxis(low_spectrum, 1, 2).reshape(routed, RB * 2 * box_size)
    payload = jnp.concatenate([low_spectrum, block_info], axis=1)
    send = jnp.einsum(
        "rs,rx->sx", seat_pick, payload, preferred_element_type=jnp.float32
    ).astype(jnp.bfloat16)
    rows_half, rows_each = half_rows(box_size, device_count)
    top_rows = -(-rows_half // RB) * RB
    low_half = jnp.stack([transform(r, tables[:, :top_rows]) for r in rowwise])[:, :, :rows_half]
    power_half = jnp.sum(low_half * low_half, axis=(0, 1))
    if rows_each:
        pieces = power_half.reshape(device_count, rows_each, box_size)
    else:
        pieces = power_half.reshape(device_count, rows_half * box_size // device_count)
    gathered = lax.all_to_all(pieces, ("img", "slab"), 0, 0, tiled=True)
    got = lax.all_to_all(send, "slab", 0, 0, tiled=True)
    got_blocks = got[:, : RB * 2 * box_size].reshape(seat_count, RB, 2 * box_size)
    got_info = got[:, RB * 2 * box_size : RB * 2 * box_size + 6].astype(jnp.int32)

    live = got_info[:, 0].astype(jnp.float32)[:, None, None]
    slot_of = got_info[:, 1] * row_blocks + got_info[:, 2]
    slot_pick = (slot_of[:, None] == jnp.arange(slots, dtype=jnp.int32)[None, :]).astype(
        jnp.bfloat16
    )
    blend_weight = ((got_info[:, 3].astype(jnp.float32) + 0.5) / WL)[:, None, None]
    volume_slots = volume.reshape(planes, row_blocks, RB, 2, box_size)
    volume_slots = jnp.transpose(volume_slots, (0, 1, 3, 2, 4)).reshape(slots, 2, RB, box_size)
    nearby = jnp.einsum(
        "sq,qhix->shix", slot_pick, volume_slots, preferred_element_type=jnp.float32
    )
    blend_4 = blend_weight[:, :, :, None]
    projected = (
        ((1.0 - blend_4) * nearby + blend_4 * jnp.roll(nearby, -1, axis=-1)) * live[..., None]
    ).astype(jnp.bfloat16)

    total = jnp.sum(gathered, axis=0, keepdims=True)
    power = power_gather(total, device_count, rows_half, box_size)
    noise_level = jnp.sqrt(power / (particles * device_count) + 1e-06)
    level_both = jnp.concatenate([noise_level, noise_level], axis=1)

    returned_rows = lax.all_to_all(projected, "slab", 0, 0, tiled=True)

    got_rows = low_row_ids(got_info[:, 4], box_size)
    got_contrast = contrast_curve(lookup_defocus(got_info[:, 5], defocus), got_rows, box_size)
    level_low = jnp.concatenate(
        [level_both[:low_rows], level_both[box_size - low_rows :]], axis=0
    ).reshape(blocks_per, RB, 2 * box_size)
    block_pick = (got_info[:, 4:5] == jnp.arange(blocks_per, dtype=jnp.int32)[None, :]).astype(
        jnp.float32
    )
    got_level = jnp.einsum(
        "sj,jix->six", block_pick, level_low, precision=HI, preferred_element_type=jnp.float32
    )
    got_contrast_both = jnp.concatenate([got_contrast, got_contrast], axis=-1).astype(jnp.float32)
    received = got_contrast_both * got_blocks.astype(jnp.float32) / got_level
    inserted = (1.0 - blend_weight) * received + blend_weight * shift_halves(received, 1, box_size)
    contrast_rows = got_contrast.astype(jnp.float32)
    squared = contrast_rows * contrast_rows
    weights = (1.0 - blend_weight) * squared + blend_weight * jnp.roll(squared, 1, axis=-1)
    seat_data = jnp.concatenate([inserted, weights], axis=-1) * live
    numerator = jnp.einsum(
        "sq,srx->qrx", slot_pick.astype(jnp.float32), seat_data, precision=HI,
        preferred_element_type=jnp.float32,
    )
    share = vrows // img_count
    numerator = numerator.reshape(planes, img_count, share, 3 * box_size).astype(jnp.bfloat16)
    numerator = jnp.swapaxes(numerator, 0, 1)
    volume_part = reduce_over_img(numerator, img_count)
    weight_sum = volume_part[..., 2 * box_size :]
    reconstruction = volume_part[..., : 2 * box_size] / (
        jnp.concatenate([weight_sum, weight_sum], axis=-1) + 1.0
    )

    whitened = spectrum / noise_level
    row_all = jnp.arange(box_size, dtype=jnp.int32)[None, :]
    contrast = contrast_curve(lookup_defocus(micrograph, defocus), row_all, box_size)
    own_rows = jnp.einsum(
        "rs,shix->rhix", seat_pick, returned_rows, preferred_element_type=jnp.float32
    ).astype(jnp.bfloat16)
    own_rows = own_rows.reshape(particles, blocks_per, 2, RB, box_size)
    own_rows = jnp.moveaxis(own_rows, 2, 1).reshape(particles, 2, 2 * low_rows, box_size)
    inner = box_size - 2 * low_rows
    inner_rows = whitened[:, :, low_rows : box_size - low_rows].astype(jnp.bfloat16)
    residual = []
    for n in range(particles):
        inner_back = back_rows_of(inner_rows[n], tables)
        edge = jnp.zeros((2, low_rows, box_size), jnp.bfloat16)
        inner_part = picture_of(jnp.concatenate([edge, inner_back, edge], axis=1), tables)
        routed_white = jnp.concatenate(
            [whitened[n, :, :low_rows], whitened[n, :, box_size - low_rows :]], axis=1
        )
        routed_contrast = jnp.concatenate(
            [contrast[n, :low_rows], contrast[n, box_size - low_rows :]], axis=0
        ).astype(jnp.float32)
        routed_difference = (
            routed_white - routed_contrast[None] * own_rows[n].astype(jnp.float32)
        ).astype(jnp.bfloat16)
        routed_back = back_rows_of(routed_difference, tables)
        middle = jnp.zeros((2, inner, box_size), jnp.bfloat16)
        routed_part = picture_of(
            jnp.concatenate([routed_back[:, :low_rows], middle, routed_back[:, low_rows:]], axis=1),
            tables,
        )
        residual.append(((inner_part + routed_part) / box_size).astype(jnp.bfloat16))
    residual = jnp.stack(residual)
    return (residual, reconstruction)


def solution(mesh):
    in_specs = (
        P(("img", "slab"), None, None),
        P(("img", "slab")),
        P(),
        P(("img", "slab"), None, None),
        P(("img", "slab"), None),
        P(("img", "slab"), None),
        P(("img", "slab"), None),
        P("slab", None, None),
    )
    out_specs = (P(("img", "slab"), None, None), P("slab", "img", None))
    return jax.shard_map(body, mesh=mesh, in_specs=in_specs, out_specs=out_specs, check_vma=False)
```

```python
import math

import jax
import ml_dtypes
import numpy as np
import jax.numpy as jnp
from jax import lax
from jax.sharding import PartitionSpec as P

RB = 16
LOW = 4
WL = 8
HI = lax.Precision.HIGHEST


def table_stack(box_size):
    positions = np.arange(box_size)
    angles = ((positions[:, None] * positions[None, :]) % box_size) * (2.0 * np.pi / box_size)
    both = np.stack([np.cos(angles), np.sin(angles)]).astype(ml_dtypes.bfloat16)
    return jnp.asarray(both)


def rowwise_of(image, tables):
    return jnp.einsum(
        "yx,hmx->hym", image, tables, preferred_element_type=jnp.float32
    ).astype(jnp.bfloat16)


def transform(rowwise, tables):
    products = jnp.einsum("gky,hym->ghkm", tables, rowwise, preferred_element_type=jnp.float32)
    real = products[0, 0] - products[1, 1]
    imag = -(products[0, 1] + products[1, 0])
    return jnp.stack([real, imag])


def back_rows_of(difference, tables):
    products = jnp.einsum(
        "hyj,gmj->hgym", difference, tables, preferred_element_type=jnp.float32
    )
    back_real = products[0, 0] - products[1, 1]
    back_imag = products[0, 1] + products[1, 0]
    return jnp.stack([back_real, -back_imag]).astype(jnp.bfloat16)


def picture_of(back_rows, tables):
    picture = jnp.einsum("hxk,hkm->hxm", tables, back_rows, preferred_element_type=jnp.float32)
    return picture[0] + picture[1]


def radius_sq(row_ids, box_size):
    half_size = box_size // 2
    columns = jnp.arange(box_size, dtype=jnp.int32)
    freq_rows = jnp.where(row_ids < half_size, row_ids, row_ids - box_size)
    freq_cols = jnp.where(columns < half_size, columns, columns - box_size)
    total = freq_rows[..., None] * freq_rows[..., None] + freq_cols * freq_cols
    return total.astype(jnp.float32) / float(half_size * half_size)


def contrast_curve(defocus_of, row_ids, box_size):
    radius = radius_sq(row_ids, box_size)
    return (-jnp.sin(defocus_of[:, None, None] * radius + 0.1)).astype(jnp.bfloat16)


def lookup_defocus(mic_ids, defocus):
    labels = jnp.arange(defocus.shape[0], dtype=jnp.int32)
    return jnp.sum(jnp.where(mic_ids[:, None] == labels[None, :], defocus[None, :], 0.0), axis=1)


def shift_halves(values, steps, box_size):
    column = lax.broadcasted_iota(jnp.int32, values.shape, values.ndim - 1) % box_size
    seam = 0 if steps == 1 else box_size - 1
    rolled = jnp.roll(values, steps, axis=-1)
    wrapped = jnp.roll(values, -steps * (box_size - 1), axis=-1)
    return jnp.where(column == seam, wrapped, rolled)


def low_row_ids(block_ids, box_size):
    base = block_ids * RB + jnp.where(block_ids < LOW, 0, box_size - 2 * LOW * RB)
    return base[..., None] + jnp.arange(RB, dtype=jnp.int32)


def power_gather(total, device_count, rows, box_size):
    spread = jnp.broadcast_to(total, (device_count, total.shape[1]))
    back = lax.all_to_all(spread, ("img", "slab"), 0, 0, tiled=True)
    half = back.reshape(rows, box_size)
    zero = lax.optimization_barrier(jnp.zeros((), jnp.int32))
    n = lax.broadcasted_iota(jnp.int32, (box_size, box_size), 0) + zero
    m = lax.broadcasted_iota(jnp.int32, (box_size, box_size), 1)
    flip_columns = (n == (box_size - m) % box_size).astype(jnp.float32)
    flipped = jnp.dot(half, flip_columns, precision=HI)
    k = lax.broadcasted_iota(jnp.int32, (box_size, rows), 0) + zero
    j = lax.broadcasted_iota(jnp.int32, (box_size, rows), 1)
    keep = ((j == k) & (k <= box_size // 2)).astype(jnp.float32)
    turn = ((j == box_size - k) & (k > box_size // 2)).astype(jnp.float32)
    return jnp.dot(keep, half, precision=HI) + jnp.dot(turn, flipped, precision=HI)


def shift_exchange(values, count, capacity, direction):
    pieces = [values[:capacity]]
    for d in range(1, count):
        pairs = [(i, (i + direction * d) % count) for i in range(count)]
        pieces.append(lax.ppermute(values[d * capacity : (d + 1) * capacity], "slab", pairs))
    return jnp.concatenate(pieces, axis=0)


def reduce_over_img(numerator, count):
    me = lax.axis_index("img")
    total = lax.dynamic_index_in_dim(numerator, me, 0, keepdims=False).astype(jnp.float32)
    for d in range(1, count):
        piece = lax.dynamic_index_in_dim(numerator, (me + d) % count, 0, keepdims=False)
        pairs = [(i, (i + d) % count) for i in range(count)]
        total = total + lax.ppermute(piece, "img", pairs).astype(jnp.float32)
    return total


def half_rows(box_size, device_count):
    rows = box_size // 2 + 1
    while (rows * box_size) % device_count:
        rows += 1
    return rows


def body(images, micrograph, defocus, target_slab, target_plane, target_rows, shift_index, volume):
    particles, box_size = (images.shape[0], images.shape[1])
    slab_count = lax.axis_size("slab")
    img_count = lax.axis_size("img")
    device_count = img_count * slab_count
    low_rows = LOW * RB
    blocks_per = 2 * LOW
    routed = particles * blocks_per
    planes, vrows = volume.shape[0], volume.shape[1]
    row_blocks = vrows // RB
    slots = planes * row_blocks
    tables = lax.optimization_barrier(table_stack(box_size))

    destination = target_slab.reshape(routed)
    capacity = max(2, (2 * routed + slab_count - 1) // slab_count)
    member = (destination[:, None] == jnp.arange(slab_count, dtype=jnp.int32)[None, :]).astype(
        jnp.int32
    )
    before = jnp.cumsum(member, axis=0) - member
    slot_rank = jnp.sum(member * before, axis=1)
    me = lax.axis_index("slab")
    seat_index = destination * capacity + slot_rank
    seat_count = slab_count * capacity
    seat_pick = (seat_index[:, None] == jnp.arange(seat_count, dtype=jnp.int32)[None, :]).astype(
        jnp.bfloat16
    )
    source_block = jnp.tile(jnp.arange(blocks_per, dtype=jnp.int32), particles)
    block_info = jnp.stack(
        [
            jnp.ones((routed,), jnp.int32),
            target_plane.reshape(routed),
            target_rows.reshape(routed),
            shift_index.reshape(routed),
            source_block,
            jnp.repeat(micrograph, blocks_per),
        ],
        axis=1,
    ).astype(jnp.bfloat16)
    info_width = 128
    block_info = jnp.pad(block_info, ((0, 0), (0, info_width - block_info.shape[1])))

    rowwise = [rowwise_of(images[n], tables) for n in range(particles)]
    spectrum = jnp.stack([transform(r, tables) for r in rowwise])
    low_spectrum = jnp.concatenate(
        [spectrum[:, :, :low_rows], spectrum[:, :, box_size - low_rows :]], axis=2
    ).astype(jnp.bfloat16)
    low_spectrum = jnp.moveaxis(low_spectrum, 1, 2).reshape(routed, RB * 2 * box_size)
    payload = jnp.concatenate([low_spectrum, block_info], axis=1)
    send = jnp.einsum(
        "rs,rx->sx", seat_pick, payload, preferred_element_type=jnp.float32
    ).astype(jnp.bfloat16)
    rows_half = half_rows(box_size, device_count)
    top_rows = -(-rows_half // RB) * RB
    low_half = jnp.stack([transform(r, tables[:, :top_rows]) for r in rowwise])[:, :, :rows_half]
    power_half = jnp.sum(low_half * low_half, axis=(0, 1))
    pieces = power_half.reshape(device_count, rows_half * box_size // device_count)
    gathered = lax.all_to_all(pieces, ("img", "slab"), 0, 0, tiled=True)
    got = lax.all_to_all(send, "slab", 0, 0, tiled=True)
    got_blocks = got[:, : RB * 2 * box_size].reshape(seat_count, RB, 2 * box_size)
    got_info = got[:, RB * 2 * box_size : RB * 2 * box_size + 6].astype(jnp.int32)

    live = got_info[:, 0].astype(jnp.float32)[:, None, None]
    slot_of = got_info[:, 1] * row_blocks + got_info[:, 2]
    slot_pick = (slot_of[:, None] == jnp.arange(slots, dtype=jnp.int32)[None, :]).astype(
        jnp.bfloat16
    )
    blend_weight = ((got_info[:, 3].astype(jnp.float32) + 0.5) / WL)[:, None, None]
    volume_slots = volume.reshape(planes, row_blocks, RB, 2, box_size)
    volume_slots = jnp.transpose(volume_slots, (0, 1, 3, 2, 4)).reshape(slots, 2, RB, box_size)
    nearby = jnp.einsum(
        "sq,qhix->shix", slot_pick, volume_slots, preferred_element_type=jnp.float32
    )
    blend_4 = blend_weight[:, :, :, None]
    projected = (
        ((1.0 - blend_4) * nearby + blend_4 * jnp.roll(nearby, -1, axis=-1)) * live[..., None]
    ).astype(jnp.bfloat16)

    total = jnp.sum(gathered, axis=0, keepdims=True)
    power = power_gather(total, device_count, rows_half, box_size)
    noise_level = jnp.sqrt(power / (particles * device_count) + 1e-06)
    level_both = jnp.concatenate([noise_level, noise_level], axis=1)

    returned_rows = lax.all_to_all(
        projected.reshape(seat_count, 2 * RB * box_size), "slab", 0, 0, tiled=True
    ).reshape(projected.shape)

    got_rows = low_row_ids(got_info[:, 4], box_size)
    got_contrast = contrast_curve(lookup_defocus(got_info[:, 5], defocus), got_rows, box_size)
    level_low = jnp.concatenate(
        [level_both[:low_rows], level_both[box_size - low_rows :]], axis=0
    ).reshape(blocks_per, RB, 2 * box_size)
    block_pick = (got_info[:, 4:5] == jnp.arange(blocks_per, dtype=jnp.int32)[None, :]).astype(
        jnp.float32
    )
    got_level = jnp.einsum(
        "sj,jix->six", block_pick, level_low, precision=HI, preferred_element_type=jnp.float32
    )
    got_contrast_both = jnp.concatenate([got_contrast, got_contrast], axis=-1).astype(jnp.float32)
    received = got_contrast_both * got_blocks.astype(jnp.float32) / got_level
    inserted = (1.0 - blend_weight) * received + blend_weight * shift_halves(received, 1, box_size)
    contrast_rows = got_contrast.astype(jnp.float32)
    squared = contrast_rows * contrast_rows
    weights = (1.0 - blend_weight) * squared + blend_weight * jnp.roll(squared, 1, axis=-1)
    seat_data = jnp.concatenate([inserted, weights], axis=-1) * live
    numerator = jnp.einsum(
        "sq,srx->qrx", slot_pick.astype(jnp.float32), seat_data, precision=HI,
        preferred_element_type=jnp.float32,
    )
    share = vrows // img_count
    numerator = numerator.reshape(planes, img_count, share, 3 * box_size).astype(jnp.bfloat16)
    numerator = jnp.swapaxes(numerator, 0, 1)
    volume_part = reduce_over_img(numerator, img_count)
    weight_sum = volume_part[..., 2 * box_size :]
    reconstruction = volume_part[..., : 2 * box_size] / (
        jnp.concatenate([weight_sum, weight_sum], axis=-1) + 1.0
    )

    whitened = spectrum / noise_level
    row_all = jnp.arange(box_size, dtype=jnp.int32)[None, :]
    contrast = contrast_curve(lookup_defocus(micrograph, defocus), row_all, box_size)
    own_rows = jnp.einsum(
        "rs,shix->rhix", seat_pick, returned_rows, preferred_element_type=jnp.float32
    ).astype(jnp.bfloat16)
    own_rows = own_rows.reshape(particles, blocks_per, 2, RB, box_size)
    own_rows = jnp.moveaxis(own_rows, 2, 1).reshape(particles, 2, 2 * low_rows, box_size)
    inner = box_size - 2 * low_rows
    inner_rows = whitened[:, :, low_rows : box_size - low_rows].astype(jnp.bfloat16)
    residual = []
    for n in range(particles):
        inner_back = back_rows_of(inner_rows[n], tables)
        edge = jnp.zeros((2, low_rows, box_size), jnp.bfloat16)
        inner_part = picture_of(jnp.concatenate([edge, inner_back, edge], axis=1), tables)
        routed_white = jnp.concatenate(
            [whitened[n, :, :low_rows], whitened[n, :, box_size - low_rows :]], axis=1
        )
        routed_contrast = jnp.concatenate(
            [contrast[n, :low_rows], contrast[n, box_size - low_rows :]], axis=0
        ).astype(jnp.float32)
        routed_difference = (
            routed_white - routed_contrast[None] * own_rows[n].astype(jnp.float32)
        ).astype(jnp.bfloat16)
        routed_back = back_rows_of(routed_difference, tables)
        middle = jnp.zeros((2, inner, box_size), jnp.bfloat16)
        routed_part = picture_of(
            jnp.concatenate([routed_back[:, :low_rows], middle, routed_back[:, low_rows:]], axis=1),
            tables,
        )
        residual.append(((inner_part + routed_part) / box_size).astype(jnp.bfloat16))
    residual = jnp.stack(residual)
    return (residual, reconstruction)


def solution(mesh):
    in_specs = (
        P(("img", "slab"), None, None),
        P(("img", "slab")),
        P(),
        P(("img", "slab"), None, None),
        P(("img", "slab"), None),
        P(("img", "slab"), None),
        P(("img", "slab"), None),
        P("slab", None, None),
    )
    out_specs = (P(("img", "slab"), None, None), P("slab", "img", None))
    return jax.shard_map(body, mesh=mesh, in_specs=in_specs, out_specs=out_specs, check_vma=False)
```

```python
import math

import jax
import ml_dtypes
import numpy as np
import jax.numpy as jnp
from jax import lax
from jax.sharding import PartitionSpec as P

RB = 16
LOW = 4
WL = 8
HI = lax.Precision.HIGHEST


def table_stack(box_size):
    positions = np.arange(box_size)
    angles = ((positions[:, None] * positions[None, :]) % box_size) * (2.0 * np.pi / box_size)
    both = np.stack([np.cos(angles), np.sin(angles)]).astype(ml_dtypes.bfloat16)
    return jnp.asarray(both)


def rowwise_of(image, tables):
    return jnp.einsum(
        "yx,hmx->hym", image, tables, preferred_element_type=jnp.float32
    ).astype(jnp.bfloat16)


def transform(rowwise, tables):
    products = jnp.einsum("gky,hym->ghkm", tables, rowwise, preferred_element_type=jnp.float32)
    real = products[0, 0] - products[1, 1]
    imag = -(products[0, 1] + products[1, 0])
    return jnp.stack([real, imag])


def back_rows_of(difference, tables):
    products = jnp.einsum(
        "hyj,gmj->hgym", difference, tables, preferred_element_type=jnp.float32
    )
    back_real = products[0, 0] - products[1, 1]
    back_imag = products[0, 1] + products[1, 0]
    return jnp.stack([back_real, -back_imag]).astype(jnp.bfloat16)


def picture_of(back_rows, tables):
    picture = jnp.einsum("hxk,hkm->hxm", tables, back_rows, preferred_element_type=jnp.float32)
    return picture[0] + picture[1]


def radius_sq(row_ids, box_size):
    half_size = box_size // 2
    columns = jnp.arange(box_size, dtype=jnp.int32)
    freq_rows = jnp.where(row_ids < half_size, row_ids, row_ids - box_size)
    freq_cols = jnp.where(columns < half_size, columns, columns - box_size)
    total = freq_rows[..., None] * freq_rows[..., None] + freq_cols * freq_cols
    return total.astype(jnp.float32) / float(half_size * half_size)


def contrast_curve(defocus_of, row_ids, box_size):
    radius = radius_sq(row_ids, box_size)
    return (-jnp.sin(defocus_of[:, None, None] * radius + 0.1)).astype(jnp.bfloat16)


def lookup_defocus(mic_ids, defocus):
    labels = jnp.arange(defocus.shape[0], dtype=jnp.int32)
    return jnp.sum(jnp.where(mic_ids[:, None] == labels[None, :], defocus[None, :], 0.0), axis=1)


def shift_halves(values, steps, box_size):
    column = lax.broadcasted_iota(jnp.int32, values.shape, values.ndim - 1) % box_size
    seam = 0 if steps == 1 else box_size - 1
    rolled = jnp.roll(values, steps, axis=-1)
    wrapped = jnp.roll(values, -steps * (box_size - 1), axis=-1)
    return jnp.where(column == seam, wrapped, rolled)


def low_row_ids(block_ids, box_size):
    base = block_ids * RB + jnp.where(block_ids < LOW, 0, box_size - 2 * LOW * RB)
    return base[..., None] + jnp.arange(RB, dtype=jnp.int32)


def power_gather(total, device_count, rows, box_size):
    spread = jnp.broadcast_to(total, (device_count, total.shape[1]))
    back = lax.all_to_all(spread, ("img", "slab"), 0, 0, tiled=True)
    half = back.reshape(rows, box_size)
    zero = lax.optimization_barrier(jnp.zeros((), jnp.int32))
    n = lax.broadcasted_iota(jnp.int32, (box_size, box_size), 0) + zero
    m = lax.broadcasted_iota(jnp.int32, (box_size, box_size), 1)
    flip_columns = (n == (box_size - m) % box_size).astype(jnp.float32)
    flipped = jnp.dot(half, flip_columns, precision=HI)
    k = lax.broadcasted_iota(jnp.int32, (box_size, rows), 0) + zero
    j = lax.broadcasted_iota(jnp.int32, (box_size, rows), 1)
    keep = ((j == k) & (k <= box_size // 2)).astype(jnp.float32)
    turn = ((j == box_size - k) & (k > box_size // 2)).astype(jnp.float32)
    return jnp.dot(keep, half, precision=HI) + jnp.dot(turn, flipped, precision=HI)


def shift_exchange(values, count, capacity, direction):
    pieces = [values[:capacity]]
    for d in range(1, count):
        pairs = [(i, (i + direction * d) % count) for i in range(count)]
        pieces.append(lax.ppermute(values[d * capacity : (d + 1) * capacity], "slab", pairs))
    return jnp.concatenate(pieces, axis=0)


def reduce_over_img(numerator, count):
    me = lax.axis_index("img")
    total = lax.dynamic_index_in_dim(numerator, me, 0, keepdims=False).astype(jnp.float32)
    for d in range(1, count):
        piece = lax.dynamic_index_in_dim(numerator, (me + d) % count, 0, keepdims=False)
        pairs = [(i, (i + d) % count) for i in range(count)]
        total = total + lax.ppermute(piece, "img", pairs).astype(jnp.float32)
    return total


def half_rows(box_size, device_count):
    rows = box_size // 2 + 1
    while (rows * box_size) % device_count:
        rows += 1
    return rows


def body(images, micrograph, defocus, target_slab, target_plane, target_rows, shift_index, volume):
    particles, box_size = (images.shape[0], images.shape[1])
    slab_count = lax.axis_size("slab")
    img_count = lax.axis_size("img")
    device_count = img_count * slab_count
    low_rows = LOW * RB
    blocks_per = 2 * LOW
    routed = particles * blocks_per
    planes, vrows = volume.shape[0], volume.shape[1]
    row_blocks = vrows // RB
    slots = planes * row_blocks
    tables = lax.optimization_barrier(table_stack(box_size))

    destination = target_slab.reshape(routed)
    capacity = max(2, (2 * routed + slab_count - 1) // slab_count)
    member = (destination[:, None] == jnp.arange(slab_count, dtype=jnp.int32)[None, :]).astype(
        jnp.int32
    )
    before = jnp.cumsum(member, axis=0) - member
    slot_rank = jnp.sum(member * before, axis=1)
    me = lax.axis_index("slab")
    seat_index = destination * capacity + slot_rank
    seat_count = slab_count * capacity
    seat_pick = (seat_index[:, None] == jnp.arange(seat_count, dtype=jnp.int32)[None, :]).astype(
        jnp.bfloat16
    )
    source_block = jnp.tile(jnp.arange(blocks_per, dtype=jnp.int32), particles)
    block_info = jnp.stack(
        [
            jnp.ones((routed,), jnp.int32),
            target_plane.reshape(routed),
            target_rows.reshape(routed),
            shift_index.reshape(routed),
            source_block,
            jnp.repeat(micrograph, blocks_per),
        ],
        axis=1,
    ).astype(jnp.bfloat16)
    info_width = 128
    block_info = jnp.pad(block_info, ((0, 0), (0, info_width - block_info.shape[1])))

    rowwise = [rowwise_of(images[n], tables) for n in range(particles)]
    spectrum = jnp.stack([transform(r, tables) for r in rowwise])
    low_spectrum = jnp.concatenate(
        [spectrum[:, :, :low_rows], spectrum[:, :, box_size - low_rows :]], axis=2
    ).astype(jnp.bfloat16)
    low_spectrum = jnp.moveaxis(low_spectrum, 1, 2).reshape(routed, RB * 2 * box_size)
    payload = jnp.concatenate([low_spectrum, block_info], axis=1)
    send = jnp.einsum(
        "rs,rx->sx", seat_pick, payload, preferred_element_type=jnp.float32
    ).astype(jnp.bfloat16)
    rows_half = half_rows(box_size, device_count)
    top_rows = -(-rows_half // RB) * RB
    low_half = jnp.stack([transform(r, tables[:, :top_rows]) for r in rowwise])[:, :, :rows_half]
    power_half = jnp.sum(low_half * low_half, axis=(0, 1))
    pieces = power_half.reshape(device_count, rows_half * box_size // device_count)
    gathered = lax.all_to_all(pieces, ("img", "slab"), 0, 0, tiled=True)
    got = lax.all_to_all(send, "slab", 0, 0, tiled=True)
    got_blocks = got[:, : RB * 2 * box_size].reshape(seat_count, RB, 2 * box_size)
    got_info = got[:, RB * 2 * box_size : RB * 2 * box_size + 6].astype(jnp.int32)

    live = got_info[:, 0].astype(jnp.float32)[:, None, None]
    slot_of = got_info[:, 1] * row_blocks + got_info[:, 2]
    slot_pick = (slot_of[:, None] == jnp.arange(slots, dtype=jnp.int32)[None, :]).astype(
        jnp.bfloat16
    )
    blend_weight = ((got_info[:, 3].astype(jnp.float32) + 0.5) / WL)[:, None, None]
    volume_slots = volume.reshape(planes, row_blocks, RB, 2, box_size)
    volume_slots = jnp.transpose(volume_slots, (0, 1, 3, 2, 4)).reshape(slots, 2, RB, box_size)
    nearby = jnp.einsum(
        "sq,qhix->shix", slot_pick, volume_slots, preferred_element_type=jnp.float32
    )
    blend_4 = blend_weight[:, :, :, None]
    projected = (
        ((1.0 - blend_4) * nearby + blend_4 * jnp.roll(nearby, -1, axis=-1)) * live[..., None]
    ).astype(jnp.bfloat16)

    total = jnp.sum(gathered, axis=0, keepdims=True)
    power = power_gather(total, device_count, rows_half, box_size)
    noise_level = jnp.sqrt(power / (particles * device_count) + 1e-06)
    level_both = jnp.concatenate([noise_level, noise_level], axis=1)

    returned_rows = lax.all_to_all(projected, "slab", 0, 0, tiled=True)

    got_rows = low_row_ids(got_info[:, 4], box_size)
    got_contrast = contrast_curve(lookup_defocus(got_info[:, 5], defocus), got_rows, box_size)
    level_low = jnp.concatenate(
        [level_both[:low_rows], level_both[box_size - low_rows :]], axis=0
    ).reshape(blocks_per, RB, 2 * box_size)
    block_pick = (got_info[:, 4:5] == jnp.arange(blocks_per, dtype=jnp.int32)[None, :]).astype(
        jnp.float32
    )
    got_level = jnp.einsum(
        "sj,jix->six", block_pick, level_low, precision=HI, preferred_element_type=jnp.float32
    )
    got_contrast_both = jnp.concatenate([got_contrast, got_contrast], axis=-1).astype(jnp.float32)
    received = got_contrast_both * got_blocks.astype(jnp.float32) / got_level
    inserted = (1.0 - blend_weight) * received + blend_weight * shift_halves(received, 1, box_size)
    contrast_rows = got_contrast.astype(jnp.float32)
    squared = contrast_rows * contrast_rows
    weights = (1.0 - blend_weight) * squared + blend_weight * jnp.roll(squared, 1, axis=-1)
    seat_data = jnp.concatenate([inserted, weights], axis=-1) * live
    numerator = jnp.einsum(
        "sq,srx->qrx", slot_pick.astype(jnp.float32), seat_data, precision=HI,
        preferred_element_type=jnp.float32,
    )
    share = vrows // img_count
    numerator = numerator.reshape(planes, img_count, share, 3 * box_size).astype(jnp.bfloat16)
    numerator = jnp.swapaxes(numerator, 0, 1)
    volume_part = reduce_over_img(numerator, img_count)
    weight_sum = volume_part[..., 2 * box_size :]
    reconstruction = volume_part[..., : 2 * box_size] / (
        jnp.concatenate([weight_sum, weight_sum], axis=-1) + 1.0
    )

    whitened = spectrum / noise_level
    row_all = jnp.arange(box_size, dtype=jnp.int32)[None, :]
    contrast = contrast_curve(lookup_defocus(micrograph, defocus), row_all, box_size)
    own_rows = jnp.einsum(
        "rs,shix->rhix", seat_pick, returned_rows, preferred_element_type=jnp.float32
    ).astype(jnp.bfloat16)
    own_rows = own_rows.reshape(particles, blocks_per, 2, RB, box_size)
    own_rows = jnp.moveaxis(own_rows, 2, 1).reshape(particles, 2, 2 * low_rows, box_size)
    inner = box_size - 2 * low_rows
    inner_rows = whitened[:, :, low_rows : box_size - low_rows].astype(jnp.bfloat16)
    routed_tables = jnp.concatenate(
        [tables[:, :, :low_rows], tables[:, :, box_size - low_rows :]], axis=2
    )
    residual = []
    for n in range(particles):
        inner_back = back_rows_of(inner_rows[n], tables)
        edge = jnp.zeros((2, low_rows, box_size), jnp.bfloat16)
        inner_part = picture_of(jnp.concatenate([edge, inner_back, edge], axis=1), tables)
        routed_white = jnp.concatenate(
            [whitened[n, :, :low_rows], whitened[n, :, box_size - low_rows :]], axis=1
        )
        routed_contrast = jnp.concatenate(
            [contrast[n, :low_rows], contrast[n, box_size - low_rows :]], axis=0
        ).astype(jnp.float32)
        routed_difference = (
            routed_white - routed_contrast[None] * own_rows[n].astype(jnp.float32)
        ).astype(jnp.bfloat16)
        routed_back = back_rows_of(routed_difference, tables)
        routed_part = picture_of(routed_back, routed_tables)
        residual.append(((inner_part + routed_part) / box_size).astype(jnp.bfloat16))
    residual = jnp.stack(residual)
    return (residual, reconstruction)


def solution(mesh):
    in_specs = (
        P(("img", "slab"), None, None),
        P(("img", "slab")),
        P(),
        P(("img", "slab"), None, None),
        P(("img", "slab"), None),
        P(("img", "slab"), None),
        P(("img", "slab"), None),
        P("slab", None, None),
    )
    out_specs = (P(("img", "slab"), None, None), P("slab", "img", None))
    return jax.shard_map(body, mesh=mesh, in_specs=in_specs, out_specs=out_specs, check_vma=False)
```

```python
import math

import jax
import ml_dtypes
import numpy as np
import jax.numpy as jnp
from jax import lax
from jax.sharding import PartitionSpec as P

RB = 16
LOW = 4
WL = 8
HI = lax.Precision.HIGHEST


def table_stack(box_size):
    positions = np.arange(box_size)
    angles = ((positions[:, None] * positions[None, :]) % box_size) * (2.0 * np.pi / box_size)
    both = np.stack([np.cos(angles), np.sin(angles)]).astype(ml_dtypes.bfloat16)
    return jnp.asarray(both)


def rowwise_of(image, tables):
    return jnp.einsum(
        "yx,hmx->hym", image, tables, preferred_element_type=jnp.float32
    ).astype(jnp.bfloat16)


def transform(rowwise, tables):
    products = jnp.einsum("gky,hym->ghkm", tables, rowwise, preferred_element_type=jnp.float32)
    real = products[0, 0] - products[1, 1]
    imag = -(products[0, 1] + products[1, 0])
    return jnp.stack([real, imag])


def back_rows_of(difference, tables):
    products = jnp.einsum(
        "hyj,gmj->hgym", difference, tables, preferred_element_type=jnp.float32
    )
    back_real = products[0, 0] - products[1, 1]
    back_imag = products[0, 1] + products[1, 0]
    return jnp.stack([back_real, -back_imag]).astype(jnp.bfloat16)


def picture_of(back_rows, tables):
    picture = jnp.einsum("hxk,hkm->hxm", tables, back_rows, preferred_element_type=jnp.float32)
    return picture[0] + picture[1]


def radius_sq(row_ids, box_size):
    half_size = box_size // 2
    columns = jnp.arange(box_size, dtype=jnp.int32)
    freq_rows = jnp.where(row_ids < half_size, row_ids, row_ids - box_size)
    freq_cols = jnp.where(columns < half_size, columns, columns - box_size)
    total = freq_rows[..., None] * freq_rows[..., None] + freq_cols * freq_cols
    return total.astype(jnp.float32) / float(half_size * half_size)


def contrast_curve(defocus_of, row_ids, box_size):
    radius = radius_sq(row_ids, box_size)
    return (-jnp.sin(defocus_of[:, None, None] * radius + 0.1)).astype(jnp.bfloat16)


def lookup_defocus(mic_ids, defocus):
    labels = jnp.arange(defocus.shape[0], dtype=jnp.int32)
    return jnp.sum(jnp.where(mic_ids[:, None] == labels[None, :], defocus[None, :], 0.0), axis=1)


def shift_halves(values, steps, box_size):
    column = lax.broadcasted_iota(jnp.int32, values.shape, values.ndim - 1) % box_size
    seam = 0 if steps == 1 else box_size - 1
    rolled = jnp.roll(values, steps, axis=-1)
    wrapped = jnp.roll(values, -steps * (box_size - 1), axis=-1)
    return jnp.where(column == seam, wrapped, rolled)


def low_row_ids(block_ids, box_size):
    base = block_ids * RB + jnp.where(block_ids < LOW, 0, box_size - 2 * LOW * RB)
    return base[..., None] + jnp.arange(RB, dtype=jnp.int32)


def power_gather(total, device_count, rows, box_size):
    spread = jnp.broadcast_to(total, (device_count, total.shape[1]))
    back = lax.all_to_all(spread, ("img", "slab"), 0, 0, tiled=True)
    half = back.reshape(rows, box_size)
    zero = lax.optimization_barrier(jnp.zeros((), jnp.int32))
    n = lax.broadcasted_iota(jnp.int32, (box_size, box_size), 0) + zero
    m = lax.broadcasted_iota(jnp.int32, (box_size, box_size), 1)
    flip_columns = (n == (box_size - m) % box_size).astype(jnp.float32)
    flipped = jnp.dot(half, flip_columns, precision=HI)
    k = lax.broadcasted_iota(jnp.int32, (box_size, rows), 0) + zero
    j = lax.broadcasted_iota(jnp.int32, (box_size, rows), 1)
    keep = ((j == k) & (k <= box_size // 2)).astype(jnp.float32)
    turn = ((j == box_size - k) & (k > box_size // 2)).astype(jnp.float32)
    return jnp.dot(keep, half, precision=HI) + jnp.dot(turn, flipped, precision=HI)


def shift_exchange(values, count, capacity, direction):
    pieces = [values[:capacity]]
    for d in range(1, count):
        pairs = [(i, (i + direction * d) % count) for i in range(count)]
        pieces.append(lax.ppermute(values[d * capacity : (d + 1) * capacity], "slab", pairs))
    return jnp.concatenate(pieces, axis=0)


def reduce_over_img(numerator, count):
    me = lax.axis_index("img")
    total = lax.dynamic_index_in_dim(numerator, me, 0, keepdims=False).astype(jnp.float32)
    for d in range(1, count):
        piece = lax.dynamic_index_in_dim(numerator, (me + d) % count, 0, keepdims=False)
        pairs = [(i, (i + d) % count) for i in range(count)]
        total = total + lax.ppermute(piece, "img", pairs).astype(jnp.float32)
    return total


def half_rows(box_size, device_count):
    rows = box_size // 2 + 1
    while (rows * box_size) % device_count:
        rows += 1
    return rows


def body(images, micrograph, defocus, target_slab, target_plane, target_rows, shift_index, volume):
    particles, box_size = (images.shape[0], images.shape[1])
    slab_count = lax.axis_size("slab")
    img_count = lax.axis_size("img")
    device_count = img_count * slab_count
    low_rows = LOW * RB
    blocks_per = 2 * LOW
    routed = particles * blocks_per
    planes, vrows = volume.shape[0], volume.shape[1]
    row_blocks = vrows // RB
    slots = planes * row_blocks
    tables = lax.optimization_barrier(table_stack(box_size))

    destination = target_slab.reshape(routed)
    capacity = max(2, (2 * routed + slab_count - 1) // slab_count)
    member = (destination[:, None] == jnp.arange(slab_count, dtype=jnp.int32)[None, :]).astype(
        jnp.int32
    )
    before = jnp.cumsum(member, axis=0) - member
    slot_rank = jnp.sum(member * before, axis=1)
    me = lax.axis_index("slab")
    seat_index = destination * capacity + slot_rank
    seat_count = slab_count * capacity
    seat_pick = (seat_index[:, None] == jnp.arange(seat_count, dtype=jnp.int32)[None, :]).astype(
        jnp.bfloat16
    )
    source_block = jnp.tile(jnp.arange(blocks_per, dtype=jnp.int32), particles)
    block_info = jnp.stack(
        [
            jnp.ones((routed,), jnp.int32),
            target_plane.reshape(routed),
            target_rows.reshape(routed),
            shift_index.reshape(routed),
            source_block,
            jnp.repeat(micrograph, blocks_per),
        ],
        axis=1,
    ).astype(jnp.bfloat16)
    info_width = 128
    block_info = jnp.pad(block_info, ((0, 0), (0, info_width - block_info.shape[1])))

    rowwise = [rowwise_of(images[n], tables) for n in range(particles)]
    spectrum = jnp.stack([transform(r, tables) for r in rowwise])
    low_spectrum = jnp.concatenate(
        [spectrum[:, :, :low_rows], spectrum[:, :, box_size - low_rows :]], axis=2
    ).astype(jnp.bfloat16)
    low_spectrum = jnp.moveaxis(low_spectrum, 1, 2).reshape(routed, RB * 2 * box_size)
    payload = jnp.concatenate([low_spectrum, block_info], axis=1)
    send = jnp.einsum(
        "rs,rx->sx", seat_pick, payload, preferred_element_type=jnp.float32
    ).astype(jnp.bfloat16)
    rows_half = half_rows(box_size, device_count)
    top_rows = -(-rows_half // RB) * RB
    low_half = jnp.stack([transform(r, tables[:, :top_rows]) for r in rowwise])[:, :, :rows_half]
    power_half = jnp.sum(low_half * low_half, axis=(0, 1))
    pieces = power_half.reshape(device_count, rows_half * box_size // device_count)
    gathered = lax.all_to_all(pieces, ("img", "slab"), 0, 0, tiled=True)
    got = lax.all_to_all(send, "slab", 0, 0, tiled=True)
    got_blocks = got[:, : RB * 2 * box_size].reshape(seat_count, RB, 2 * box_size)
    got_info = got[:, RB * 2 * box_size : RB * 2 * box_size + 6].astype(jnp.int32)

    live = got_info[:, 0].astype(jnp.float32)[:, None, None]
    slot_of = got_info[:, 1] * row_blocks + got_info[:, 2]
    slot_pick = (slot_of[:, None] == jnp.arange(slots, dtype=jnp.int32)[None, :]).astype(
        jnp.bfloat16
    )
    blend_weight = ((got_info[:, 3].astype(jnp.float32) + 0.5) / WL)[:, None, None]
    volume_slots = volume.reshape(planes, row_blocks, RB, 2, box_size)
    volume_slots = jnp.transpose(volume_slots, (0, 1, 3, 2, 4)).reshape(slots, 2, RB, box_size)
    nearby = jnp.einsum(
        "sq,qhix->shix", slot_pick, volume_slots, preferred_element_type=jnp.float32
    )
    blend_4 = blend_weight[:, :, :, None]
    projected = (
        ((1.0 - blend_4) * nearby + blend_4 * jnp.roll(nearby, -1, axis=-1)) * live[..., None]
    ).astype(jnp.bfloat16)

    total = jnp.sum(gathered, axis=0, keepdims=True)
    power = power_gather(total, device_count, rows_half, box_size)
    noise_level = jnp.sqrt(power / (particles * device_count) + 1e-06)
    level_both = jnp.concatenate([noise_level, noise_level], axis=1)

    returned_rows = lax.all_to_all(projected, "slab", 0, 0, tiled=True)

    got_rows = low_row_ids(got_info[:, 4], box_size)
    got_contrast = contrast_curve(lookup_defocus(got_info[:, 5], defocus), got_rows, box_size)
    level_low = jnp.concatenate(
        [level_both[:low_rows], level_both[box_size - low_rows :]], axis=0
    ).reshape(blocks_per, RB, 2 * box_size)
    block_pick = (got_info[:, 4:5] == jnp.arange(blocks_per, dtype=jnp.int32)[None, :]).astype(
        jnp.float32
    )
    got_level = jnp.einsum(
        "sj,jix->six", block_pick, level_low, precision=HI, preferred_element_type=jnp.float32
    )
    got_contrast_both = jnp.concatenate([got_contrast, got_contrast], axis=-1).astype(jnp.float32)
    received = got_contrast_both * got_blocks.astype(jnp.float32) / got_level
    inserted = (1.0 - blend_weight) * received + blend_weight * shift_halves(received, 1, box_size)
    contrast_rows = got_contrast.astype(jnp.float32)
    squared = contrast_rows * contrast_rows
    weights = (1.0 - blend_weight) * squared + blend_weight * jnp.roll(squared, 1, axis=-1)
    seat_data = jnp.concatenate([inserted, weights], axis=-1) * live
    numerator = jnp.einsum(
        "sq,srx->qrx", slot_pick.astype(jnp.float32), seat_data, precision=HI,
        preferred_element_type=jnp.float32,
    )
    share = vrows // img_count
    numerator = numerator.reshape(planes, img_count, share, 3 * box_size).astype(jnp.bfloat16)
    numerator = jnp.swapaxes(numerator, 0, 1)
    numerator, returned_rows = lax.optimization_barrier((numerator, returned_rows))
    volume_part = reduce_over_img(numerator, img_count)
    weight_sum = volume_part[..., 2 * box_size :]
    reconstruction = volume_part[..., : 2 * box_size] / (
        jnp.concatenate([weight_sum, weight_sum], axis=-1) + 1.0
    )

    whitened = spectrum / noise_level
    row_all = jnp.arange(box_size, dtype=jnp.int32)[None, :]
    contrast = contrast_curve(lookup_defocus(micrograph, defocus), row_all, box_size)
    own_rows = jnp.einsum(
        "rs,shix->rhix", seat_pick, returned_rows, preferred_element_type=jnp.float32
    ).astype(jnp.bfloat16)
    own_rows = own_rows.reshape(particles, blocks_per, 2, RB, box_size)
    own_rows = jnp.moveaxis(own_rows, 2, 1).reshape(particles, 2, 2 * low_rows, box_size)
    inner = box_size - 2 * low_rows
    inner_rows = whitened[:, :, low_rows : box_size - low_rows].astype(jnp.bfloat16)
    residual = []
    for n in range(particles):
        inner_back = back_rows_of(inner_rows[n], tables)
        edge = jnp.zeros((2, low_rows, box_size), jnp.bfloat16)
        inner_part = picture_of(jnp.concatenate([edge, inner_back, edge], axis=1), tables)
        routed_white = jnp.concatenate(
            [whitened[n, :, :low_rows], whitened[n, :, box_size - low_rows :]], axis=1
        )
        routed_contrast = jnp.concatenate(
            [contrast[n, :low_rows], contrast[n, box_size - low_rows :]], axis=0
        ).astype(jnp.float32)
        routed_difference = (
            routed_white - routed_contrast[None] * own_rows[n].astype(jnp.float32)
        ).astype(jnp.bfloat16)
        routed_back = back_rows_of(routed_difference, tables)
        middle = jnp.zeros((2, inner, box_size), jnp.bfloat16)
        routed_part = picture_of(
            jnp.concatenate([routed_back[:, :low_rows], middle, routed_back[:, low_rows:]], axis=1),
            tables,
        )
        residual.append(((inner_part + routed_part) / box_size).astype(jnp.bfloat16))
    residual = jnp.stack(residual)
    return (residual, reconstruction)


def solution(mesh):
    in_specs = (
        P(("img", "slab"), None, None),
        P(("img", "slab")),
        P(),
        P(("img", "slab"), None, None),
        P(("img", "slab"), None),
        P(("img", "slab"), None),
        P(("img", "slab"), None),
        P("slab", None, None),
    )
    out_specs = (P(("img", "slab"), None, None), P("slab", "img", None))
    return jax.shard_map(body, mesh=mesh, in_specs=in_specs, out_specs=out_specs, check_vma=False)
```

```python
import math

import jax
import ml_dtypes
import numpy as np
import jax.numpy as jnp
from jax import lax
from jax.sharding import PartitionSpec as P

RB = 16
LOW = 4
WL = 8
HI = lax.Precision.HIGHEST


def table_stack(box_size):
    positions = np.arange(box_size)
    angles = ((positions[:, None] * positions[None, :]) % box_size) * (2.0 * np.pi / box_size)
    both = np.stack([np.cos(angles), np.sin(angles)]).astype(ml_dtypes.bfloat16)
    return jnp.asarray(both)


def rowwise_of(image, tables):
    return jnp.einsum(
        "yx,hmx->hym", image, tables, preferred_element_type=jnp.float32
    ).astype(jnp.bfloat16)


def transform(rowwise, tables):
    products = jnp.einsum("gky,hym->ghkm", tables, rowwise, preferred_element_type=jnp.float32)
    real = products[0, 0] - products[1, 1]
    imag = -(products[0, 1] + products[1, 0])
    return jnp.stack([real, imag])


def back_rows_of(difference, tables):
    products = jnp.einsum(
        "hyj,gmj->hgym", difference, tables, preferred_element_type=jnp.float32
    )
    back_real = products[0, 0] - products[1, 1]
    back_imag = products[0, 1] + products[1, 0]
    return jnp.stack([back_real, -back_imag]).astype(jnp.bfloat16)


def picture_of(back_rows, tables):
    picture = jnp.einsum("hxk,hkm->hxm", tables, back_rows, preferred_element_type=jnp.float32)
    return picture[0] + picture[1]


def radius_sq(row_ids, box_size):
    half_size = box_size // 2
    columns = jnp.arange(box_size, dtype=jnp.int32)
    freq_rows = jnp.where(row_ids < half_size, row_ids, row_ids - box_size)
    freq_cols = jnp.where(columns < half_size, columns, columns - box_size)
    total = freq_rows[..., None] * freq_rows[..., None] + freq_cols * freq_cols
    return total.astype(jnp.float32) / float(half_size * half_size)


def contrast_curve(defocus_of, row_ids, box_size):
    radius = radius_sq(row_ids, box_size)
    return (-jnp.sin(defocus_of[:, None, None] * radius + 0.1)).astype(jnp.bfloat16)


def lookup_defocus(mic_ids, defocus):
    labels = jnp.arange(defocus.shape[0], dtype=jnp.int32)
    return jnp.sum(jnp.where(mic_ids[:, None] == labels[None, :], defocus[None, :], 0.0), axis=1)


def shift_halves(values, steps, box_size):
    column = lax.broadcasted_iota(jnp.int32, values.shape, values.ndim - 1) % box_size
    seam = 0 if steps == 1 else box_size - 1
    rolled = jnp.roll(values, steps, axis=-1)
    wrapped = jnp.roll(values, -steps * (box_size - 1), axis=-1)
    return jnp.where(column == seam, wrapped, rolled)


def low_row_ids(block_ids, box_size):
    base = block_ids * RB + jnp.where(block_ids < LOW, 0, box_size - 2 * LOW * RB)
    return base[..., None] + jnp.arange(RB, dtype=jnp.int32)


def power_gather(total, device_count, rows, box_size):
    spread = jnp.broadcast_to(total, (device_count, total.shape[1]))
    back = lax.all_to_all(spread, ("img", "slab"), 0, 0, tiled=True)
    half = back.reshape(rows, box_size).astype(jnp.float32)
    zero = lax.optimization_barrier(jnp.zeros((), jnp.int32))
    n = lax.broadcasted_iota(jnp.int32, (box_size, box_size), 0) + zero
    m = lax.broadcasted_iota(jnp.int32, (box_size, box_size), 1)
    flip_columns = (n == (box_size - m) % box_size).astype(jnp.float32)
    flipped = jnp.dot(half, flip_columns, precision=HI)
    k = lax.broadcasted_iota(jnp.int32, (box_size, rows), 0) + zero
    j = lax.broadcasted_iota(jnp.int32, (box_size, rows), 1)
    keep = ((j == k) & (k <= box_size // 2)).astype(jnp.float32)
    turn = ((j == box_size - k) & (k > box_size // 2)).astype(jnp.float32)
    return jnp.dot(keep, half, precision=HI) + jnp.dot(turn, flipped, precision=HI)


def shift_exchange(values, count, capacity, direction):
    pieces = [values[:capacity]]
    for d in range(1, count):
        pairs = [(i, (i + direction * d) % count) for i in range(count)]
        pieces.append(lax.ppermute(values[d * capacity : (d + 1) * capacity], "slab", pairs))
    return jnp.concatenate(pieces, axis=0)


def reduce_over_img(numerator, count):
    me = lax.axis_index("img")
    total = lax.dynamic_index_in_dim(numerator, me, 0, keepdims=False).astype(jnp.float32)
    for d in range(1, count):
        piece = lax.dynamic_index_in_dim(numerator, (me + d) % count, 0, keepdims=False)
        pairs = [(i, (i + d) % count) for i in range(count)]
        total = total + lax.ppermute(piece, "img", pairs).astype(jnp.float32)
    return total


def half_rows(box_size, device_count):
    rows = box_size // 2 + 1
    while (rows * box_size) % device_count:
        rows += 1
    return rows


def body(images, micrograph, defocus, target_slab, target_plane, target_rows, shift_index, volume):
    particles, box_size = (images.shape[0], images.shape[1])
    slab_count = lax.axis_size("slab")
    img_count = lax.axis_size("img")
    device_count = img_count * slab_count
    low_rows = LOW * RB
    blocks_per = 2 * LOW
    routed = particles * blocks_per
    planes, vrows = volume.shape[0], volume.shape[1]
    row_blocks = vrows // RB
    slots = planes * row_blocks
    tables = lax.optimization_barrier(table_stack(box_size))

    destination = target_slab.reshape(routed)
    capacity = max(2, (2 * routed + slab_count - 1) // slab_count)
    member = (destination[:, None] == jnp.arange(slab_count, dtype=jnp.int32)[None, :]).astype(
        jnp.int32
    )
    before = jnp.cumsum(member, axis=0) - member
    slot_rank = jnp.sum(member * before, axis=1)
    me = lax.axis_index("slab")
    seat_index = destination * capacity + slot_rank
    seat_count = slab_count * capacity
    seat_pick = (seat_index[:, None] == jnp.arange(seat_count, dtype=jnp.int32)[None, :]).astype(
        jnp.bfloat16
    )
    source_block = jnp.tile(jnp.arange(blocks_per, dtype=jnp.int32), particles)
    block_info = jnp.stack(
        [
            jnp.ones((routed,), jnp.int32),
            target_plane.reshape(routed),
            target_rows.reshape(routed),
            shift_index.reshape(routed),
            source_block,
            jnp.repeat(micrograph, blocks_per),
        ],
        axis=1,
    ).astype(jnp.bfloat16)
    info_width = 128
    block_info = jnp.pad(block_info, ((0, 0), (0, info_width - block_info.shape[1])))

    rowwise = [rowwise_of(images[n], tables) for n in range(particles)]
    spectrum = jnp.stack([transform(r, tables) for r in rowwise])
    low_spectrum = jnp.concatenate(
        [spectrum[:, :, :low_rows], spectrum[:, :, box_size - low_rows :]], axis=2
    ).astype(jnp.bfloat16)
    low_spectrum = jnp.moveaxis(low_spectrum, 1, 2).reshape(routed, RB * 2 * box_size)
    payload = jnp.concatenate([low_spectrum, block_info], axis=1)
    send = jnp.einsum(
        "rs,rx->sx", seat_pick, payload, preferred_element_type=jnp.float32
    ).astype(jnp.bfloat16)
    rows_half = half_rows(box_size, device_count)
    top_rows = -(-rows_half // RB) * RB
    low_half = jnp.stack([transform(r, tables[:, :top_rows]) for r in rowwise])[:, :, :rows_half]
    power_half = jnp.sum(low_half * low_half, axis=(0, 1))
    pieces = power_half.reshape(device_count, rows_half * box_size // device_count)
    gathered = lax.all_to_all(pieces.astype(jnp.bfloat16), ("img", "slab"), 0, 0, tiled=True)
    got = lax.all_to_all(send, "slab", 0, 0, tiled=True)
    got_blocks = got[:, : RB * 2 * box_size].reshape(seat_count, RB, 2 * box_size)
    got_info = got[:, RB * 2 * box_size : RB * 2 * box_size + 6].astype(jnp.int32)

    live = got_info[:, 0].astype(jnp.float32)[:, None, None]
    slot_of = got_info[:, 1] * row_blocks + got_info[:, 2]
    slot_pick = (slot_of[:, None] == jnp.arange(slots, dtype=jnp.int32)[None, :]).astype(
        jnp.bfloat16
    )
    blend_weight = ((got_info[:, 3].astype(jnp.float32) + 0.5) / WL)[:, None, None]
    volume_slots = volume.reshape(planes, row_blocks, RB, 2, box_size)
    volume_slots = jnp.transpose(volume_slots, (0, 1, 3, 2, 4)).reshape(slots, 2, RB, box_size)
    nearby = jnp.einsum(
        "sq,qhix->shix", slot_pick, volume_slots, preferred_element_type=jnp.float32
    )
    blend_4 = blend_weight[:, :, :, None]
    projected = (
        ((1.0 - blend_4) * nearby + blend_4 * jnp.roll(nearby, -1, axis=-1)) * live[..., None]
    ).astype(jnp.bfloat16)

    total = jnp.sum(gathered.astype(jnp.float32), axis=0, keepdims=True).astype(jnp.bfloat16)
    power = power_gather(total, device_count, rows_half, box_size)
    noise_level = jnp.sqrt(power / (particles * device_count) + 1e-06)
    level_both = jnp.concatenate([noise_level, noise_level], axis=1)

    returned_rows = lax.all_to_all(projected, "slab", 0, 0, tiled=True)

    got_rows = low_row_ids(got_info[:, 4], box_size)
    got_contrast = contrast_curve(lookup_defocus(got_info[:, 5], defocus), got_rows, box_size)
    level_low = jnp.concatenate(
        [level_both[:low_rows], level_both[box_size - low_rows :]], axis=0
    ).reshape(blocks_per, RB, 2 * box_size)
    block_pick = (got_info[:, 4:5] == jnp.arange(blocks_per, dtype=jnp.int32)[None, :]).astype(
        jnp.float32
    )
    got_level = jnp.einsum(
        "sj,jix->six", block_pick, level_low, precision=HI, preferred_element_type=jnp.float32
    )
    got_contrast_both = jnp.concatenate([got_contrast, got_contrast], axis=-1).astype(jnp.float32)
    received = got_contrast_both * got_blocks.astype(jnp.float32) / got_level
    inserted = (1.0 - blend_weight) * received + blend_weight * shift_halves(received, 1, box_size)
    contrast_rows = got_contrast.astype(jnp.float32)
    squared = contrast_rows * contrast_rows
    weights = (1.0 - blend_weight) * squared + blend_weight * jnp.roll(squared, 1, axis=-1)
    seat_data = jnp.concatenate([inserted, weights], axis=-1) * live
    numerator = jnp.einsum(
        "sq,srx->qrx", slot_pick.astype(jnp.float32), seat_data, precision=HI,
        preferred_element_type=jnp.float32,
    )
    share = vrows // img_count
    numerator = numerator.reshape(planes, img_count, share, 3 * box_size).astype(jnp.bfloat16)
    numerator = jnp.swapaxes(numerator, 0, 1)
    volume_part = reduce_over_img(numerator, img_count)
    weight_sum = volume_part[..., 2 * box_size :]
    reconstruction = volume_part[..., : 2 * box_size] / (
        jnp.concatenate([weight_sum, weight_sum], axis=-1) + 1.0
    )

    whitened = spectrum / noise_level
    row_all = jnp.arange(box_size, dtype=jnp.int32)[None, :]
    contrast = contrast_curve(lookup_defocus(micrograph, defocus), row_all, box_size)
    own_rows = jnp.einsum(
        "rs,shix->rhix", seat_pick, returned_rows, preferred_element_type=jnp.float32
    ).astype(jnp.bfloat16)
    own_rows = own_rows.reshape(particles, blocks_per, 2, RB, box_size)
    own_rows = jnp.moveaxis(own_rows, 2, 1).reshape(particles, 2, 2 * low_rows, box_size)
    inner = box_size - 2 * low_rows
    inner_rows = whitened[:, :, low_rows : box_size - low_rows].astype(jnp.bfloat16)
    residual = []
    for n in range(particles):
        inner_back = back_rows_of(inner_rows[n], tables)
        edge = jnp.zeros((2, low_rows, box_size), jnp.bfloat16)
        inner_part = picture_of(jnp.concatenate([edge, inner_back, edge], axis=1), tables)
        routed_white = jnp.concatenate(
            [whitened[n, :, :low_rows], whitened[n, :, box_size - low_rows :]], axis=1
        )
        routed_contrast = jnp.concatenate(
            [contrast[n, :low_rows], contrast[n, box_size - low_rows :]], axis=0
        ).astype(jnp.float32)
        routed_difference = (
            routed_white - routed_contrast[None] * own_rows[n].astype(jnp.float32)
        ).astype(jnp.bfloat16)
        routed_back = back_rows_of(routed_difference, tables)
        middle = jnp.zeros((2, inner, box_size), jnp.bfloat16)
        routed_part = picture_of(
            jnp.concatenate([routed_back[:, :low_rows], middle, routed_back[:, low_rows:]], axis=1),
            tables,
        )
        residual.append(((inner_part + routed_part) / box_size).astype(jnp.bfloat16))
    residual = jnp.stack(residual)
    return (residual, reconstruction)


def solution(mesh):
    in_specs = (
        P(("img", "slab"), None, None),
        P(("img", "slab")),
        P(),
        P(("img", "slab"), None, None),
        P(("img", "slab"), None),
        P(("img", "slab"), None),
        P(("img", "slab"), None),
        P("slab", None, None),
    )
    out_specs = (P(("img", "slab"), None, None), P("slab", "img", None))
    return jax.shard_map(body, mesh=mesh, in_specs=in_specs, out_specs=out_specs, check_vma=False)
```
